256 devices in a mesh: req: 64 (over z_hi, x, y, core), tp: 4 (over z_lo).
Axes of the slice: x: 4, y: 4, z: 8 (z_hi: 2, z_lo: 4; z = z_hi * 4 + z_lo), core: 2. Of those that a mesh axis runs over, the one named last changes fastest.
Arguments:
- layer_in: bfloat16 [8192, 2048], P('req'), may hold values from -15 to 15
- q_nope: bfloat16 [8192, 2048], P('req', 'tp'), may hold values from -6 to 6
- q_pe: bfloat16 [8192, 1024], P('req', 'tp'), may hold values from -100 to 100
- kv_cache: bfloat16 [128, 1024, 576], P('req'), may hold values from -6 to 6
- lengths: int32 [128], P('req'), may hold values from 2 to 1024, as said below
- parents: int32 [128, 64], P('req'), may hold values from 0 to 62, as said below
- accepted: int32 [128], P('req'), may hold values from 0 to 63
- kv_a: bfloat16 [2048, 576], P(None, 'tp'), may hold values from -0.125 to 0.125
- kv_gain: float32 [512], replicated, may hold values from 0.1 to 1.9
- w_uk: bfloat16 [2048, 512], P('tp'), may hold values from -0.5 to 0.5
- w_uv: bfloat16 [512, 2048], P(None, 'tp'), may hold values from -0.25 to 0.25
- o_proj: bfloat16 [2048, 2048], P('tp'), may hold values from -0.125 to 0.125
- post_gain: float32 [2048], replicated, may hold values from 0.1 to 1.9
- routes: int32 [8192, 6], P('req'), may hold values from 0 to 63, all different within a row; in each aligned block of 128 rows (0 to 127, 128 to 255, ...) at most 16 rows name the same one
- gates: bfloat16 [8192, 6], P('req'), may hold values from 0.14941406 to 0.59765625
- w_gate: bfloat16 [64, 2048, 1408], P('req', None, 'tp'), may hold values from -0.125 to 0.125
- w_up: bfloat16 [64, 2048, 1408], P('req', None, 'tp'), may hold values from -0.125 to 0.125
- w_down: bfloat16 [64, 1408, 2048], P('req', 'tp'), may hold values from -0.15625 to 0.15625
Outputs:
- layer_out: bfloat16 [8192, 2048], P('req', 'tp')
- accepted_rows: bfloat16 [128, 64, 576], P('req')
The draws below stay inside these ranges and needn't reach their ends.
Inputs may be any that keep to these rules, and one draw needn't show every extreme that they name: `lengths`: at least one request of every draw has 1024 live slots. parents[r, 0] = 0; for i >= 1, parents[r, i] lies from i - 4 to i - 1. `routes`: the 6 experts of a token differ; within each aligned block of 128 rows (the tokens of one device) no expert is named more than 16 times.
All inputs are finite; a program needn't handle non-finite values.
Results may differ from the reference program's by a relative error of at most 0.012.
Values may be sent and summed in bfloat16 or wider, within the bound.
No kernel may reach another device: no remote copies, remote signals or barrier semaphores. Data moves between devices by JAX's collectives and lax.ppermute only.
A program may use at most 128 MiB of HBM per device.

```python
import math
import jax
import jax.numpy as jnp
import numpy as np
from jax import lax

D = 2048
HEADS = 16
NOPE = 128
ROPE = 64
VDIM = 128
LATENT = 512
MOE_FF = 1408
TOP = 6
TREE = 64
CACHE_MAX = 1024
KVW = 576
EXPERTS = 64
REQ = 128
TOK_DEV = 128
TOKENS = 8192
CAP = 16
N_REQ = 64


def draw_layer_in(key, part):
    key_base, key_rows, key_cols = jax.random.split(jax.random.fold_in(key, 1), 3)
    base_draw = jnp.clip(jax.random.normal(key_base, (TOKENS, D), jnp.float32), -6.0, 6.0)
    row_scale = jnp.exp(jax.random.uniform(key_rows, (TOKENS, 1), jnp.float32, math.log(0.3), math.log(3.0)))
    col_scale = (0.5 + jnp.arange(D, dtype=jnp.float32) / D)[None, :] * jnp.exp(jax.random.uniform(key_cols, (1, D), jnp.float32, math.log(0.6), math.log(1.6)))
    return (0.3 * base_draw * row_scale * col_scale).astype(jnp.bfloat16)


def draw_q_nope(key, part):
    key_base = jax.random.fold_in(key, 2)
    base_draw = jnp.clip(jax.random.normal(key_base, (TOKENS, HEADS * NOPE), jnp.float32), -6.0, 6.0)
    return base_draw.astype(jnp.bfloat16)


def draw_q_pe(key, part):
    key_base = jax.random.fold_in(key, 3)
    base_draw = jnp.clip(jax.random.normal(key_base, (TOKENS, HEADS * ROPE), jnp.float32), -6.0, 6.0)
    return base_draw.astype(jnp.bfloat16)


def draw_kv_cache(key, part):
    key_base = jax.random.fold_in(key, 4)
    base_draw = jnp.clip(jax.random.normal(key_base, (REQ, CACHE_MAX, KVW), jnp.float32), -6.0, 6.0)
    return base_draw.astype(jnp.bfloat16)


def draw_lengths(key, part):
    key_draw, key_long = jax.random.split(jax.random.fold_in(key, 5))
    cubes = jax.random.randint(key_draw, (REQ,), 0, 64)
    lengths_drawn = 2 + cubes * cubes * cubes * (CACHE_MAX - 2) // 262144
    longest = jax.random.randint(key_long, (), 0, REQ)
    return jnp.where(jnp.arange(REQ, dtype=jnp.int32) == longest, CACHE_MAX, lengths_drawn).astype(jnp.int32)


def draw_parents(key, part):
    indices = jnp.arange(TREE, dtype=jnp.int32)
    raw_steps = jax.random.randint(jax.random.fold_in(key, 6), (REQ, TREE), 0, 1 << 20)
    step_back = raw_steps % jnp.maximum(jnp.minimum(indices, 4), 1)[None, :]
    return jnp.where(indices[None, :] == 0, 0, indices[None, :] - 1 - step_back).astype(jnp.int32)


def plant(drawn, stream_key, low, top_value):
    place = [jax.random.randint(jax.random.fold_in(stream_key, axis), (), 0, length) for axis, length in enumerate(drawn.shape)]
    widest = drawn.shape.index(max(drawn.shape))
    neighbour = place[:widest] + [(place[widest] + 1) % drawn.shape[widest]] + place[widest + 1:]
    return drawn.at[tuple(place)].set(low).at[tuple(neighbour)].set(top_value)


def block_scale(own_key, shape, cuts, least, largest):
    loudness, own = 1.0, jax.random.fold_in(own_key, 6)
    for position, shards_of in cuts:
        draws = jnp.exp(jax.random.uniform(jax.random.fold_in(own, position), (shards_of,), jnp.float32, least / len(cuts), largest / len(cuts)))
        loudness = loudness * jnp.repeat(draws, shape[position] // shards_of).reshape([-1 if axis == position else 1 for axis in range(len(shape))])
    return loudness


def deal_out(own_key, own, number, rows, count, top, limit, lean):
    order = jax.random.permutation(own_key, count)
    heavy_load, usual = load_shares(count, rows * top, limit, lean, True), load_shares(count, rows * top, limit, lean, False)
    places = jnp.arange(count)

    def named(sizes, turn):
        used = int((sizes > 0).sum())
        fixed = max(1, used // 4)
        shifted = fixed + (places - fixed + turn * (used - fixed)) % max(1, count - fixed)
        return jnp.zeros((count,), jnp.int32).at[order[jnp.where(places < fixed, places, shifted)]].set(jnp.asarray(sizes, jnp.int32))

    sizes = jnp.where(number % 4 == 0, named(heavy_load, number // 4), named(usual, number - number // 4 - 1))
    mixed = jax.random.permutation(jax.random.fold_in(own, 3), count)
    donor, sink = mixed[0:count // 2 * 2:2], mixed[1:count // 2 * 2:2]
    slack = jnp.minimum(sizes[donor] - 1, limit - sizes[sink]) // 2
    slack = jnp.where((donor == order[0]) | (sink == order[0]) | (sizes[sink] == 0), 0, jnp.maximum(slack, 0))
    shifted = jax.random.randint(jax.random.fold_in(own, 4), (count // 2,), 0, 1 << 20) % (slack + 1)
    sizes = sizes.at[donor].add(-shifted).at[sink].add(shifted)
    items = jnp.searchsorted(jnp.cumsum(sizes), jnp.arange(rows * top), side="right").astype(jnp.int32)
    grid = items.reshape(top, rows).T
    grid = grid[jax.random.permutation(jax.random.fold_in(own, 1), rows)]
    turn = jax.random.randint(jax.random.fold_in(own, 2), (rows, 1), 0, top)
    return jnp.take_along_axis(grid, (jnp.arange(top)[None, :] + turn) % top, axis=1)


def load_shares(amount, total, bound, slope, full):
    weights = [(1 << 20) // math.isqrt(grade ** slope) + 1 for grade in range(1, amount + 1)]
    largest = bound if full else min(bound, max(-(-total // amount), total * weights[0] // sum(weights)))
    least = 1 if total - largest >= amount - 1 else 0
    given, spare = [largest] + [least] * (amount - 1), total - largest - least * (amount - 1)
    while spare > 0:
        candidates = [i for i in range(1, amount) if given[i] < largest] or [i for i in range(1, amount) if given[i] < bound]
        whole, left = sum([weights[i] for i in candidates]), spare
        for i in candidates:
            extra = min(bound - given[i], max(1, left * weights[i] // whole), spare)
            given[i] = given[i] + extra
            spare = spare - extra
    return np.array(given)


def noise(key, shape, width, most, cuts=(), held_as=jnp.bfloat16):
    result = width * jax.random.normal(key, shape, jnp.float32)
    if cuts:
        result = result * block_scale(key, shape, cuts, -0.22, 0.18)
    return jnp.clip(result, -most, most).astype(held_as)


def setup_inputs(seed: int = 0) -> dict:
    streams_of = jax.random.split(jax.random.key(seed), 19)
    layer_in = draw_layer_in(jax.random.fold_in(streams_of[18], 71), 0)
    q_nope = draw_q_nope(jax.random.fold_in(streams_of[18], 71), 0)
    q_pe = draw_q_pe(jax.random.fold_in(streams_of[18], 71), 0)
    kv_cache = draw_kv_cache(jax.random.fold_in(streams_of[18], 71), 0)
    lengths = draw_lengths(jax.random.fold_in(streams_of[18], 71), 0)
    parents = draw_parents(jax.random.fold_in(streams_of[18], 71), 0)
    accepted = plant(jax.random.randint(streams_of[6], (REQ,), 0, TREE), jax.random.fold_in(streams_of[6], 1), 0, TREE - 1).astype(jnp.int32)
    kv_a = noise(streams_of[7], (D, KVW), D ** -0.5, 0.125, ((1, 4),))
    kv_gain = jnp.clip(1.0 + 0.18 * jax.random.normal(streams_of[8], (LATENT,), jnp.float32), 0.1, 1.9)
    w_uk = noise(streams_of[9], (HEADS * NOPE, LATENT), NOPE ** -0.5, 0.5, ((0, 4),))
    w_uv = noise(streams_of[10], (LATENT, HEADS * VDIM), LATENT ** -0.5, 0.25, ((1, 4),))
    o_proj = noise(streams_of[11], (HEADS * VDIM, D), (HEADS * VDIM) ** -0.5, 0.125, ((0, 4),))
    post_gain = jnp.clip(1.0 + 0.18 * jax.random.normal(streams_of[12], (D,), jnp.float32), 0.1, 1.9)
    routes_keys = jax.random.split(jax.random.fold_in(streams_of[13], 1), TOKENS // TOK_DEV)
    routes_turns = jax.random.permutation(jax.random.fold_in(streams_of[13], 3), TOKENS // TOK_DEV)
    routes = jax.vmap(lambda own, number: deal_out(jax.random.fold_in(streams_of[13], 2), own, number, TOK_DEV, EXPERTS, TOP, CAP, 2))(routes_keys, routes_turns).reshape((TOKENS, TOP))
    gates = jnp.clip(0.14941406 + 0.4482422 * jax.random.uniform(streams_of[14], (TOKENS, TOP), jnp.float32) ** block_scale(streams_of[14], (TOKENS, TOP), ((0, 64),), -0.2, 0.2), 0.14941406, 0.59765625).astype(jnp.bfloat16)
    w_gate = noise(streams_of[15], (EXPERTS, D, MOE_FF), D ** -0.5, 0.125, ((0, 64), (2, 4)))
    w_up = noise(streams_of[16], (EXPERTS, D, MOE_FF), D ** -0.5, 0.125, ((0, 64), (2, 4)))
    w_down = noise(streams_of[17], (EXPERTS, MOE_FF, D), MOE_FF ** -0.5, 0.15625, ((0, 64), (1, 4)))
    return {"layer_in": layer_in, "q_nope": q_nope, "q_pe": q_pe, "kv_cache": kv_cache, "lengths": lengths, "parents": parents, "accepted": accepted, "kv_a": kv_a, "kv_gain": kv_gain, "w_uk": w_uk, "w_uv": w_uv, "o_proj": o_proj, "post_gain": post_gain, "routes": routes, "gates": gates, "w_gate": w_gate, "w_up": w_up, "w_down": w_down}


epsilon = 1e-06

def ancestors(parent_row):
    tree_size = parent_row.shape[0]
    indices = jnp.arange(tree_size, dtype=jnp.int32)
    link = ((parent_row[:, None] == indices[None, :]) | (indices[:, None] == indices[None, :])).astype(jnp.float32)
    for repeat_index in range(tree_size.bit_length()):
        link = jnp.minimum(jnp.dot(link, link, precision=lax.Precision.HIGHEST), 1.0)
    return link

def rotate(vector, positions):
    half_width = vector.shape[-1] // 2
    frequency = 10000.0 ** (-jnp.arange(half_width, dtype=jnp.float32) / half_width)
    angles = positions[:, None] * frequency[None, :]
    first_half = vector[:, :half_width]
    second_half = vector[:, half_width:]
    return jnp.concatenate([first_half * jnp.cos(angles) - second_half * jnp.sin(angles), first_half * jnp.sin(angles) + second_half * jnp.cos(angles)], -1)

def make_rows(compressed, kv_gain, positions):
    latent_raw = compressed[:, :LATENT].astype(jnp.float32)
    new_latent = (latent_raw * lax.rsqrt(lax.optimization_barrier(jnp.mean(latent_raw * latent_raw, -1, keepdims=True)) + epsilon) * kv_gain).astype(jnp.bfloat16)
    new_rotary = rotate(compressed[:, LATENT:].astype(jnp.float32), positions).astype(jnp.bfloat16)
    return jnp.concatenate([new_latent, new_rotary], -1)

def compact(ancestry, depths, node_index, row_set):
    tree_size = ancestry.shape[0]
    chain_mask = jnp.take(ancestry, node_index, axis=0)
    selector = (depths[None, :] == jnp.arange(tree_size, dtype=jnp.float32)[:, None]).astype(jnp.float32) * chain_mask[None, :]
    return jnp.dot(selector.astype(jnp.bfloat16), row_set, preferred_element_type=jnp.float32).astype(jnp.bfloat16)

def reference(layer_in, q_nope, q_pe, kv_cache, lengths, parents, accepted, kv_a, kv_gain, w_uk, w_uv, o_proj, post_gain, routes, gates, w_gate, w_up, w_down):
    compressed = jnp.dot(layer_in, kv_a, preferred_element_type=jnp.float32).astype(jnp.bfloat16)
    ancestry = jax.vmap(ancestors)(parents)
    depths = lax.optimization_barrier(jnp.sum(ancestry, -1)) - 1.0
    positions = (lengths.astype(jnp.float32)[:, None] + depths).reshape(-1)
    new_rows = make_rows(compressed, kv_gain, positions)
    rows_by_request = new_rows.reshape(REQ, TREE, KVW)
    accepted_rows = jax.vmap(compact)(ancestry, depths, accepted, rows_by_request)
    query_latent = jnp.einsum('thn,hnl->thl', q_nope.reshape(TOKENS, HEADS, NOPE).astype(jnp.float32), w_uk.reshape(HEADS, NOPE, LATENT).astype(jnp.float32)).astype(jnp.bfloat16)
    queries = jnp.concatenate([query_latent, q_pe.reshape(TOKENS, HEADS, ROPE)], -1).reshape(REQ, TREE, HEADS, KVW)
    score_scale = (NOPE + ROPE) ** (-0.5)

    def attend(bundle):
        q_rows, cache_r, len_r, new_r, ancestry_r = bundle
        q_float = q_rows.astype(jnp.float32)
        cache_scores = jnp.einsum('thk,ck->thc', q_float, cache_r.astype(jnp.float32)) * score_scale
        valid = jnp.arange(CACHE_MAX, dtype=jnp.int32) < len_r
        cache_scores = jnp.where(valid[None, None, :], cache_scores, -jnp.inf)
        tree_scores = jnp.einsum('thk,uk->thu', q_float, new_r.astype(jnp.float32)) * score_scale
        tree_scores = jnp.where(ancestry_r[:, None, :] > 0, tree_scores, -jnp.inf)
        row_max = jnp.maximum(lax.optimization_barrier(jnp.max(cache_scores, -1)), lax.optimization_barrier(jnp.max(tree_scores, -1)))
        cache_exps = jnp.exp(cache_scores - row_max[..., None])
        tree_exps = jnp.exp(tree_scores - row_max[..., None])
        totals = lax.optimization_barrier(jnp.sum(cache_exps, -1)) + lax.optimization_barrier(jnp.sum(tree_exps, -1))
        cache_weights = lax.optimization_barrier(cache_exps.astype(jnp.bfloat16)).astype(jnp.float32)
        tree_weights = lax.optimization_barrier(tree_exps.astype(jnp.bfloat16)).astype(jnp.float32)
        summed = jnp.einsum('thc,cl->thl', cache_weights, cache_r[:, :LATENT].astype(jnp.float32))
        summed = summed + jnp.einsum('thu,ul->thl', tree_weights, new_r[:, :LATENT].astype(jnp.float32))
        return (summed / totals[..., None]).astype(jnp.bfloat16)
    latent_out = lax.map(attend, (queries, kv_cache, lengths, rows_by_request, ancestry))
    head_out = jnp.einsum('thl,lhv->thv', latent_out.reshape(TOKENS, HEADS, LATENT).astype(jnp.float32), w_uv.reshape(LATENT, HEADS, VDIM).astype(jnp.float32)).astype(jnp.bfloat16)
    residual_sum = layer_in.astype(jnp.float32) + jnp.dot(head_out.reshape(TOKENS, HEADS * VDIM), o_proj, preferred_element_type=jnp.float32)
    normed = (residual_sum * lax.rsqrt(lax.optimization_barrier(jnp.mean(residual_sum * residual_sum, -1, keepdims=True)) + epsilon) * post_gain).astype(jnp.bfloat16)
    flat_ids = routes.reshape(N_REQ, TOK_DEV * TOP)
    hit_table = (flat_ids[..., None] == jnp.arange(EXPERTS, dtype=jnp.int32)).astype(jnp.int32)
    slot_rank = lax.optimization_barrier(jnp.sum((jnp.cumsum(hit_table, 1) - hit_table) * hit_table, -1)).astype(jnp.int32)
    token_ids = jnp.broadcast_to(jnp.arange(TOKENS, dtype=jnp.int32).reshape(N_REQ, TOK_DEV, 1), (N_REQ, TOK_DEV, TOP)).reshape(N_REQ, TOK_DEV * TOP)
    block_ids = jnp.broadcast_to(jnp.arange(N_REQ, dtype=jnp.int32)[:, None], (N_REQ, TOK_DEV * TOP))
    slot_index = block_ids * CAP + slot_rank
    slot_table = jnp.full((EXPERTS, N_REQ * CAP), TOKENS, dtype=jnp.int32).at[flat_ids, slot_index].set(token_ids)
    padded = jnp.concatenate([normed, jnp.zeros((1, D), jnp.bfloat16)], 0)

    def expert(bundle):
        indices, gate_w, up_w, down_w = bundle
        row_set = jnp.take(padded, indices, axis=0)
        gate_act = jnp.dot(row_set, gate_w, preferred_element_type=jnp.float32)
        up_act = jnp.dot(row_set, up_w, preferred_element_type=jnp.float32)
        hidden = (jax.nn.silu(gate_act) * up_act).astype(jnp.bfloat16)
        return jnp.dot(hidden, down_w, preferred_element_type=jnp.float32).astype(jnp.bfloat16)
    expert_rows = lax.map(expert, (slot_table, w_gate, w_up, w_down))
    picked = expert_rows[flat_ids, slot_index].reshape(TOKENS, TOP, D)
    routed = jnp.zeros((TOKENS, D), jnp.float32)
    for choice_index in range(TOP):
        routed = routed + gates[:, choice_index:choice_index + 1].astype(jnp.float32) * picked[:, choice_index].astype(jnp.float32)
    layer_out = (residual_sum + routed).astype(jnp.bfloat16)
    return (layer_out, accepted_rows)
```

```python
import jax
import jax.numpy as jnp
from jax import lax
from jax.sharding import PartitionSpec as P

D = 2048
NOPE = 128
ROPE = 64
VDIM = 128
LATENT = 512


epsilon = 1e-06


def ancestors(parent_row):
    tree_size = parent_row.shape[0]
    indices = jnp.arange(tree_size, dtype=jnp.int32)
    link = (
        (parent_row[:, None] == indices[None, :]) | (indices[:, None] == indices[None, :])
    ).astype(jnp.float32)
    for repeat_index in range(tree_size.bit_length()):
        link = jnp.minimum(jnp.dot(link, link, precision=lax.Precision.HIGHEST), 1.0)
    return link


def rotate(vector, positions):
    half_width = vector.shape[-1] // 2
    frequency = 10000.0 ** (-jnp.arange(half_width, dtype=jnp.float32) / half_width)
    angles = positions[:, None] * frequency[None, :]
    first_half = vector[:, :half_width]
    second_half = vector[:, half_width:]
    return jnp.concatenate(
        [
            first_half * jnp.cos(angles) - second_half * jnp.sin(angles),
            first_half * jnp.sin(angles) + second_half * jnp.cos(angles),
        ],
        -1,
    )


def make_rows(compressed, kv_gain, positions):
    latent_raw = compressed[:, :LATENT].astype(jnp.float32)
    new_latent = (
        latent_raw
        * lax.rsqrt(jnp.mean(latent_raw * latent_raw, -1, keepdims=True) + epsilon)
        * kv_gain
    ).astype(jnp.bfloat16)
    new_rotary = rotate(compressed[:, LATENT:].astype(jnp.float32), positions).astype(jnp.bfloat16)
    return jnp.concatenate([new_latent, new_rotary], -1)


def compact(ancestry, depths, node_index, row_set):
    tree_size = ancestry.shape[0]
    chain_mask = jnp.take(ancestry, node_index, axis=0)
    selector = (depths[None, :] == jnp.arange(tree_size, dtype=jnp.float32)[:, None]).astype(
        jnp.float32
    ) * chain_mask[None, :]
    return jnp.dot(
        selector.astype(jnp.bfloat16), row_set, preferred_element_type=jnp.float32
    ).astype(jnp.bfloat16)


def attend_request(q_rows, cache_r, length, new_r, mask_rows):
    score_scale = (NOPE + ROPE) ** (-0.5)
    cache_slots = cache_r.shape[0]
    block_size = min(cache_slots, 512)
    block_total = cache_slots // block_size
    offsets = jnp.arange(block_size, dtype=jnp.int32)
    tree_scores = jnp.dot(q_rows, new_r.T, preferred_element_type=jnp.float32) * score_scale
    tree_scores = jnp.where(mask_rows, tree_scores, -jnp.inf)

    def block_scores(block_index):
        key_block = lax.dynamic_slice_in_dim(cache_r, block_index * block_size, block_size, 0)
        scores = jnp.dot(q_rows, key_block.T, preferred_element_type=jnp.float32) * score_scale
        valid = block_index * block_size + offsets < length
        return (jnp.where(valid[None, :], scores, -jnp.inf), key_block)

    def raise_max(block_index, row_max):
        scores, key_block = block_scores(block_index)
        return jnp.maximum(row_max, jnp.max(scores, -1))

    row_max = lax.fori_loop(0, block_total, raise_max, jnp.max(tree_scores, -1))
    tree_exps = jnp.exp(tree_scores - row_max[:, None])
    start_totals = jnp.sum(tree_exps, -1)
    start_sums = jnp.dot(
        tree_exps.astype(jnp.bfloat16), new_r[:, :LATENT], preferred_element_type=jnp.float32
    )

    def accumulate(block_index, carry):
        totals, weighted = carry
        scores, key_block = block_scores(block_index)
        exps = jnp.exp(scores - row_max[:, None])
        weighted = weighted + jnp.dot(
            exps.astype(jnp.bfloat16), key_block[:, :LATENT], preferred_element_type=jnp.float32
        )
        return (totals + jnp.sum(exps, -1), weighted)

    totals, weighted = lax.fori_loop(0, block_total, accumulate, (start_totals, start_sums))
    return (weighted / totals[:, None]).astype(jnp.bfloat16)


def route_tables(routes, gates, experts_all, capacity):
    tok_rows, top_count = routes.shape
    flat_ids = routes.reshape(-1)
    pair_count = flat_ids.shape[0]
    hit_table = (flat_ids[:, None] == jnp.arange(experts_all, dtype=jnp.int32)[None, :]).astype(
        jnp.bfloat16
    )
    earlier = (
        jnp.arange(pair_count, dtype=jnp.int32)[:, None]
        > jnp.arange(pair_count, dtype=jnp.int32)[None, :]
    ).astype(jnp.bfloat16)
    before = jnp.dot(earlier, hit_table, preferred_element_type=jnp.float32)
    slot_rank = jnp.sum(before * hit_table.astype(jnp.float32), -1).astype(jnp.int32)
    slot_index = flat_ids * capacity + slot_rank
    places = (
        slot_index[:, None] == jnp.arange(experts_all * capacity, dtype=jnp.int32)[None, :]
    ).reshape(tok_rows, top_count, -1)
    pick_table = jnp.any(places, 1).astype(jnp.bfloat16)
    weights = jnp.sum(jnp.where(places, gates[:, :, None], jnp.zeros((), jnp.bfloat16)), 1)
    return (pick_table, weights)


def run_expert(row_set, w_gate, w_up, w_down):
    local_experts = w_gate.shape[0]
    sources = row_set.shape[0] // local_experts
    grouped = row_set.reshape(sources, local_experts, row_set.shape[1], row_set.shape[2])
    gate_act = jnp.einsum("secd,edf->secf", grouped, w_gate, preferred_element_type=jnp.float32)
    up_act = jnp.einsum("secd,edf->secf", grouped, w_up, preferred_element_type=jnp.float32)
    hidden = (jax.nn.silu(gate_act) * up_act).astype(jnp.bfloat16)
    partial_value = jnp.einsum("secf,efd->secd", hidden, w_down, preferred_element_type=jnp.float32)
    return partial_value.reshape(sources * local_experts, row_set.shape[1], -1)


def on_device(
    layer_in,
    q_nope,
    q_pe,
    kv_cache,
    lengths,
    parents,
    accepted,
    kv_a,
    kv_gain,
    w_uk,
    w_uv,
    o_proj,
    post_gain,
    routes,
    gates,
    w_gate,
    w_up,
    w_down,
):
    tok_rows = layer_in.shape[0]
    local_requests, tree_size = parents.shape
    local_heads = q_nope.shape[1] // NOPE
    compressed_part = jnp.dot(layer_in, kv_a, preferred_element_type=jnp.float32).astype(
        jnp.bfloat16
    )
    compressed = lax.all_gather(compressed_part, "tp", axis=1, tiled=True)
    ancestry = jax.vmap(ancestors)(parents)
    depths = jnp.sum(ancestry, -1) - 1.0
    positions = (lengths.astype(jnp.float32)[:, None] + depths).reshape(-1)
    new_rows = make_rows(compressed, kv_gain, positions)
    rows_by_request = new_rows.reshape(local_requests, tree_size, -1)
    accepted_rows = jax.vmap(compact)(ancestry, depths, accepted, rows_by_request)
    query_latent = jnp.einsum(
        "thn,hnl->thl",
        q_nope.reshape(tok_rows, local_heads, NOPE),
        w_uk.reshape(local_heads, NOPE, LATENT),
        preferred_element_type=jnp.float32,
    ).astype(jnp.bfloat16)
    queries = jnp.concatenate([query_latent, q_pe.reshape(tok_rows, local_heads, ROPE)], -1)
    outputs = []
    for request in range(local_requests):
        q_rows = queries[request * tree_size : (request + 1) * tree_size].reshape(
            tree_size * local_heads, -1
        )
        mask_rows = jnp.repeat(ancestry[request] > 0, local_heads, axis=0)
        result = attend_request(
            q_rows, kv_cache[request], lengths[request], rows_by_request[request], mask_rows
        )
        outputs.append(result.reshape(tree_size, local_heads, LATENT))
    latent_out = jnp.concatenate(outputs, 0)
    head_out = jnp.einsum(
        "thl,lhv->thv",
        latent_out,
        w_uv.reshape(LATENT, local_heads, VDIM),
        preferred_element_type=jnp.float32,
    ).astype(jnp.bfloat16)
    experts_all = w_gate.shape[0] * lax.axis_size("req")
    top_count = routes.shape[1]
    capacity = 4 * tok_rows * top_count // (3 * experts_all)
    pick_table, weights = route_tables(routes, gates, experts_all, capacity)
    tp_size = lax.axis_size("tp")
    tp_index = lax.axis_index("tp")
    quarter = D // tp_size
    attention_parts = jnp.einsum(
        "tk,kqf->qtf",
        head_out.reshape(tok_rows, local_heads * VDIM),
        o_proj.reshape(o_proj.shape[0], tp_size, quarter),
        preferred_element_type=jnp.float32,
    )
    attention_quarter = lax.psum_scatter(attention_parts, "tp", scatter_dimension=0, tiled=True)
    attention_quarter = attention_quarter.reshape(tok_rows, quarter)
    hidden_quarter = lax.dynamic_slice_in_dim(layer_in, tp_index * quarter, quarter, 1)
    residual_quarter = hidden_quarter.astype(jnp.float32) + attention_quarter
    square_sum = lax.psum(jnp.sum(residual_quarter * residual_quarter, -1, keepdims=True), "tp")
    gain_quarter = lax.dynamic_slice_in_dim(post_gain, tp_index * quarter, quarter, 0)
    normed_quarter = (
        residual_quarter * lax.rsqrt(square_sum / D + epsilon) * gain_quarter
    ).astype(jnp.bfloat16)
    outgoing = lax.dot_general(
        pick_table, normed_quarter, (((0,), (0,)), ((), ())), preferred_element_type=jnp.float32
    ).astype(jnp.bfloat16)
    outgoing = outgoing.reshape(experts_all, capacity, quarter)
    arrived = lax.all_to_all(outgoing, "req", split_axis=0, concat_axis=0, tiled=True)
    row_set = lax.all_gather(arrived, "tp", axis=0, tiled=False)
    gate_w = w_gate[0].reshape(tp_size, quarter, -1)
    up_w = w_up[0].reshape(tp_size, quarter, -1)
    gate_act = jnp.einsum("qscf,qfh->sch", row_set, gate_w, preferred_element_type=jnp.float32)
    up_act = jnp.einsum("qscf,qfh->sch", row_set, up_w, preferred_element_type=jnp.float32)
    expert_hidden = (jax.nn.silu(gate_act) * up_act).astype(jnp.bfloat16)
    partial_value = jnp.einsum(
        "sch,hqf->qscf",
        expert_hidden,
        w_down[0].reshape(w_down.shape[1], tp_size, quarter),
        preferred_element_type=jnp.float32,
    )
    partial_parts = lax.all_to_all(
        partial_value.astype(jnp.bfloat16), "tp", split_axis=0, concat_axis=0, tiled=True
    )
    expert_out = jnp.sum(partial_parts.astype(jnp.float32), 0).astype(jnp.bfloat16)
    shares = lax.all_to_all(expert_out, "req", split_axis=0, concat_axis=0, tiled=True)
    routed = jnp.dot(
        weights, shares.reshape(experts_all * capacity, quarter), preferred_element_type=jnp.float32
    )
    layer_out = (residual_quarter + routed).astype(jnp.bfloat16)
    return (layer_out, accepted_rows)


def solution(mesh):
    return jax.shard_map(
        on_device,
        mesh=mesh,
        in_specs=(
            P("req", None),
            P("req", "tp"),
            P("req", "tp"),
            P("req", None, None),
            P("req"),
            P("req", None),
            P("req"),
            P(None, "tp"),
            P(),
            P("tp", None),
            P(None, "tp"),
            P("tp", None),
            P(),
            P("req", None),
            P("req", None),
            P("req", None, "tp"),
            P("req", None, "tp"),
            P("req", "tp", None),
        ),
        out_specs=(P("req", "tp"), P("req", None, None)),
        check_vma=False,
    )
```

```python
import jax
import jax.numpy as jnp
from jax import lax
from jax.sharding import PartitionSpec as P

D = 2048
NOPE = 128
ROPE = 64
VDIM = 128
LATENT = 512


epsilon = 1e-06


def ancestors(parent_row):
    tree_size = parent_row.shape[0]
    indices = jnp.arange(tree_size, dtype=jnp.int32)
    link = (
        (parent_row[:, None] == indices[None, :]) | (indices[:, None] == indices[None, :])
    ).astype(jnp.float32)
    for repeat_index in range(tree_size.bit_length()):
        link = jnp.minimum(jnp.dot(link, link, precision=lax.Precision.HIGHEST), 1.0)
    return link


def rotate(vector, positions):
    half_width = vector.shape[-1] // 2
    frequency = 10000.0 ** (-jnp.arange(half_width, dtype=jnp.float32) / half_width)
    angles = positions[:, None] * frequency[None, :]
    first_half = vector[:, :half_width]
    second_half = vector[:, half_width:]
    return jnp.concatenate(
        [
            first_half * jnp.cos(angles) - second_half * jnp.sin(angles),
            first_half * jnp.sin(angles) + second_half * jnp.cos(angles),
        ],
        -1,
    )


def make_rows(compressed, kv_gain, positions):
    latent_raw = compressed[:, :LATENT].astype(jnp.float32)
    new_latent = (
        latent_raw
        * lax.rsqrt(jnp.mean(latent_raw * latent_raw, -1, keepdims=True) + epsilon)
        * kv_gain
    ).astype(jnp.bfloat16)
    new_rotary = rotate(compressed[:, LATENT:].astype(jnp.float32), positions).astype(jnp.bfloat16)
    return jnp.concatenate([new_latent, new_rotary], -1)


def compact(ancestry, depths, node_index, row_set):
    tree_size = ancestry.shape[0]
    chain_mask = jnp.take(ancestry, node_index, axis=0)
    selector = (depths[None, :] == jnp.arange(tree_size, dtype=jnp.float32)[:, None]).astype(
        jnp.float32
    ) * chain_mask[None, :]
    return jnp.dot(
        selector.astype(jnp.bfloat16), row_set, preferred_element_type=jnp.float32
    ).astype(jnp.bfloat16)


def attend_request(q_rows, cache_r, length, new_r, mask_rows):
    score_scale = (NOPE + ROPE) ** (-0.5)
    cache_slots = cache_r.shape[0]
    block_size = min(cache_slots, 512)
    block_total = cache_slots // block_size
    offsets = jnp.arange(block_size, dtype=jnp.int32)
    tree_scores = jnp.dot(q_rows, new_r.T, preferred_element_type=jnp.float32) * score_scale
    tree_scores = jnp.where(mask_rows, tree_scores, -jnp.inf)

    def block_scores(block_index):
        key_block = lax.dynamic_slice_in_dim(cache_r, block_index * block_size, block_size, 0)
        scores = jnp.dot(q_rows, key_block.T, preferred_element_type=jnp.float32) * score_scale
        valid = block_index * block_size + offsets < length
        return (jnp.where(valid[None, :], scores, -jnp.inf), key_block)

    def raise_max(block_index, row_max):
        scores, key_block = block_scores(block_index)
        return jnp.maximum(row_max, jnp.max(scores, -1))

    row_max = lax.fori_loop(0, block_total, raise_max, jnp.max(tree_scores, -1))
    tree_exps = jnp.exp(tree_scores - row_max[:, None])
    start_totals = jnp.sum(tree_exps, -1)
    start_sums = jnp.dot(
        tree_exps.astype(jnp.bfloat16), new_r[:, :LATENT], preferred_element_type=jnp.float32
    )

    def accumulate(block_index, carry):
        totals, weighted = carry
        scores, key_block = block_scores(block_index)
        exps = jnp.exp(scores - row_max[:, None])
        weighted = weighted + jnp.dot(
            exps.astype(jnp.bfloat16), key_block[:, :LATENT], preferred_element_type=jnp.float32
        )
        return (totals + jnp.sum(exps, -1), weighted)

    totals, weighted = lax.fori_loop(0, block_total, accumulate, (start_totals, start_sums))
    return (weighted / totals[:, None]).astype(jnp.bfloat16)


def attend_dense(q_rows, cache, lengths, new_rows, mask_rows):
    score_scale = (NOPE + ROPE) ** (-0.5)
    cache_slots = cache.shape[1]
    cache_scores = (
        jnp.einsum("rqk,rck->rqc", q_rows, cache, preferred_element_type=jnp.float32) * score_scale
    )
    valid = jnp.arange(cache_slots, dtype=jnp.int32)[None, :] < lengths[:, None]
    cache_scores = jnp.where(valid[:, None, :], cache_scores, -jnp.inf)
    tree_scores = (
        jnp.einsum("rqk,ruk->rqu", q_rows, new_rows, preferred_element_type=jnp.float32)
        * score_scale
    )
    tree_scores = jnp.where(mask_rows, tree_scores, -jnp.inf)
    row_max = jnp.maximum(jnp.max(cache_scores, -1), jnp.max(tree_scores, -1))
    cache_exps = jnp.exp(cache_scores - row_max[..., None])
    tree_exps = jnp.exp(tree_scores - row_max[..., None])
    totals = jnp.sum(cache_exps, -1) + jnp.sum(tree_exps, -1)
    summed = jnp.einsum(
        "rqc,rck->rqk", cache_exps.astype(jnp.bfloat16), cache, preferred_element_type=jnp.float32
    )
    summed = summed + jnp.einsum(
        "rqu,ruk->rqk", tree_exps.astype(jnp.bfloat16), new_rows, preferred_element_type=jnp.float32
    )
    return (summed[..., :LATENT] / totals[..., None]).astype(jnp.bfloat16)


def route_tables(routes, gates, experts_all, capacity):
    tok_rows, top_count = routes.shape
    flat_ids = routes.reshape(-1)
    pair_count = flat_ids.shape[0]
    hit_table = (flat_ids[:, None] == jnp.arange(experts_all, dtype=jnp.int32)[None, :]).astype(
        jnp.bfloat16
    )
    earlier = (
        jnp.arange(pair_count, dtype=jnp.int32)[:, None]
        > jnp.arange(pair_count, dtype=jnp.int32)[None, :]
    ).astype(jnp.bfloat16)
    before = jnp.dot(earlier, hit_table, preferred_element_type=jnp.float32)
    slot_rank = jnp.sum(before * hit_table.astype(jnp.float32), -1).astype(jnp.int32)
    slot_index = flat_ids * capacity + slot_rank
    places = (
        slot_index[:, None] == jnp.arange(experts_all * capacity, dtype=jnp.int32)[None, :]
    ).reshape(tok_rows, top_count, -1)
    pick_table = jnp.any(places, 1).astype(jnp.bfloat16)
    weights = jnp.sum(jnp.where(places, gates[:, :, None], jnp.zeros((), jnp.bfloat16)), 1)
    return (pick_table, weights)


def run_expert(row_set, w_gate, w_up, w_down):
    local_experts = w_gate.shape[0]
    sources = row_set.shape[0] // local_experts
    grouped = row_set.reshape(sources, local_experts, row_set.shape[1], row_set.shape[2])
    gate_act = jnp.einsum("secd,edf->secf", grouped, w_gate, preferred_element_type=jnp.float32)
    up_act = jnp.einsum("secd,edf->secf", grouped, w_up, preferred_element_type=jnp.float32)
    hidden = (jax.nn.silu(gate_act) * up_act).astype(jnp.bfloat16)
    partial_value = jnp.einsum("secf,efd->secd", hidden, w_down, preferred_element_type=jnp.float32)
    return partial_value.reshape(sources * local_experts, row_set.shape[1], -1)


def on_device(
    layer_in,
    q_nope,
    q_pe,
    kv_cache,
    lengths,
    parents,
    accepted,
    kv_a,
    kv_gain,
    w_uk,
    w_uv,
    o_proj,
    post_gain,
    routes,
    gates,
    w_gate,
    w_up,
    w_down,
):
    tok_rows = layer_in.shape[0]
    local_requests, tree_size = parents.shape
    local_heads = q_nope.shape[1] // NOPE
    compressed_part = jnp.dot(layer_in, kv_a, preferred_element_type=jnp.float32).astype(
        jnp.bfloat16
    )
    compressed = lax.all_gather(compressed_part, "tp", axis=1, tiled=True)
    ancestry = jax.vmap(ancestors)(parents)
    depths = jnp.sum(ancestry, -1) - 1.0
    positions = (lengths.astype(jnp.float32)[:, None] + depths).reshape(-1)
    new_rows = make_rows(compressed, kv_gain, positions)
    rows_by_request = new_rows.reshape(local_requests, tree_size, -1)
    accepted_rows = jax.vmap(compact)(ancestry, depths, accepted, rows_by_request)
    query_latent = jnp.einsum(
        "thn,hnl->thl",
        q_nope.reshape(tok_rows, local_heads, NOPE),
        w_uk.reshape(local_heads, NOPE, LATENT),
        preferred_element_type=jnp.float32,
    ).astype(jnp.bfloat16)
    queries = jnp.concatenate([query_latent, q_pe.reshape(tok_rows, local_heads, ROPE)], -1)
    q_rows = queries.reshape(local_requests, tree_size * local_heads, -1)
    mask_rows = jnp.repeat(ancestry > 0, local_heads, axis=1)
    latent_out = attend_dense(q_rows, kv_cache, lengths, rows_by_request, mask_rows)
    latent_out = latent_out.reshape(tok_rows, local_heads, LATENT)
    head_out = jnp.einsum(
        "thl,lhv->thv",
        latent_out,
        w_uv.reshape(LATENT, local_heads, VDIM),
        preferred_element_type=jnp.float32,
    ).astype(jnp.bfloat16)
    experts_all = w_gate.shape[0] * lax.axis_size("req")
    top_count = routes.shape[1]
    capacity = 4 * tok_rows * top_count // (3 * experts_all)
    pick_table, weights = route_tables(routes, gates, experts_all, capacity)
    tp_size = lax.axis_size("tp")
    tp_index = lax.axis_index("tp")
    quarter = D // tp_size
    attention_parts = jnp.einsum(
        "tk,kqf->qtf",
        head_out.reshape(tok_rows, local_heads * VDIM),
        o_proj.reshape(o_proj.shape[0], tp_size, quarter),
        preferred_element_type=jnp.float32,
    )
    attention_quarter = lax.psum_scatter(attention_parts, "tp", scatter_dimension=0, tiled=True)
    attention_quarter = attention_quarter.reshape(tok_rows, quarter)
    hidden_quarter = lax.dynamic_slice_in_dim(layer_in, tp_index * quarter, quarter, 1)
    residual_quarter = hidden_quarter.astype(jnp.float32) + attention_quarter
    square_sum = lax.psum(jnp.sum(residual_quarter * residual_quarter, -1, keepdims=True), "tp")
    gain_quarter = lax.dynamic_slice_in_dim(post_gain, tp_index * quarter, quarter, 0)
    normed_quarter = (
        residual_quarter * lax.rsqrt(square_sum / D + epsilon) * gain_quarter
    ).astype(jnp.bfloat16)
    outgoing = lax.dot_general(
        pick_table, normed_quarter, (((0,), (0,)), ((), ())), preferred_element_type=jnp.float32
    ).astype(jnp.bfloat16)
    outgoing = outgoing.reshape(experts_all, capacity, quarter)
    arrived = lax.all_to_all(outgoing, "req", split_axis=0, concat_axis=0, tiled=True)
    row_set = lax.all_gather(arrived, "tp", axis=0, tiled=False)
    gate_w = w_gate[0].reshape(tp_size, quarter, -1)
    up_w = w_up[0].reshape(tp_size, quarter, -1)
    gate_act = jnp.einsum("qscf,qfh->sch", row_set, gate_w, preferred_element_type=jnp.float32)
    up_act = jnp.einsum("qscf,qfh->sch", row_set, up_w, preferred_element_type=jnp.float32)
    expert_hidden = (jax.nn.silu(gate_act) * up_act).astype(jnp.bfloat16)
    partial_value = jnp.einsum(
        "sch,hqf->qscf",
        expert_hidden,
        w_down[0].reshape(w_down.shape[1], tp_size, quarter),
        preferred_element_type=jnp.float32,
    )
    partial_parts = lax.all_to_all(
        partial_value.astype(jnp.bfloat16), "tp", split_axis=0, concat_axis=0, tiled=True
    )
    expert_out = jnp.sum(partial_parts.astype(jnp.float32), 0).astype(jnp.bfloat16)
    shares = lax.all_to_all(expert_out, "req", split_axis=0, concat_axis=0, tiled=True)
    routed = jnp.dot(
        weights, shares.reshape(experts_all * capacity, quarter), preferred_element_type=jnp.float32
    )
    layer_out = (residual_quarter + routed).astype(jnp.bfloat16)
    return (layer_out, accepted_rows)


def solution(mesh):
    return jax.shard_map(
        on_device,
        mesh=mesh,
        in_specs=(
            P("req", None),
            P("req", "tp"),
            P("req", "tp"),
            P("req", None, None),
            P("req"),
            P("req", None),
            P("req"),
            P(None, "tp"),
            P(),
            P("tp", None),
            P(None, "tp"),
            P("tp", None),
            P(),
            P("req", None),
            P("req", None),
            P("req", None, "tp"),
            P("req", None, "tp"),
            P("req", "tp", None),
        ),
        out_specs=(P("req", "tp"), P("req", None, None)),
        check_vma=False,
    )
```

```python
import jax
import jax.numpy as jnp
from jax import lax
from jax.sharding import PartitionSpec as P

D = 2048
NOPE = 128
ROPE = 64
VDIM = 128
LATENT = 512


epsilon = 1e-06


def ancestors(parent_row):
    tree_size = parent_row.shape[0]
    indices = jnp.arange(tree_size, dtype=jnp.int32)
    link = (
        (parent_row[:, None] == indices[None, :]) | (indices[:, None] == indices[None, :])
    ).astype(jnp.float32)
    for repeat_index in range(tree_size.bit_length()):
        link = jnp.minimum(jnp.dot(link, link, precision=lax.Precision.HIGHEST), 1.0)
    return link


def rotate(vector, positions):
    half_width = vector.shape[-1] // 2
    frequency = 10000.0 ** (-jnp.arange(half_width, dtype=jnp.float32) / half_width)
    angles = positions[:, None] * frequency[None, :]
    first_half = vector[:, :half_width]
    second_half = vector[:, half_width:]
    return jnp.concatenate(
        [
            first_half * jnp.cos(angles) - second_half * jnp.sin(angles),
            first_half * jnp.sin(angles) + second_half * jnp.cos(angles),
        ],
        -1,
    )


def make_rows(compressed, kv_gain, positions):
    latent_raw = compressed[:, :LATENT].astype(jnp.float32)
    new_latent = (
        latent_raw
        * lax.rsqrt(jnp.mean(latent_raw * latent_raw, -1, keepdims=True) + epsilon)
        * kv_gain
    ).astype(jnp.bfloat16)
    new_rotary = rotate(compressed[:, LATENT:].astype(jnp.float32), positions).astype(jnp.bfloat16)
    return jnp.concatenate([new_latent, new_rotary], -1)


def compact(ancestry, depths, node_index, row_set):
    tree_size = ancestry.shape[0]
    chain_mask = jnp.take(ancestry, node_index, axis=0)
    selector = (depths[None, :] == jnp.arange(tree_size, dtype=jnp.float32)[:, None]).astype(
        jnp.float32
    ) * chain_mask[None, :]
    return jnp.dot(
        selector.astype(jnp.bfloat16), row_set, preferred_element_type=jnp.float32
    ).astype(jnp.bfloat16)


def attend_request(q_rows, cache_r, length, new_r, mask_rows):
    score_scale = (NOPE + ROPE) ** (-0.5)
    cache_slots = cache_r.shape[0]
    block_size = min(cache_slots, 512)
    block_total = cache_slots // block_size
    offsets = jnp.arange(block_size, dtype=jnp.int32)
    tree_scores = jnp.dot(q_rows, new_r.T, preferred_element_type=jnp.float32) * score_scale
    tree_scores = jnp.where(mask_rows, tree_scores, -jnp.inf)

    def block_scores(block_index):
        key_block = lax.dynamic_slice_in_dim(cache_r, block_index * block_size, block_size, 0)
        scores = jnp.dot(q_rows, key_block.T, preferred_element_type=jnp.float32) * score_scale
        valid = block_index * block_size + offsets < length
        return (jnp.where(valid[None, :], scores, -jnp.inf), key_block)

    def raise_max(block_index, row_max):
        scores, key_block = block_scores(block_index)
        return jnp.maximum(row_max, jnp.max(scores, -1))

    row_max = lax.fori_loop(0, block_total, raise_max, jnp.max(tree_scores, -1))
    tree_exps = jnp.exp(tree_scores - row_max[:, None])
    start_totals = jnp.sum(tree_exps, -1)
    start_sums = jnp.dot(
        tree_exps.astype(jnp.bfloat16), new_r[:, :LATENT], preferred_element_type=jnp.float32
    )

    def accumulate(block_index, carry):
        totals, weighted = carry
        scores, key_block = block_scores(block_index)
        exps = jnp.exp(scores - row_max[:, None])
        weighted = weighted + jnp.dot(
            exps.astype(jnp.bfloat16), key_block[:, :LATENT], preferred_element_type=jnp.float32
        )
        return (totals + jnp.sum(exps, -1), weighted)

    totals, weighted = lax.fori_loop(0, block_total, accumulate, (start_totals, start_sums))
    return (weighted / totals[:, None]).astype(jnp.bfloat16)


def attend_dense(q_rows, cache, lengths, new_rows, mask_rows):
    score_scale = (NOPE + ROPE) ** (-0.5)
    cache_slots = cache.shape[1]
    cache_scores = (
        jnp.einsum("rqk,rck->rqc", q_rows, cache, preferred_element_type=jnp.float32) * score_scale
    )
    valid = jnp.arange(cache_slots, dtype=jnp.int32)[None, :] < lengths[:, None]
    cache_scores = jnp.where(valid[:, None, :], cache_scores, -jnp.inf)
    tree_scores = (
        jnp.einsum("rqk,ruk->rqu", q_rows, new_rows, preferred_element_type=jnp.float32)
        * score_scale
    )
    tree_scores = jnp.where(mask_rows, tree_scores, -jnp.inf)
    row_max = jnp.maximum(jnp.max(cache_scores, -1), jnp.max(tree_scores, -1))
    cache_exps = jnp.exp(cache_scores - row_max[..., None])
    tree_exps = jnp.exp(tree_scores - row_max[..., None])
    totals = jnp.sum(cache_exps, -1) + jnp.sum(tree_exps, -1)
    summed = jnp.einsum(
        "rqc,rck->rqk", cache_exps.astype(jnp.bfloat16), cache, preferred_element_type=jnp.float32
    )
    summed = summed + jnp.einsum(
        "rqu,ruk->rqk", tree_exps.astype(jnp.bfloat16), new_rows, preferred_element_type=jnp.float32
    )
    return (summed[..., :LATENT] / totals[..., None]).astype(jnp.bfloat16)


def route_tables(routes, gates, experts_all, capacity):
    tok_rows, top_count = routes.shape
    flat_ids = routes.reshape(-1)
    pair_count = flat_ids.shape[0]
    hit_table = (flat_ids[:, None] == jnp.arange(experts_all, dtype=jnp.int32)[None, :]).astype(
        jnp.bfloat16
    )
    earlier = (
        jnp.arange(pair_count, dtype=jnp.int32)[:, None]
        > jnp.arange(pair_count, dtype=jnp.int32)[None, :]
    ).astype(jnp.bfloat16)
    before = jnp.dot(earlier, hit_table, preferred_element_type=jnp.float32)
    slot_rank = jnp.sum(before * hit_table.astype(jnp.float32), -1).astype(jnp.int32)
    slot_index = flat_ids * capacity + slot_rank
    places = (
        slot_index[:, None] == jnp.arange(experts_all * capacity, dtype=jnp.int32)[None, :]
    ).reshape(tok_rows, top_count, -1)
    pick_table = jnp.any(places, 1).astype(jnp.bfloat16)
    weights = jnp.sum(jnp.where(places, gates[:, :, None], jnp.zeros((), jnp.bfloat16)), 1)
    return (pick_table, weights)


def run_expert(row_set, w_gate, w_up, w_down):
    local_experts = w_gate.shape[0]
    sources = row_set.shape[0] // local_experts
    grouped = row_set.reshape(sources, local_experts, row_set.shape[1], row_set.shape[2])
    gate_act = jnp.einsum("secd,edf->secf", grouped, w_gate, preferred_element_type=jnp.float32)
    up_act = jnp.einsum("secd,edf->secf", grouped, w_up, preferred_element_type=jnp.float32)
    hidden = (jax.nn.silu(gate_act) * up_act).astype(jnp.bfloat16)
    partial_value = jnp.einsum("secf,efd->secd", hidden, w_down, preferred_element_type=jnp.float32)
    return partial_value.reshape(sources * local_experts, row_set.shape[1], -1)


def on_device(
    layer_in,
    q_nope,
    q_pe,
    kv_cache,
    lengths,
    parents,
    accepted,
    kv_a,
    kv_gain,
    w_uk,
    w_uv,
    o_proj,
    post_gain,
    routes,
    gates,
    w_gate,
    w_up,
    w_down,
):
    tok_rows = layer_in.shape[0]
    local_requests, tree_size = parents.shape
    local_heads = q_nope.shape[1] // NOPE
    compressed_part = jnp.dot(layer_in, kv_a, preferred_element_type=jnp.float32).astype(
        jnp.bfloat16
    )
    compressed = lax.all_gather(compressed_part, "tp", axis=1, tiled=True)
    ancestry = jax.vmap(ancestors)(parents)
    depths = jnp.sum(ancestry, -1) - 1.0
    positions = (lengths.astype(jnp.float32)[:, None] + depths).reshape(-1)
    new_rows = make_rows(compressed, kv_gain, positions)
    rows_by_request = new_rows.reshape(local_requests, tree_size, -1)
    accepted_rows = jax.vmap(compact)(ancestry, depths, accepted, rows_by_request)
    query_latent = jnp.einsum(
        "thn,hnl->thl",
        q_nope.reshape(tok_rows, local_heads, NOPE),
        w_uk.reshape(local_heads, NOPE, LATENT),
        preferred_element_type=jnp.float32,
    ).astype(jnp.bfloat16)
    queries = jnp.concatenate([query_latent, q_pe.reshape(tok_rows, local_heads, ROPE)], -1)
    q_rows = queries.reshape(local_requests, tree_size * local_heads, -1)
    mask_rows = jnp.repeat(ancestry > 0, local_heads, axis=1)
    latent_out = attend_dense(q_rows, kv_cache, lengths, rows_by_request, mask_rows)
    latent_out = latent_out.reshape(tok_rows, local_heads, LATENT)
    head_out = jnp.einsum(
        "thl,lhv->thv",
        latent_out,
        w_uv.reshape(LATENT, local_heads, VDIM),
        preferred_element_type=jnp.float32,
    ).astype(jnp.bfloat16)
    experts_all = w_gate.shape[0] * lax.axis_size("req")
    top_count = routes.shape[1]
    capacity = 4 * tok_rows * top_count // (3 * experts_all)
    pick_table, weights = route_tables(routes, gates, experts_all, capacity)
    tp_size = lax.axis_size("tp")
    tp_index = lax.axis_index("tp")
    quarter = D // tp_size
    attention_parts = jnp.einsum(
        "tk,kqf->qtf",
        head_out.reshape(tok_rows, local_heads * VDIM),
        o_proj.reshape(o_proj.shape[0], tp_size, quarter),
        preferred_element_type=jnp.float32,
    )
    attention_quarter = lax.psum_scatter(attention_parts, "tp", scatter_dimension=0, tiled=True)
    attention_quarter = attention_quarter.reshape(tok_rows, quarter)
    hidden_quarter = lax.dynamic_slice_in_dim(layer_in, tp_index * quarter, quarter, 1)
    residual_quarter = hidden_quarter.astype(jnp.float32) + attention_quarter
    square_sum = lax.psum(jnp.sum(residual_quarter * residual_quarter, -1, keepdims=True), "tp")
    gain_quarter = lax.dynamic_slice_in_dim(post_gain, tp_index * quarter, quarter, 0)
    normed_quarter = (
        residual_quarter * lax.rsqrt(square_sum / D + epsilon) * gain_quarter
    ).astype(jnp.bfloat16)
    parity = tp_index % 2
    upper = tp_index // 2
    across = [(t, t ^ 2) for t in range(tp_size)]
    beside = [(t, t ^ 1) for t in range(tp_size)]
    other_quarter = lax.ppermute(normed_quarter, "tp", across)
    half_rows = jnp.where(
        upper == 0,
        jnp.stack([normed_quarter, other_quarter], 1),
        jnp.stack([other_quarter, normed_quarter], 1),
    ).reshape(tok_rows, 2 * quarter)
    outgoing = lax.dot_general(
        pick_table, half_rows, (((0,), (0,)), ((), ())), preferred_element_type=jnp.float32
    ).astype(jnp.bfloat16)
    outgoing = outgoing.reshape(experts_all, capacity, 2, quarter)
    own_rows = lax.all_to_all(outgoing, "req", split_axis=0, concat_axis=0, tiled=True)
    partner_rows = lax.ppermute(own_rows, "tp", beside)
    sources = own_rows.shape[0]
    gate_w = w_gate[0].reshape(2, 2, quarter, -1)
    up_w = w_up[0].reshape(2, 2, quarter, -1)
    down_w = w_down[0].reshape(w_down.shape[1], 2, 2, quarter)

    def half_of(weight, axis, which):
        return lax.dynamic_index_in_dim(weight, which, axis=axis, keepdims=False)

    gate_act = jnp.einsum(
        "scjf,jfh->sch", own_rows, half_of(gate_w, 1, parity), preferred_element_type=jnp.float32
    ) + jnp.einsum(
        "scjf,jfh->sch", partner_rows, half_of(gate_w, 1, 1 - parity),
        preferred_element_type=jnp.float32,
    )
    up_act = jnp.einsum(
        "scjf,jfh->sch", own_rows, half_of(up_w, 1, parity), preferred_element_type=jnp.float32
    ) + jnp.einsum(
        "scjf,jfh->sch", partner_rows, half_of(up_w, 1, 1 - parity),
        preferred_element_type=jnp.float32,
    )
    expert_hidden = (jax.nn.silu(gate_act) * up_act).astype(jnp.bfloat16)
    own_value = jnp.einsum(
        "sch,hjf->scjf", expert_hidden, half_of(down_w, 2, parity),
        preferred_element_type=jnp.float32,
    )
    partner_value = jnp.einsum(
        "sch,hjf->scjf", expert_hidden, half_of(down_w, 2, 1 - parity),
        preferred_element_type=jnp.float32,
    ).astype(jnp.bfloat16)
    pair_value = (
        own_value + lax.ppermute(partner_value, "tp", beside).astype(jnp.float32)
    ).astype(jnp.bfloat16)
    shares = lax.all_to_all(pair_value, "req", split_axis=0, concat_axis=0, tiled=True)
    routed_half = jnp.dot(
        weights, shares.reshape(experts_all * capacity, 2 * quarter),
        preferred_element_type=jnp.float32,
    ).reshape(tok_rows, 2, quarter)
    keep = half_of(routed_half, 1, upper)
    give = half_of(routed_half, 1, 1 - upper)
    routed = keep + lax.ppermute(give, "tp", across)
    layer_out = (residual_quarter + routed).astype(jnp.bfloat16)
    return (layer_out, accepted_rows)


def solution(mesh):
    return jax.shard_map(
        on_device,
        mesh=mesh,
        in_specs=(
            P("req", None),
            P("req", "tp"),
            P("req", "tp"),
            P("req", None, None),
            P("req"),
            P("req", None),
            P("req"),
            P(None, "tp"),
            P(),
            P("tp", None),
            P(None, "tp"),
            P("tp", None),
            P(),
            P("req", None),
            P("req", None),
            P("req", None, "tp"),
            P("req", None, "tp"),
            P("req", "tp", None),
        ),
        out_specs=(P("req", "tp"), P("req", None, None)),
        check_vma=False,
    )
```

```python
import jax
import jax.numpy as jnp
from jax import lax
from jax.sharding import PartitionSpec as P

D = 2048
NOPE = 128
ROPE = 64
VDIM = 128
LATENT = 512


epsilon = 1e-06


def ancestors(parent_row):
    tree_size = parent_row.shape[0]
    indices = jnp.arange(tree_size, dtype=jnp.int32)
    link = (
        (parent_row[:, None] == indices[None, :]) | (indices[:, None] == indices[None, :])
    ).astype(jnp.float32)
    for repeat_index in range(tree_size.bit_length()):
        link = jnp.minimum(jnp.dot(link, link, precision=lax.Precision.HIGHEST), 1.0)
    return link


def rotate(vector, positions):
    half_width = vector.shape[-1] // 2
    frequency = 10000.0 ** (-jnp.arange(half_width, dtype=jnp.float32) / half_width)
    angles = positions[:, None] * frequency[None, :]
    first_half = vector[:, :half_width]
    second_half = vector[:, half_width:]
    return jnp.concatenate(
        [
            first_half * jnp.cos(angles) - second_half * jnp.sin(angles),
            first_half * jnp.sin(angles) + second_half * jnp.cos(angles),
        ],
        -1,
    )


def make_rows(compressed, kv_gain, positions):
    latent_raw = compressed[:, :LATENT].astype(jnp.float32)
    new_latent = (
        latent_raw
        * lax.rsqrt(jnp.mean(latent_raw * latent_raw, -1, keepdims=True) + epsilon)
        * kv_gain
    ).astype(jnp.bfloat16)
    new_rotary = rotate(compressed[:, LATENT:].astype(jnp.float32), positions).astype(jnp.bfloat16)
    return jnp.concatenate([new_latent, new_rotary], -1)


def compact(ancestry, depths, node_index, row_set):
    tree_size = ancestry.shape[0]
    chain_mask = jnp.take(ancestry, node_index, axis=0)
    selector = (depths[None, :] == jnp.arange(tree_size, dtype=jnp.float32)[:, None]).astype(
        jnp.float32
    ) * chain_mask[None, :]
    return jnp.dot(
        selector.astype(jnp.bfloat16), row_set, preferred_element_type=jnp.float32
    ).astype(jnp.bfloat16)


def attend_request(q_rows, cache_r, length, new_r, mask_rows):
    score_scale = (NOPE + ROPE) ** (-0.5)
    cache_slots = cache_r.shape[0]
    block_size = min(cache_slots, 512)
    block_total = cache_slots // block_size
    offsets = jnp.arange(block_size, dtype=jnp.int32)
    tree_scores = jnp.dot(q_rows, new_r.T, preferred_element_type=jnp.float32) * score_scale
    tree_scores = jnp.where(mask_rows, tree_scores, -jnp.inf)

    def block_scores(block_index):
        key_block = lax.dynamic_slice_in_dim(cache_r, block_index * block_size, block_size, 0)
        scores = jnp.dot(q_rows, key_block.T, preferred_element_type=jnp.float32) * score_scale
        valid = block_index * block_size + offsets < length
        return (jnp.where(valid[None, :], scores, -jnp.inf), key_block)

    def raise_max(block_index, row_max):
        scores, key_block = block_scores(block_index)
        return jnp.maximum(row_max, jnp.max(scores, -1))

    row_max = lax.fori_loop(0, block_total, raise_max, jnp.max(tree_scores, -1))
    tree_exps = jnp.exp(tree_scores - row_max[:, None])
    start_totals = jnp.sum(tree_exps, -1)
    start_sums = jnp.dot(
        tree_exps.astype(jnp.bfloat16), new_r[:, :LATENT], preferred_element_type=jnp.float32
    )

    def accumulate(block_index, carry):
        totals, weighted = carry
        scores, key_block = block_scores(block_index)
        exps = jnp.exp(scores - row_max[:, None])
        weighted = weighted + jnp.dot(
            exps.astype(jnp.bfloat16), key_block[:, :LATENT], preferred_element_type=jnp.float32
        )
        return (totals + jnp.sum(exps, -1), weighted)

    totals, weighted = lax.fori_loop(0, block_total, accumulate, (start_totals, start_sums))
    return (weighted / totals[:, None]).astype(jnp.bfloat16)


def attend_dense(q_rows, cache, lengths, new_rows, mask_rows):
    score_scale = (NOPE + ROPE) ** (-0.5)
    cache_slots = cache.shape[1]
    cache_scores = (
        jnp.einsum("rqk,rck->rqc", q_rows, cache, preferred_element_type=jnp.float32) * score_scale
    )
    valid = jnp.arange(cache_slots, dtype=jnp.int32)[None, :] < lengths[:, None]
    cache_scores = jnp.where(valid[:, None, :], cache_scores, -jnp.inf)
    tree_scores = (
        jnp.einsum("rqk,ruk->rqu", q_rows, new_rows, preferred_element_type=jnp.float32)
        * score_scale
    )
    tree_scores = jnp.where(mask_rows, tree_scores, -jnp.inf)
    row_max = jnp.maximum(jnp.max(cache_scores, -1), jnp.max(tree_scores, -1))
    cache_exps = jnp.exp(cache_scores - row_max[..., None])
    tree_exps = jnp.exp(tree_scores - row_max[..., None])
    totals = jnp.sum(cache_exps, -1) + jnp.sum(tree_exps, -1)
    summed = jnp.einsum(
        "rqc,rck->rqk", cache_exps.astype(jnp.bfloat16), cache, preferred_element_type=jnp.float32
    )
    summed = summed + jnp.einsum(
        "rqu,ruk->rqk", tree_exps.astype(jnp.bfloat16), new_rows, preferred_element_type=jnp.float32
    )
    return (summed[..., :LATENT] / totals[..., None]).astype(jnp.bfloat16)


def route_tables(routes, gates, experts_all, capacity):
    tok_rows, top_count = routes.shape
    flat_ids = routes.reshape(-1)
    pair_count = flat_ids.shape[0]
    hit_table = (flat_ids[:, None] == jnp.arange(experts_all, dtype=jnp.int32)[None, :]).astype(
        jnp.bfloat16
    )
    earlier = (
        jnp.arange(pair_count, dtype=jnp.int32)[:, None]
        > jnp.arange(pair_count, dtype=jnp.int32)[None, :]
    ).astype(jnp.bfloat16)
    before = jnp.dot(earlier, hit_table, preferred_element_type=jnp.float32)
    slot_rank = jnp.sum(before * hit_table.astype(jnp.float32), -1).astype(jnp.int32)
    slot_index = flat_ids * capacity + slot_rank
    places = (
        slot_index[:, None] == jnp.arange(experts_all * capacity, dtype=jnp.int32)[None, :]
    ).reshape(tok_rows, top_count, -1)
    pick_table = jnp.any(places, 1).astype(jnp.bfloat16)
    weights = jnp.sum(jnp.where(places, gates[:, :, None], jnp.zeros((), jnp.bfloat16)), 1)
    return (pick_table, weights)


def run_expert(row_set, w_gate, w_up, w_down):
    local_experts = w_gate.shape[0]
    sources = row_set.shape[0] // local_experts
    grouped = row_set.reshape(sources, local_experts, row_set.shape[1], row_set.shape[2])
    gate_act = jnp.einsum("secd,edf->secf", grouped, w_gate, preferred_element_type=jnp.float32)
    up_act = jnp.einsum("secd,edf->secf", grouped, w_up, preferred_element_type=jnp.float32)
    hidden = (jax.nn.silu(gate_act) * up_act).astype(jnp.bfloat16)
    partial_value = jnp.einsum("secf,efd->secd", hidden, w_down, preferred_element_type=jnp.float32)
    return partial_value.reshape(sources * local_experts, row_set.shape[1], -1)


def on_device(
    layer_in,
    q_nope,
    q_pe,
    kv_cache,
    lengths,
    parents,
    accepted,
    kv_a,
    kv_gain,
    w_uk,
    w_uv,
    o_proj,
    post_gain,
    routes,
    gates,
    w_gate,
    w_up,
    w_down,
):
    tok_rows = layer_in.shape[0]
    local_requests, tree_size = parents.shape
    local_heads = q_nope.shape[1] // NOPE
    compressed_part = jnp.dot(layer_in, kv_a, preferred_element_type=jnp.float32).astype(
        jnp.bfloat16
    )
    compressed = lax.all_gather(compressed_part, "tp", axis=1, tiled=True)
    ancestry = jax.vmap(ancestors)(parents)
    depths = jnp.sum(ancestry, -1) - 1.0
    positions = (lengths.astype(jnp.float32)[:, None] + depths).reshape(-1)
    new_rows = make_rows(compressed, kv_gain, positions)
    rows_by_request = new_rows.reshape(local_requests, tree_size, -1)
    accepted_rows = jax.vmap(compact)(ancestry, depths, accepted, rows_by_request)
    query_latent = jnp.einsum(
        "thn,hnl->thl",
        q_nope.reshape(tok_rows, local_heads, NOPE),
        w_uk.reshape(local_heads, NOPE, LATENT),
        preferred_element_type=jnp.float32,
    ).astype(jnp.bfloat16)
    queries = jnp.concatenate([query_latent, q_pe.reshape(tok_rows, local_heads, ROPE)], -1)
    q_rows = queries.reshape(local_requests, tree_size * local_heads, -1)
    mask_rows = jnp.repeat(ancestry > 0, local_heads, axis=1)
    latent_out = attend_dense(q_rows, kv_cache, lengths, rows_by_request, mask_rows)
    latent_out = latent_out.reshape(tok_rows, local_heads, LATENT)
    head_out = jnp.einsum(
        "thl,lhv->thv",
        latent_out,
        w_uv.reshape(LATENT, local_heads, VDIM),
        preferred_element_type=jnp.float32,
    ).astype(jnp.bfloat16)
    experts_all = w_gate.shape[0] * lax.axis_size("req")
    top_count = routes.shape[1]
    capacity = 4 * tok_rows * top_count // (3 * experts_all)
    pick_table, weights = route_tables(routes, gates, experts_all, capacity)
    tp_size = lax.axis_size("tp")
    tp_index = lax.axis_index("tp")
    quarter = D // tp_size
    attention_parts = jnp.einsum(
        "tk,kqf->qtf",
        head_out.reshape(tok_rows, local_heads * VDIM),
        o_proj.reshape(o_proj.shape[0], tp_size, quarter),
        preferred_element_type=jnp.float32,
    )
    attention_quarter = lax.psum_scatter(attention_parts, "tp", scatter_dimension=0, tiled=True)
    attention_quarter = attention_quarter.reshape(tok_rows, quarter)
    hidden_quarter = lax.dynamic_slice_in_dim(layer_in, tp_index * quarter, quarter, 1)
    residual_quarter = hidden_quarter.astype(jnp.float32) + attention_quarter
    square_sum = lax.psum(jnp.sum(residual_quarter * residual_quarter, -1, keepdims=True), "tp")
    gain_quarter = lax.dynamic_slice_in_dim(post_gain, tp_index * quarter, quarter, 0)
    normed_quarter = (
        residual_quarter * lax.rsqrt(square_sum / D + epsilon) * gain_quarter
    ).astype(jnp.bfloat16)
    parity = tp_index % 2
    upper = tp_index // 2
    across = [(t, t ^ 2) for t in range(tp_size)]
    beside = [(t, t ^ 1) for t in range(tp_size)]
    other_quarter = lax.ppermute(normed_quarter, "tp", across)
    half_rows = jnp.where(
        upper == 0,
        jnp.stack([normed_quarter, other_quarter], 1),
        jnp.stack([other_quarter, normed_quarter], 1),
    ).reshape(tok_rows, 2 * quarter)
    outgoing = lax.dot_general(
        pick_table, half_rows, (((0,), (0,)), ((), ())), preferred_element_type=jnp.float32
    ).astype(jnp.bfloat16)
    outgoing = outgoing.reshape(experts_all, capacity, 2, quarter)
    gate_w = w_gate[0].reshape(2, 2, quarter, -1)
    up_w = w_up[0].reshape(2, 2, quarter, -1)
    down_w = w_down[0].reshape(w_down.shape[1], 2, 2, quarter)

    def half_of(weight, axis, which):
        return lax.dynamic_index_in_dim(weight, which, axis=axis, keepdims=False)

    gate_own, gate_partner = half_of(gate_w, 1, parity), half_of(gate_w, 1, 1 - parity)
    up_own, up_partner = half_of(up_w, 1, parity), half_of(up_w, 1, 1 - parity)
    down_own, down_partner = half_of(down_w, 2, parity), half_of(down_w, 2, 1 - parity)
    chunks = 2
    slot_step = capacity // chunks
    weights_by_slot = weights.reshape(tok_rows, experts_all, capacity)
    routed_half = jnp.zeros((tok_rows, 2 * quarter), jnp.float32)
    for chunk in range(chunks):
        slots = slice(chunk * slot_step, (chunk + 1) * slot_step)
        own_rows = lax.all_to_all(outgoing[:, slots], "req", split_axis=0, concat_axis=0, tiled=True)
        partner_rows = lax.ppermute(own_rows, "tp", beside)
        gate_act = jnp.einsum(
            "scjf,jfh->sch", own_rows, gate_own, preferred_element_type=jnp.float32
        ) + jnp.einsum("scjf,jfh->sch", partner_rows, gate_partner, preferred_element_type=jnp.float32)
        up_act = jnp.einsum(
            "scjf,jfh->sch", own_rows, up_own, preferred_element_type=jnp.float32
        ) + jnp.einsum("scjf,jfh->sch", partner_rows, up_partner, preferred_element_type=jnp.float32)
        expert_hidden = (jax.nn.silu(gate_act) * up_act).astype(jnp.bfloat16)
        partner_value = jnp.einsum(
            "sch,hjf->scjf", expert_hidden, down_partner, preferred_element_type=jnp.float32
        ).astype(jnp.bfloat16)
        arrived_value = lax.ppermute(partner_value, "tp", beside)
        own_value = jnp.einsum(
            "sch,hjf->scjf", expert_hidden, down_own, preferred_element_type=jnp.float32
        )
        pair_value = (own_value + arrived_value.astype(jnp.float32)).astype(jnp.bfloat16)
        shares = lax.all_to_all(pair_value, "req", split_axis=0, concat_axis=0, tiled=True)
        routed_half = routed_half + jnp.dot(
            weights_by_slot[:, :, slots].reshape(tok_rows, experts_all * slot_step),
            shares.reshape(experts_all * slot_step, 2 * quarter),
            preferred_element_type=jnp.float32,
        )
    routed_half = routed_half.reshape(tok_rows, 2, quarter)
    keep = half_of(routed_half, 1, upper)
    give = half_of(routed_half, 1, 1 - upper)
    routed = keep + lax.ppermute(give, "tp", across)
    layer_out = (residual_quarter + routed).astype(jnp.bfloat16)
    return (layer_out, accepted_rows)


def solution(mesh):
    return jax.shard_map(
        on_device,
        mesh=mesh,
        in_specs=(
            P("req", None),
            P("req", "tp"),
            P("req", "tp"),
            P("req", None, None),
            P("req"),
            P("req", None),
            P("req"),
            P(None, "tp"),
            P(),
            P("tp", None),
            P(None, "tp"),
            P("tp", None),
            P(),
            P("req", None),
            P("req", None),
            P("req", None, "tp"),
            P("req", None, "tp"),
            P("req", "tp", None),
        ),
        out_specs=(P("req", "tp"), P("req", None, None)),
        check_vma=False,
    )
```

```python
import jax
import jax.numpy as jnp
from jax import lax
from jax.sharding import PartitionSpec as P

D = 2048
NOPE = 128
ROPE = 64
VDIM = 128
LATENT = 512


epsilon = 1e-06


def ancestors(parent_row):
    tree_size = parent_row.shape[0]
    indices = jnp.arange(tree_size, dtype=jnp.int32)
    link = (
        (parent_row[:, None] == indices[None, :]) | (indices[:, None] == indices[None, :])
    ).astype(jnp.float32)
    for repeat_index in range(tree_size.bit_length()):
        link = jnp.minimum(jnp.dot(link, link, precision=lax.Precision.HIGHEST), 1.0)
    return link


def rotate(vector, positions):
    half_width = vector.shape[-1] // 2
    frequency = 10000.0 ** (-jnp.arange(half_width, dtype=jnp.float32) / half_width)
    angles = positions[:, None] * frequency[None, :]
    first_half = vector[:, :half_width]
    second_half = vector[:, half_width:]
    return jnp.concatenate(
        [
            first_half * jnp.cos(angles) - second_half * jnp.sin(angles),
            first_half * jnp.sin(angles) + second_half * jnp.cos(angles),
        ],
        -1,
    )


def make_rows(compressed, kv_gain, positions):
    latent_raw = compressed[:, :LATENT].astype(jnp.float32)
    new_latent = (
        latent_raw
        * lax.rsqrt(jnp.mean(latent_raw * latent_raw, -1, keepdims=True) + epsilon)
        * kv_gain
    ).astype(jnp.bfloat16)
    new_rotary = rotate(compressed[:, LATENT:].astype(jnp.float32), positions).astype(jnp.bfloat16)
    return jnp.concatenate([new_latent, new_rotary], -1)


def compact(ancestry, depths, node_index, row_set):
    tree_size = ancestry.shape[0]
    chain_mask = jnp.take(ancestry, node_index, axis=0)
    selector = (depths[None, :] == jnp.arange(tree_size, dtype=jnp.float32)[:, None]).astype(
        jnp.float32
    ) * chain_mask[None, :]
    return jnp.dot(
        selector.astype(jnp.bfloat16), row_set, preferred_element_type=jnp.float32
    ).astype(jnp.bfloat16)


def attend_request(q_rows, cache_r, length, new_r, mask_rows):
    score_scale = (NOPE + ROPE) ** (-0.5)
    cache_slots = cache_r.shape[0]
    block_size = min(cache_slots, 512)
    block_total = cache_slots // block_size
    offsets = jnp.arange(block_size, dtype=jnp.int32)
    tree_scores = jnp.dot(q_rows, new_r.T, preferred_element_type=jnp.float32) * score_scale
    tree_scores = jnp.where(mask_rows, tree_scores, -jnp.inf)

    def block_scores(block_index):
        key_block = lax.dynamic_slice_in_dim(cache_r, block_index * block_size, block_size, 0)
        scores = jnp.dot(q_rows, key_block.T, preferred_element_type=jnp.float32) * score_scale
        valid = block_index * block_size + offsets < length
        return (jnp.where(valid[None, :], scores, -jnp.inf), key_block)

    def raise_max(block_index, row_max):
        scores, key_block = block_scores(block_index)
        return jnp.maximum(row_max, jnp.max(scores, -1))

    row_max = lax.fori_loop(0, block_total, raise_max, jnp.max(tree_scores, -1))
    tree_exps = jnp.exp(tree_scores - row_max[:, None])
    start_totals = jnp.sum(tree_exps, -1)
    start_sums = jnp.dot(
        tree_exps.astype(jnp.bfloat16), new_r[:, :LATENT], preferred_element_type=jnp.float32
    )

    def accumulate(block_index, carry):
        totals, weighted = carry
        scores, key_block = block_scores(block_index)
        exps = jnp.exp(scores - row_max[:, None])
        weighted = weighted + jnp.dot(
            exps.astype(jnp.bfloat16), key_block[:, :LATENT], preferred_element_type=jnp.float32
        )
        return (totals + jnp.sum(exps, -1), weighted)

    totals, weighted = lax.fori_loop(0, block_total, accumulate, (start_totals, start_sums))
    return (weighted / totals[:, None]).astype(jnp.bfloat16)


def attend_dense(q_rows, cache, lengths, new_rows, mask_rows):
    score_scale = (NOPE + ROPE) ** (-0.5)
    cache_slots = cache.shape[1]
    cache_scores = (
        jnp.einsum("rqk,rck->rqc", q_rows, cache, preferred_element_type=jnp.float32) * score_scale
    )
    valid = jnp.arange(cache_slots, dtype=jnp.int32)[None, :] < lengths[:, None]
    cache_scores = jnp.where(valid[:, None, :], cache_scores, -jnp.inf)
    tree_scores = (
        jnp.einsum("rqk,ruk->rqu", q_rows, new_rows, preferred_element_type=jnp.float32)
        * score_scale
    )
    tree_scores = jnp.where(mask_rows, tree_scores, -jnp.inf)
    row_max = jnp.maximum(jnp.max(cache_scores, -1), jnp.max(tree_scores, -1))
    cache_exps = jnp.exp(cache_scores - row_max[..., None])
    tree_exps = jnp.exp(tree_scores - row_max[..., None])
    totals = jnp.sum(cache_exps, -1) + jnp.sum(tree_exps, -1)
    summed = jnp.einsum(
        "rqc,rck->rqk", cache_exps.astype(jnp.bfloat16), cache, preferred_element_type=jnp.float32
    )
    summed = summed + jnp.einsum(
        "rqu,ruk->rqk", tree_exps.astype(jnp.bfloat16), new_rows, preferred_element_type=jnp.float32
    )
    return (summed[..., :LATENT] / totals[..., None]).astype(jnp.bfloat16)


def route_tables(routes, gates, experts_all, capacity):
    tok_rows, top_count = routes.shape
    flat_ids = routes.reshape(-1)
    pair_count = flat_ids.shape[0]
    hit_table = (flat_ids[:, None] == jnp.arange(experts_all, dtype=jnp.int32)[None, :]).astype(
        jnp.bfloat16
    )
    earlier = (
        jnp.arange(pair_count, dtype=jnp.int32)[:, None]
        > jnp.arange(pair_count, dtype=jnp.int32)[None, :]
    ).astype(jnp.bfloat16)
    before = jnp.dot(earlier, hit_table, preferred_element_type=jnp.float32)
    slot_rank = jnp.sum(before * hit_table.astype(jnp.float32), -1).astype(jnp.int32)
    slot_index = flat_ids * capacity + slot_rank
    places = (
        slot_index[:, None] == jnp.arange(experts_all * capacity, dtype=jnp.int32)[None, :]
    ).reshape(tok_rows, top_count, -1)
    pick_table = jnp.any(places, 1).astype(jnp.bfloat16)
    weights = jnp.sum(jnp.where(places, gates[:, :, None], jnp.zeros((), jnp.bfloat16)), 1)
    return (pick_table, weights)


def run_expert(row_set, w_gate, w_up, w_down):
    local_experts = w_gate.shape[0]
    sources = row_set.shape[0] // local_experts
    grouped = row_set.reshape(sources, local_experts, row_set.shape[1], row_set.shape[2])
    gate_act = jnp.einsum("secd,edf->secf", grouped, w_gate, preferred_element_type=jnp.float32)
    up_act = jnp.einsum("secd,edf->secf", grouped, w_up, preferred_element_type=jnp.float32)
    hidden = (jax.nn.silu(gate_act) * up_act).astype(jnp.bfloat16)
    partial_value = jnp.einsum("secf,efd->secd", hidden, w_down, preferred_element_type=jnp.float32)
    return partial_value.reshape(sources * local_experts, row_set.shape[1], -1)


def on_device(
    layer_in,
    q_nope,
    q_pe,
    kv_cache,
    lengths,
    parents,
    accepted,
    kv_a,
    kv_gain,
    w_uk,
    w_uv,
    o_proj,
    post_gain,
    routes,
    gates,
    w_gate,
    w_up,
    w_down,
):
    tok_rows = layer_in.shape[0]
    local_requests, tree_size = parents.shape
    local_heads = q_nope.shape[1] // NOPE
    compressed_part = jnp.dot(layer_in, kv_a, preferred_element_type=jnp.float32).astype(
        jnp.bfloat16
    )
    compressed = lax.all_gather(compressed_part, "tp", axis=1, tiled=True)
    ancestry = jax.vmap(ancestors)(parents)
    depths = jnp.sum(ancestry, -1) - 1.0
    positions = (lengths.astype(jnp.float32)[:, None] + depths).reshape(-1)
    new_rows = make_rows(compressed, kv_gain, positions)
    rows_by_request = new_rows.reshape(local_requests, tree_size, -1)
    accepted_rows = jax.vmap(compact)(ancestry, depths, accepted, rows_by_request)
    query_latent = jnp.einsum(
        "thn,hnl->thl",
        q_nope.reshape(tok_rows, local_heads, NOPE),
        w_uk.reshape(local_heads, NOPE, LATENT),
        preferred_element_type=jnp.float32,
    ).astype(jnp.bfloat16)
    queries = jnp.concatenate([query_latent, q_pe.reshape(tok_rows, local_heads, ROPE)], -1)
    q_rows = queries.reshape(local_requests, tree_size * local_heads, -1)
    mask_rows = jnp.repeat(ancestry > 0, local_heads, axis=1)
    latent_out = attend_dense(q_rows, kv_cache, lengths, rows_by_request, mask_rows)
    latent_out = latent_out.reshape(tok_rows, local_heads, LATENT)
    head_out = jnp.einsum(
        "thl,lhv->thv",
        latent_out,
        w_uv.reshape(LATENT, local_heads, VDIM),
        preferred_element_type=jnp.float32,
    ).astype(jnp.bfloat16)
    experts_all = w_gate.shape[0] * lax.axis_size("req")
    top_count = routes.shape[1]
    capacity = 4 * tok_rows * top_count // (3 * experts_all)
    pick_table, weights = route_tables(routes, gates, experts_all, capacity)
    tp_size = lax.axis_size("tp")
    tp_index = lax.axis_index("tp")
    quarter = D // tp_size
    attention_parts = jnp.einsum(
        "tk,kqf->qtf",
        head_out.reshape(tok_rows, local_heads * VDIM),
        o_proj.reshape(o_proj.shape[0], tp_size, quarter),
        preferred_element_type=jnp.float32,
    )
    attention_quarter = lax.psum_scatter(attention_parts, "tp", scatter_dimension=0, tiled=True)
    attention_quarter = attention_quarter.reshape(tok_rows, quarter)
    hidden_quarter = lax.dynamic_slice_in_dim(layer_in, tp_index * quarter, quarter, 1)
    residual_quarter = hidden_quarter.astype(jnp.float32) + attention_quarter
    square_sum = lax.psum(jnp.sum(residual_quarter * residual_quarter, -1, keepdims=True), "tp")
    gain_quarter = lax.dynamic_slice_in_dim(post_gain, tp_index * quarter, quarter, 0)
    normed_quarter = (
        residual_quarter * lax.rsqrt(square_sum / D + epsilon) * gain_quarter
    ).astype(jnp.bfloat16)
    parity = tp_index % 2
    upper = tp_index // 2
    across = [(t, t ^ 2) for t in range(tp_size)]
    beside = [(t, t ^ 1) for t in range(tp_size)]
    other_quarter = lax.ppermute(normed_quarter, "tp", across)
    half_rows = jnp.where(
        upper == 0,
        jnp.concatenate([normed_quarter, other_quarter], 1),
        jnp.concatenate([other_quarter, normed_quarter], 1),
    )
    outgoing = lax.dot_general(
        pick_table, half_rows, (((0,), (0,)), ((), ())), preferred_element_type=jnp.float32
    ).astype(jnp.bfloat16)
    outgoing = outgoing.reshape(experts_all, capacity, 2 * quarter)

    def features(block, first):
        return lax.dynamic_slice_in_dim(block, first * quarter, quarter, block.ndim - 1)

    chunks = 1
    slot_step = capacity // chunks
    weights_by_slot = weights.reshape(tok_rows, experts_all, capacity)
    routed_half = jnp.zeros((tok_rows, 2 * quarter), jnp.float32)
    for chunk in range(chunks):
        slots = slice(chunk * slot_step, (chunk + 1) * slot_step)
        own_rows = lax.all_to_all(outgoing[:, slots], "req", split_axis=0, concat_axis=0, tiled=True)
        partner_rows = lax.ppermute(own_rows, "tp", beside)
        low_own, high_own = own_rows[..., :quarter], own_rows[..., quarter:]
        low_partner, high_partner = partner_rows[..., :quarter], partner_rows[..., quarter:]
        row_set = jnp.where(
            parity == 0,
            jnp.concatenate([low_own, low_partner, high_own, high_partner], -1),
            jnp.concatenate([low_partner, low_own, high_partner, high_own], -1),
        )
        gate_act = jnp.einsum("scf,fh->sch", row_set, w_gate[0], preferred_element_type=jnp.float32)
        up_act = jnp.einsum("scf,fh->sch", row_set, w_up[0], preferred_element_type=jnp.float32)
        expert_hidden = (jax.nn.silu(gate_act) * up_act).astype(jnp.bfloat16)
        value = jnp.einsum(
            "sch,hf->scf", expert_hidden, w_down[0], preferred_element_type=jnp.float32
        )
        partner_value = jnp.concatenate(
            [features(value, 1 - parity), features(value, 3 - parity)], -1
        ).astype(jnp.bfloat16)
        arrived_value = lax.ppermute(partner_value, "tp", beside)
        own_value = jnp.concatenate([features(value, parity), features(value, parity + 2)], -1)
        pair_value = (own_value + arrived_value.astype(jnp.float32)).astype(jnp.bfloat16)
        shares = lax.all_to_all(pair_value, "req", split_axis=0, concat_axis=0, tiled=True)
        routed_half = routed_half + jnp.dot(
            weights_by_slot[:, :, slots].reshape(tok_rows, experts_all * slot_step),
            shares.reshape(experts_all * slot_step, 2 * quarter),
            preferred_element_type=jnp.float32,
        )
    keep = features(routed_half, upper)
    give = features(routed_half, 1 - upper)
    routed = keep + lax.ppermute(give, "tp", across)
    layer_out = (residual_quarter + routed).astype(jnp.bfloat16)
    return (layer_out, accepted_rows)


def solution(mesh):
    return jax.shard_map(
        on_device,
        mesh=mesh,
        in_specs=(
            P("req", None),
            P("req", "tp"),
            P("req", "tp"),
            P("req", None, None),
            P("req"),
            P("req", None),
            P("req"),
            P(None, "tp"),
            P(),
            P("tp", None),
            P(None, "tp"),
            P("tp", None),
            P(),
            P("req", None),
            P("req", None),
            P("req", None, "tp"),
            P("req", None, "tp"),
            P("req", "tp", None),
        ),
        out_specs=(P("req", "tp"), P("req", None, None)),
        check_vma=False,
    )
```

```python
import jax
import jax.numpy as jnp
from jax import lax
from jax.sharding import PartitionSpec as P

D = 2048
NOPE = 128
ROPE = 64
VDIM = 128
LATENT = 512


epsilon = 1e-06


def ancestors(parent_row):
    tree_size = parent_row.shape[0]
    indices = jnp.arange(tree_size, dtype=jnp.int32)
    link = (
        (parent_row[:, None] == indices[None, :]) | (indices[:, None] == indices[None, :])
    ).astype(jnp.float32)
    for repeat_index in range(tree_size.bit_length()):
        link = jnp.minimum(jnp.dot(link, link, precision=lax.Precision.HIGHEST), 1.0)
    return link


def rotate(vector, positions):
    half_width = vector.shape[-1] // 2
    frequency = 10000.0 ** (-jnp.arange(half_width, dtype=jnp.float32) / half_width)
    angles = positions[:, None] * frequency[None, :]
    first_half = vector[:, :half_width]
    second_half = vector[:, half_width:]
    return jnp.concatenate(
        [
            first_half * jnp.cos(angles) - second_half * jnp.sin(angles),
            first_half * jnp.sin(angles) + second_half * jnp.cos(angles),
        ],
        -1,
    )


def make_rows(compressed, kv_gain, positions):
    latent_raw = compressed[:, :LATENT].astype(jnp.float32)
    new_latent = (
        latent_raw
        * lax.rsqrt(jnp.mean(latent_raw * latent_raw, -1, keepdims=True) + epsilon)
        * kv_gain
    ).astype(jnp.bfloat16)
    new_rotary = rotate(compressed[:, LATENT:].astype(jnp.float32), positions).astype(jnp.bfloat16)
    return jnp.concatenate([new_latent, new_rotary], -1)


def compact(ancestry, depths, node_index, row_set):
    tree_size = ancestry.shape[0]
    chain_mask = jnp.take(ancestry, node_index, axis=0)
    selector = (depths[None, :] == jnp.arange(tree_size, dtype=jnp.float32)[:, None]).astype(
        jnp.float32
    ) * chain_mask[None, :]
    return jnp.dot(
        selector.astype(jnp.bfloat16), row_set, preferred_element_type=jnp.float32
    ).astype(jnp.bfloat16)


def attend_request(q_rows, cache_r, length, new_r, mask_rows):
    score_scale = (NOPE + ROPE) ** (-0.5)
    cache_slots = cache_r.shape[0]
    block_size = min(cache_slots, 512)
    block_total = cache_slots // block_size
    offsets = jnp.arange(block_size, dtype=jnp.int32)
    tree_scores = jnp.dot(q_rows, new_r.T, preferred_element_type=jnp.float32) * score_scale
    tree_scores = jnp.where(mask_rows, tree_scores, -jnp.inf)

    def block_scores(block_index):
        key_block = lax.dynamic_slice_in_dim(cache_r, block_index * block_size, block_size, 0)
        scores = jnp.dot(q_rows, key_block.T, preferred_element_type=jnp.float32) * score_scale
        valid = block_index * block_size + offsets < length
        return (jnp.where(valid[None, :], scores, -jnp.inf), key_block)

    def raise_max(block_index, row_max):
        scores, key_block = block_scores(block_index)
        return jnp.maximum(row_max, jnp.max(scores, -1))

    row_max = lax.fori_loop(0, block_total, raise_max, jnp.max(tree_scores, -1))
    tree_exps = jnp.exp(tree_scores - row_max[:, None])
    start_totals = jnp.sum(tree_exps, -1)
    start_sums = jnp.dot(
        tree_exps.astype(jnp.bfloat16), new_r[:, :LATENT], preferred_element_type=jnp.float32
    )

    def accumulate(block_index, carry):
        totals, weighted = carry
        scores, key_block = block_scores(block_index)
        exps = jnp.exp(scores - row_max[:, None])
        weighted = weighted + jnp.dot(
            exps.astype(jnp.bfloat16), key_block[:, :LATENT], preferred_element_type=jnp.float32
        )
        return (totals + jnp.sum(exps, -1), weighted)

    totals, weighted = lax.fori_loop(0, block_total, accumulate, (start_totals, start_sums))
    return (weighted / totals[:, None]).astype(jnp.bfloat16)


def attend_dense(q_rows, cache, lengths, new_rows, mask_rows):
    score_scale = (NOPE + ROPE) ** (-0.5)
    cache_slots = cache.shape[1]
    cache_scores = (
        jnp.einsum("rqk,rck->rqc", q_rows, cache, preferred_element_type=jnp.float32) * score_scale
    )
    valid = jnp.arange(cache_slots, dtype=jnp.int32)[None, :] < lengths[:, None]
    cache_scores = jnp.where(valid[:, None, :], cache_scores, -jnp.inf)
    tree_scores = (
        jnp.einsum("rqk,ruk->rqu", q_rows, new_rows, preferred_element_type=jnp.float32)
        * score_scale
    )
    tree_scores = jnp.where(mask_rows, tree_scores, -jnp.inf)
    row_max = jnp.maximum(jnp.max(cache_scores, -1), jnp.max(tree_scores, -1))
    cache_exps = jnp.exp(cache_scores - row_max[..., None])
    tree_exps = jnp.exp(tree_scores - row_max[..., None])
    totals = jnp.sum(cache_exps, -1) + jnp.sum(tree_exps, -1)
    summed = jnp.einsum(
        "rqc,rck->rqk", cache_exps.astype(jnp.bfloat16), cache, preferred_element_type=jnp.float32
    )
    summed = summed + jnp.einsum(
        "rqu,ruk->rqk", tree_exps.astype(jnp.bfloat16), new_rows, preferred_element_type=jnp.float32
    )
    return (summed[..., :LATENT] / totals[..., None]).astype(jnp.bfloat16)


def route_tables(routes, gates, experts_all, capacity):
    tok_rows, top_count = routes.shape
    flat_ids = routes.reshape(-1)
    pair_count = flat_ids.shape[0]
    hit_table = (flat_ids[:, None] == jnp.arange(experts_all, dtype=jnp.int32)[None, :]).astype(
        jnp.bfloat16
    )
    earlier = (
        jnp.arange(pair_count, dtype=jnp.int32)[:, None]
        > jnp.arange(pair_count, dtype=jnp.int32)[None, :]
    ).astype(jnp.bfloat16)
    before = jnp.dot(earlier, hit_table, preferred_element_type=jnp.float32)
    slot_rank = jnp.sum(before * hit_table.astype(jnp.float32), -1).astype(jnp.int32)
    slot_index = flat_ids * capacity + slot_rank
    places = (
        slot_index[:, None] == jnp.arange(experts_all * capacity, dtype=jnp.int32)[None, :]
    ).reshape(tok_rows, top_count, -1)
    pick_table = jnp.any(places, 1).astype(jnp.bfloat16)
    weights = jnp.sum(jnp.where(places, gates[:, :, None], jnp.zeros((), jnp.bfloat16)), 1)
    return (pick_table, weights)


def run_expert(row_set, w_gate, w_up, w_down):
    local_experts = w_gate.shape[0]
    sources = row_set.shape[0] // local_experts
    grouped = row_set.reshape(sources, local_experts, row_set.shape[1], row_set.shape[2])
    gate_act = jnp.einsum("secd,edf->secf", grouped, w_gate, preferred_element_type=jnp.float32)
    up_act = jnp.einsum("secd,edf->secf", grouped, w_up, preferred_element_type=jnp.float32)
    hidden = (jax.nn.silu(gate_act) * up_act).astype(jnp.bfloat16)
    partial_value = jnp.einsum("secf,efd->secd", hidden, w_down, preferred_element_type=jnp.float32)
    return partial_value.reshape(sources * local_experts, row_set.shape[1], -1)


def on_device(
    layer_in,
    q_nope,
    q_pe,
    kv_cache,
    lengths,
    parents,
    accepted,
    kv_a,
    kv_gain,
    w_uk,
    w_uv,
    o_proj,
    post_gain,
    routes,
    gates,
    w_gate,
    w_up,
    w_down,
):
    tok_rows = layer_in.shape[0]
    local_requests, tree_size = parents.shape
    local_heads = q_nope.shape[1] // NOPE
    compressed_part = jnp.dot(layer_in, kv_a, preferred_element_type=jnp.float32).astype(
        jnp.bfloat16
    )
    compressed = lax.all_gather(compressed_part, "tp", axis=1, tiled=True)
    tp_size = lax.axis_size("tp")
    tp_index = lax.axis_index("tp")
    quarter = D // tp_size
    parity = tp_index % 2
    beside = [(t, t ^ 1) for t in range(tp_size)]

    def features(block, first):
        return lax.dynamic_slice_in_dim(block, first * quarter, quarter, block.ndim - 1)

    down_local = w_down[0]
    down_own = jnp.concatenate([features(down_local, parity), features(down_local, parity + 2)], -1)
    down_given = jnp.concatenate(
        [features(down_local, 1 - parity), features(down_local, 3 - parity)], -1
    )
    down_partner = lax.ppermute(down_given, "tp", beside)
    down_partner, compressed = lax.optimization_barrier((down_partner, compressed))
    ancestry = jax.vmap(ancestors)(parents)
    depths = jnp.sum(ancestry, -1) - 1.0
    positions = (lengths.astype(jnp.float32)[:, None] + depths).reshape(-1)
    new_rows = make_rows(compressed, kv_gain, positions)
    rows_by_request = new_rows.reshape(local_requests, tree_size, -1)
    accepted_rows = jax.vmap(compact)(ancestry, depths, accepted, rows_by_request)
    query_latent = jnp.einsum(
        "thn,hnl->thl",
        q_nope.reshape(tok_rows, local_heads, NOPE),
        w_uk.reshape(local_heads, NOPE, LATENT),
        preferred_element_type=jnp.float32,
    ).astype(jnp.bfloat16)
    queries = jnp.concatenate([query_latent, q_pe.reshape(tok_rows, local_heads, ROPE)], -1)
    q_rows = queries.reshape(local_requests, tree_size * local_heads, -1)
    mask_rows = jnp.repeat(ancestry > 0, local_heads, axis=1)
    latent_out = attend_dense(q_rows, kv_cache, lengths, rows_by_request, mask_rows)
    latent_out = latent_out.reshape(tok_rows, local_heads, LATENT)
    head_out = jnp.einsum(
        "thl,lhv->thv",
        latent_out,
        w_uv.reshape(LATENT, local_heads, VDIM),
        preferred_element_type=jnp.float32,
    ).astype(jnp.bfloat16)
    experts_all = w_gate.shape[0] * lax.axis_size("req")
    top_count = routes.shape[1]
    capacity = 4 * tok_rows * top_count // (3 * experts_all)
    pick_table, weights = route_tables(routes, gates, experts_all, capacity)
    attention_parts = jnp.einsum(
        "tk,kqf->qtf",
        head_out.reshape(tok_rows, local_heads * VDIM),
        o_proj.reshape(o_proj.shape[0], tp_size, quarter),
        preferred_element_type=jnp.float32,
    )
    attention_quarter = lax.psum_scatter(attention_parts, "tp", scatter_dimension=0, tiled=True)
    attention_quarter = attention_quarter.reshape(tok_rows, quarter)
    hidden_quarter = lax.dynamic_slice_in_dim(layer_in, tp_index * quarter, quarter, 1)
    residual_quarter = hidden_quarter.astype(jnp.float32) + attention_quarter
    square_sum = lax.psum(jnp.sum(residual_quarter * residual_quarter, -1, keepdims=True), "tp")
    gain_quarter = lax.dynamic_slice_in_dim(post_gain, tp_index * quarter, quarter, 0)
    normed_quarter = (
        residual_quarter * lax.rsqrt(square_sum / D + epsilon) * gain_quarter
    ).astype(jnp.bfloat16)
    upper = tp_index // 2
    across = [(t, t ^ 2) for t in range(tp_size)]
    other_quarter = lax.ppermute(normed_quarter, "tp", across)
    half_rows = jnp.where(
        upper == 0,
        jnp.concatenate([normed_quarter, other_quarter], 1),
        jnp.concatenate([other_quarter, normed_quarter], 1),
    )
    outgoing = lax.dot_general(
        pick_table, half_rows, (((0,), (0,)), ((), ())), preferred_element_type=jnp.float32
    ).astype(jnp.bfloat16)
    outgoing = outgoing.reshape(experts_all, capacity, 2 * quarter)

    chunks = 1
    slot_step = capacity // chunks
    weights_by_slot = weights.reshape(tok_rows, experts_all, capacity)
    routed_half = jnp.zeros((tok_rows, 2 * quarter), jnp.float32)
    for chunk in range(chunks):
        slots = slice(chunk * slot_step, (chunk + 1) * slot_step)
        own_rows = lax.all_to_all(outgoing[:, slots], "req", split_axis=0, concat_axis=0, tiled=True)
        partner_rows = lax.ppermute(own_rows, "tp", beside)
        low_own, high_own = own_rows[..., :quarter], own_rows[..., quarter:]
        low_partner, high_partner = partner_rows[..., :quarter], partner_rows[..., quarter:]
        row_set = jnp.where(
            parity == 0,
            jnp.concatenate([low_own, low_partner, high_own, high_partner], -1),
            jnp.concatenate([low_partner, low_own, high_partner, high_own], -1),
        )
        gate_act = jnp.einsum("scf,fh->sch", row_set, w_gate[0], preferred_element_type=jnp.float32)
        up_act = jnp.einsum("scf,fh->sch", row_set, w_up[0], preferred_element_type=jnp.float32)
        expert_hidden = (jax.nn.silu(gate_act) * up_act).astype(jnp.bfloat16)
        partner_hidden = lax.ppermute(expert_hidden, "tp", beside)
        pair_value = (
            jnp.einsum("sch,hf->scf", expert_hidden, down_own, preferred_element_type=jnp.float32)
            + jnp.einsum(
                "sch,hf->scf", partner_hidden, down_partner, preferred_element_type=jnp.float32
            )
        ).astype(jnp.bfloat16)
        shares = lax.all_to_all(pair_value, "req", split_axis=0, concat_axis=0, tiled=True)
        routed_half = routed_half + jnp.dot(
            weights_by_slot[:, :, slots].reshape(tok_rows, experts_all * slot_step),
            shares.reshape(experts_all * slot_step, 2 * quarter),
            preferred_element_type=jnp.float32,
        )
    keep = features(routed_half, upper)
    give = features(routed_half, 1 - upper)
    routed = keep + lax.ppermute(give, "tp", across)
    layer_out = (residual_quarter + routed).astype(jnp.bfloat16)
    return (layer_out, accepted_rows)


def solution(mesh):
    return jax.shard_map(
        on_device,
        mesh=mesh,
        in_specs=(
            P("req", None),
            P("req", "tp"),
            P("req", "tp"),
            P("req", None, None),
            P("req"),
            P("req", None),
            P("req"),
            P(None, "tp"),
            P(),
            P("tp", None),
            P(None, "tp"),
            P("tp", None),
            P(),
            P("req", None),
            P("req", None),
            P("req", None, "tp"),
            P("req", None, "tp"),
            P("req", "tp", None),
        ),
        out_specs=(P("req", "tp"), P("req", None, None)),
        check_vma=False,
    )
```

```python
import jax
import jax.numpy as jnp
from jax import lax
from jax.sharding import PartitionSpec as P

D = 2048
NOPE = 128
ROPE = 64
VDIM = 128
LATENT = 512


epsilon = 1e-06


def ancestors(parent_row):
    tree_size = parent_row.shape[0]
    indices = jnp.arange(tree_size, dtype=jnp.int32)
    link = (
        (parent_row[:, None] == indices[None, :]) | (indices[:, None] == indices[None, :])
    ).astype(jnp.float32)
    for repeat_index in range(tree_size.bit_length()):
        link = jnp.minimum(jnp.dot(link, link, precision=lax.Precision.HIGHEST), 1.0)
    return link


def rotate(vector, positions):
    half_width = vector.shape[-1] // 2
    frequency = 10000.0 ** (-jnp.arange(half_width, dtype=jnp.float32) / half_width)
    angles = positions[:, None] * frequency[None, :]
    first_half = vector[:, :half_width]
    second_half = vector[:, half_width:]
    return jnp.concatenate(
        [
            first_half * jnp.cos(angles) - second_half * jnp.sin(angles),
            first_half * jnp.sin(angles) + second_half * jnp.cos(angles),
        ],
        -1,
    )


def make_rows(compressed, kv_gain, positions):
    latent_raw = compressed[:, :LATENT].astype(jnp.float32)
    new_latent = (
        latent_raw
        * lax.rsqrt(jnp.mean(latent_raw * latent_raw, -1, keepdims=True) + epsilon)
        * kv_gain
    ).astype(jnp.bfloat16)
    new_rotary = rotate(compressed[:, LATENT:].astype(jnp.float32), positions).astype(jnp.bfloat16)
    return jnp.concatenate([new_latent, new_rotary], -1)


def compact(ancestry, depths, node_index, row_set):
    tree_size = ancestry.shape[0]
    chain_mask = jnp.take(ancestry, node_index, axis=0)
    selector = (depths[None, :] == jnp.arange(tree_size, dtype=jnp.float32)[:, None]).astype(
        jnp.float32
    ) * chain_mask[None, :]
    return jnp.dot(
        selector.astype(jnp.bfloat16), row_set, preferred_element_type=jnp.float32
    ).astype(jnp.bfloat16)


def attend_request(q_rows, cache_r, length, new_r, mask_rows):
    score_scale = (NOPE + ROPE) ** (-0.5)
    cache_slots = cache_r.shape[0]
    block_size = min(cache_slots, 512)
    block_total = cache_slots // block_size
    offsets = jnp.arange(block_size, dtype=jnp.int32)
    tree_scores = jnp.dot(q_rows, new_r.T, preferred_element_type=jnp.float32) * score_scale
    tree_scores = jnp.where(mask_rows, tree_scores, -jnp.inf)

    def block_scores(block_index):
        key_block = lax.dynamic_slice_in_dim(cache_r, block_index * block_size, block_size, 0)
        scores = jnp.dot(q_rows, key_block.T, preferred_element_type=jnp.float32) * score_scale
        valid = block_index * block_size + offsets < length
        return (jnp.where(valid[None, :], scores, -jnp.inf), key_block)

    def raise_max(block_index, row_max):
        scores, key_block = block_scores(block_index)
        return jnp.maximum(row_max, jnp.max(scores, -1))

    row_max = lax.fori_loop(0, block_total, raise_max, jnp.max(tree_scores, -1))
    tree_exps = jnp.exp(tree_scores - row_max[:, None])
    start_totals = jnp.sum(tree_exps, -1)
    start_sums = jnp.dot(
        tree_exps.astype(jnp.bfloat16), new_r[:, :LATENT], preferred_element_type=jnp.float32
    )

    def accumulate(block_index, carry):
        totals, weighted = carry
        scores, key_block = block_scores(block_index)
        exps = jnp.exp(scores - row_max[:, None])
        weighted = weighted + jnp.dot(
            exps.astype(jnp.bfloat16), key_block[:, :LATENT], preferred_element_type=jnp.float32
        )
        return (totals + jnp.sum(exps, -1), weighted)

    totals, weighted = lax.fori_loop(0, block_total, accumulate, (start_totals, start_sums))
    return (weighted / totals[:, None]).astype(jnp.bfloat16)


def attend_dense(q_rows, cache, lengths, new_rows, mask_rows):
    score_scale = (NOPE + ROPE) ** (-0.5)
    cache_slots = cache.shape[1]
    cache_scores = (
        jnp.einsum("rqk,rck->rqc", q_rows, cache, preferred_element_type=jnp.float32) * score_scale
    )
    valid = jnp.arange(cache_slots, dtype=jnp.int32)[None, :] < lengths[:, None]
    cache_scores = jnp.where(valid[:, None, :], cache_scores, -jnp.inf)
    tree_scores = (
        jnp.einsum("rqk,ruk->rqu", q_rows, new_rows, preferred_element_type=jnp.float32)
        * score_scale
    )
    tree_scores = jnp.where(mask_rows, tree_scores, -jnp.inf)
    row_max = jnp.maximum(jnp.max(cache_scores, -1), jnp.max(tree_scores, -1))
    cache_exps = jnp.exp(cache_scores - row_max[..., None])
    tree_exps = jnp.exp(tree_scores - row_max[..., None])
    totals = jnp.sum(cache_exps, -1) + jnp.sum(tree_exps, -1)
    summed = jnp.einsum(
        "rqc,rck->rqk", cache_exps.astype(jnp.bfloat16), cache, preferred_element_type=jnp.float32
    )
    summed = summed + jnp.einsum(
        "rqu,ruk->rqk", tree_exps.astype(jnp.bfloat16), new_rows, preferred_element_type=jnp.float32
    )
    return (summed[..., :LATENT] / totals[..., None]).astype(jnp.bfloat16)


def route_tables(routes, gates, experts_all, capacity):
    tok_rows, top_count = routes.shape
    flat_ids = routes.reshape(-1)
    pair_count = flat_ids.shape[0]
    hit_table = (flat_ids[:, None] == jnp.arange(experts_all, dtype=jnp.int32)[None, :]).astype(
        jnp.bfloat16
    )
    earlier = (
        jnp.arange(pair_count, dtype=jnp.int32)[:, None]
        > jnp.arange(pair_count, dtype=jnp.int32)[None, :]
    ).astype(jnp.bfloat16)
    before = jnp.dot(earlier, hit_table, preferred_element_type=jnp.float32)
    slot_rank = jnp.sum(before * hit_table.astype(jnp.float32), -1).astype(jnp.int32)
    slot_index = flat_ids * capacity + slot_rank
    places = (
        slot_index[:, None] == jnp.arange(experts_all * capacity, dtype=jnp.int32)[None, :]
    ).reshape(tok_rows, top_count, -1)
    pick_table = jnp.any(places, 1).astype(jnp.bfloat16)
    weights = jnp.sum(jnp.where(places, gates[:, :, None], jnp.zeros((), jnp.bfloat16)), 1)
    return (pick_table, weights)


def run_expert(row_set, w_gate, w_up, w_down):
    local_experts = w_gate.shape[0]
    sources = row_set.shape[0] // local_experts
    grouped = row_set.reshape(sources, local_experts, row_set.shape[1], row_set.shape[2])
    gate_act = jnp.einsum("secd,edf->secf", grouped, w_gate, preferred_element_type=jnp.float32)
    up_act = jnp.einsum("secd,edf->secf", grouped, w_up, preferred_element_type=jnp.float32)
    hidden = (jax.nn.silu(gate_act) * up_act).astype(jnp.bfloat16)
    partial_value = jnp.einsum("secf,efd->secd", hidden, w_down, preferred_element_type=jnp.float32)
    return partial_value.reshape(sources * local_experts, row_set.shape[1], -1)


def on_device(
    layer_in,
    q_nope,
    q_pe,
    kv_cache,
    lengths,
    parents,
    accepted,
    kv_a,
    kv_gain,
    w_uk,
    w_uv,
    o_proj,
    post_gain,
    routes,
    gates,
    w_gate,
    w_up,
    w_down,
):
    tok_rows = layer_in.shape[0]
    local_requests, tree_size = parents.shape
    local_heads = q_nope.shape[1] // NOPE
    compressed_part = jnp.dot(layer_in, kv_a, preferred_element_type=jnp.float32).astype(
        jnp.bfloat16
    )
    compressed = lax.all_gather(compressed_part, "tp", axis=1, tiled=True)
    tp_size = lax.axis_size("tp")
    tp_index = lax.axis_index("tp")
    quarter = D // tp_size
    parity = tp_index % 2
    beside = [(t, t ^ 1) for t in range(tp_size)]

    def features(block, first):
        return lax.dynamic_slice_in_dim(block, first * quarter, quarter, block.ndim - 1)

    down_local = w_down[0]
    down_own = jnp.concatenate([features(down_local, parity), features(down_local, parity + 2)], -1)
    down_given = jnp.concatenate(
        [features(down_local, 1 - parity), features(down_local, 3 - parity)], -1
    )
    down_partner = lax.ppermute(down_given, "tp", beside)
    down_partner, compressed = lax.optimization_barrier((down_partner, compressed))
    ancestry = jax.vmap(ancestors)(parents)
    depths = jnp.sum(ancestry, -1) - 1.0
    positions = (lengths.astype(jnp.float32)[:, None] + depths).reshape(-1)
    new_rows = make_rows(compressed, kv_gain, positions)
    rows_by_request = new_rows.reshape(local_requests, tree_size, -1)
    accepted_rows = jax.vmap(compact)(ancestry, depths, accepted, rows_by_request)
    query_latent = jnp.einsum(
        "thn,hnl->thl",
        q_nope.reshape(tok_rows, local_heads, NOPE),
        w_uk.reshape(local_heads, NOPE, LATENT),
        preferred_element_type=jnp.float32,
    ).astype(jnp.bfloat16)
    queries = jnp.concatenate([query_latent, q_pe.reshape(tok_rows, local_heads, ROPE)], -1)
    q_rows = queries.reshape(local_requests, tree_size * local_heads, -1)
    mask_rows = jnp.repeat(ancestry > 0, local_heads, axis=1)
    latent_out = attend_dense(q_rows, kv_cache, lengths, rows_by_request, mask_rows)
    latent_out = latent_out.reshape(tok_rows, local_heads, LATENT)
    head_out = jnp.einsum(
        "thl,lhv->thv",
        latent_out,
        w_uv.reshape(LATENT, local_heads, VDIM),
        preferred_element_type=jnp.float32,
    ).astype(jnp.bfloat16)
    experts_all = w_gate.shape[0] * lax.axis_size("req")
    top_count = routes.shape[1]
    capacity = 4 * tok_rows * top_count // (3 * experts_all)
    pick_table, weights = route_tables(routes, gates, experts_all, capacity)
    upper = tp_index // 2
    across = [(t, t ^ 2) for t in range(tp_size)]

    def half_of(block, which):
        return jnp.concatenate([features(block, which), features(block, which + 2)], -1)

    attention = jnp.dot(
        head_out.reshape(tok_rows, local_heads * VDIM), o_proj, preferred_element_type=jnp.float32
    )
    pair_sum = half_of(attention, parity) + lax.ppermute(
        half_of(attention, 1 - parity).astype(jnp.bfloat16), "tp", beside
    ).astype(jnp.float32)
    attention_half = pair_sum + lax.ppermute(
        pair_sum.astype(jnp.bfloat16), "tp", across
    ).astype(jnp.float32)
    residual_half = half_of(layer_in, parity).astype(jnp.float32) + attention_half
    half_squares = jnp.sum(residual_half * residual_half, -1, keepdims=True)
    square_sum = half_squares + lax.ppermute(half_squares, "tp", beside)
    residual_quarter = features(residual_half, upper)
    gain_half = half_of(post_gain, parity)
    half_rows = (residual_half * lax.rsqrt(square_sum / D + epsilon) * gain_half).astype(
        jnp.bfloat16
    )
    outgoing = lax.dot_general(
        pick_table, half_rows, (((0,), (0,)), ((), ())), preferred_element_type=jnp.float32
    ).astype(jnp.bfloat16)
    outgoing = outgoing.reshape(experts_all, capacity, 2 * quarter)

    chunks = 1
    slot_step = capacity // chunks
    weights_by_slot = weights.reshape(tok_rows, experts_all, capacity)
    routed_half = jnp.zeros((tok_rows, 2 * quarter), jnp.float32)
    for chunk in range(chunks):
        slots = slice(chunk * slot_step, (chunk + 1) * slot_step)
        own_rows = lax.all_to_all(outgoing[:, slots], "req", split_axis=0, concat_axis=0, tiled=True)
        partner_rows = lax.ppermute(own_rows, "tp", beside)
        low_own, high_own = own_rows[..., :quarter], own_rows[..., quarter:]
        low_partner, high_partner = partner_rows[..., :quarter], partner_rows[..., quarter:]
        row_set = jnp.where(
            parity == 0,
            jnp.concatenate([low_own, low_partner, high_own, high_partner], -1),
            jnp.concatenate([low_partner, low_own, high_partner, high_own], -1),
        )
        gate_act = jnp.einsum("scf,fh->sch", row_set, w_gate[0], preferred_element_type=jnp.float32)
        up_act = jnp.einsum("scf,fh->sch", row_set, w_up[0], preferred_element_type=jnp.float32)
        expert_hidden = (jax.nn.silu(gate_act) * up_act).astype(jnp.bfloat16)
        partner_hidden = lax.ppermute(expert_hidden, "tp", beside)
        pair_value = (
            jnp.einsum("sch,hf->scf", expert_hidden, down_own, preferred_element_type=jnp.float32)
            + jnp.einsum(
                "sch,hf->scf", partner_hidden, down_partner, preferred_element_type=jnp.float32
            )
        ).astype(jnp.bfloat16)
        shares = lax.all_to_all(pair_value, "req", split_axis=0, concat_axis=0, tiled=True)
        routed_half = routed_half + jnp.dot(
            weights_by_slot[:, :, slots].reshape(tok_rows, experts_all * slot_step),
            shares.reshape(experts_all * slot_step, 2 * quarter),
            preferred_element_type=jnp.float32,
        )
    keep = features(routed_half, upper)
    give = features(routed_half, 1 - upper)
    routed = keep + lax.ppermute(give.astype(jnp.bfloat16), "tp", across).astype(jnp.float32)
    layer_out = (residual_quarter + routed).astype(jnp.bfloat16)
    return (layer_out, accepted_rows)


def solution(mesh):
    return jax.shard_map(
        on_device,
        mesh=mesh,
        in_specs=(
            P("req", None),
            P("req", "tp"),
            P("req", "tp"),
            P("req", None, None),
            P("req"),
            P("req", None),
            P("req"),
            P(None, "tp"),
            P(),
            P("tp", None),
            P(None, "tp"),
            P("tp", None),
            P(),
            P("req", None),
            P("req", None),
            P("req", None, "tp"),
            P("req", None, "tp"),
            P("req", "tp", None),
        ),
        out_specs=(P("req", "tp"), P("req", None, None)),
        check_vma=False,
    )
```

```python
import jax
import jax.numpy as jnp
from jax import lax
from jax.sharding import PartitionSpec as P

D = 2048
NOPE = 128
ROPE = 64
VDIM = 128
LATENT = 512


epsilon = 1e-06


def ancestors(parent_row):
    tree_size = parent_row.shape[0]
    indices = jnp.arange(tree_size, dtype=jnp.int32)
    link = (
        (parent_row[:, None] == indices[None, :]) | (indices[:, None] == indices[None, :])
    ).astype(jnp.float32)
    for repeat_index in range(tree_size.bit_length()):
        link = jnp.minimum(jnp.dot(link, link, precision=lax.Precision.HIGHEST), 1.0)
    return link


def rotate(vector, positions):
    half_width = vector.shape[-1] // 2
    frequency = 10000.0 ** (-jnp.arange(half_width, dtype=jnp.float32) / half_width)
    angles = positions[:, None] * frequency[None, :]
    first_half = vector[:, :half_width]
    second_half = vector[:, half_width:]
    return jnp.concatenate(
        [
            first_half * jnp.cos(angles) - second_half * jnp.sin(angles),
            first_half * jnp.sin(angles) + second_half * jnp.cos(angles),
        ],
        -1,
    )


def make_rows(compressed, kv_gain, positions):
    latent_raw = compressed[:, :LATENT].astype(jnp.float32)
    new_latent = (
        latent_raw
        * lax.rsqrt(jnp.mean(latent_raw * latent_raw, -1, keepdims=True) + epsilon)
        * kv_gain
    ).astype(jnp.bfloat16)
    new_rotary = rotate(compressed[:, LATENT:].astype(jnp.float32), positions).astype(jnp.bfloat16)
    return jnp.concatenate([new_latent, new_rotary], -1)


def compact(ancestry, depths, node_index, row_set):
    tree_size = ancestry.shape[0]
    chain_mask = jnp.take(ancestry, node_index, axis=0)
    selector = (depths[None, :] == jnp.arange(tree_size, dtype=jnp.float32)[:, None]).astype(
        jnp.float32
    ) * chain_mask[None, :]
    return jnp.dot(
        selector.astype(jnp.bfloat16), row_set, preferred_element_type=jnp.float32
    ).astype(jnp.bfloat16)


def attend_request(q_rows, cache_r, length, new_r, mask_rows):
    score_scale = (NOPE + ROPE) ** (-0.5)
    cache_slots = cache_r.shape[0]
    block_size = min(cache_slots, 512)
    block_total = cache_slots // block_size
    offsets = jnp.arange(block_size, dtype=jnp.int32)
    tree_scores = jnp.dot(q_rows, new_r.T, preferred_element_type=jnp.float32) * score_scale
    tree_scores = jnp.where(mask_rows, tree_scores, -jnp.inf)

    def block_scores(block_index):
        key_block = lax.dynamic_slice_in_dim(cache_r, block_index * block_size, block_size, 0)
        scores = jnp.dot(q_rows, key_block.T, preferred_element_type=jnp.float32) * score_scale
        valid = block_index * block_size + offsets < length
        return (jnp.where(valid[None, :], scores, -jnp.inf), key_block)

    def raise_max(block_index, row_max):
        scores, key_block = block_scores(block_index)
        return jnp.maximum(row_max, jnp.max(scores, -1))

    row_max = lax.fori_loop(0, block_total, raise_max, jnp.max(tree_scores, -1))
    tree_exps = jnp.exp(tree_scores - row_max[:, None])
    start_totals = jnp.sum(tree_exps, -1)
    start_sums = jnp.dot(
        tree_exps.astype(jnp.bfloat16), new_r[:, :LATENT], preferred_element_type=jnp.float32
    )

    def accumulate(block_index, carry):
        totals, weighted = carry
        scores, key_block = block_scores(block_index)
        exps = jnp.exp(scores - row_max[:, None])
        weighted = weighted + jnp.dot(
            exps.astype(jnp.bfloat16), key_block[:, :LATENT], preferred_element_type=jnp.float32
        )
        return (totals + jnp.sum(exps, -1), weighted)

    totals, weighted = lax.fori_loop(0, block_total, accumulate, (start_totals, start_sums))
    return (weighted / totals[:, None]).astype(jnp.bfloat16)


def attend_dense(q_rows, cache, lengths, new_rows, mask_rows):
    score_scale = (NOPE + ROPE) ** (-0.5)
    cache_slots = cache.shape[1]
    cache_scores = (
        jnp.einsum("rqk,rck->rqc", q_rows, cache, preferred_element_type=jnp.float32) * score_scale
    )
    valid = jnp.arange(cache_slots, dtype=jnp.int32)[None, :] < lengths[:, None]
    cache_scores = jnp.where(valid[:, None, :], cache_scores, -jnp.inf)
    tree_scores = (
        jnp.einsum("rqk,ruk->rqu", q_rows, new_rows, preferred_element_type=jnp.float32)
        * score_scale
    )
    tree_scores = jnp.where(mask_rows, tree_scores, -jnp.inf)
    row_max = jnp.maximum(jnp.max(cache_scores, -1), jnp.max(tree_scores, -1))
    cache_exps = jnp.exp(cache_scores - row_max[..., None])
    tree_exps = jnp.exp(tree_scores - row_max[..., None])
    totals = jnp.sum(cache_exps, -1) + jnp.sum(tree_exps, -1)
    summed = jnp.einsum(
        "rqc,rck->rqk", cache_exps.astype(jnp.bfloat16), cache, preferred_element_type=jnp.float32
    )
    summed = summed + jnp.einsum(
        "rqu,ruk->rqk", tree_exps.astype(jnp.bfloat16), new_rows, preferred_element_type=jnp.float32
    )
    return (summed[..., :LATENT] / totals[..., None]).astype(jnp.bfloat16)


def route_tables(routes, gates, experts_all, capacity):
    tok_rows, top_count = routes.shape
    flat_ids = routes.reshape(-1)
    pair_count = flat_ids.shape[0]
    hit_table = (flat_ids[:, None] == jnp.arange(experts_all, dtype=jnp.int32)[None, :]).astype(
        jnp.bfloat16
    )
    earlier = (
        jnp.arange(pair_count, dtype=jnp.int32)[:, None]
        > jnp.arange(pair_count, dtype=jnp.int32)[None, :]
    ).astype(jnp.bfloat16)
    before = jnp.dot(earlier, hit_table, preferred_element_type=jnp.float32)
    slot_rank = jnp.sum(before * hit_table.astype(jnp.float32), -1).astype(jnp.int32)
    slot_index = flat_ids * capacity + slot_rank
    places = (
        slot_index[:, None] == jnp.arange(experts_all * capacity, dtype=jnp.int32)[None, :]
    ).reshape(tok_rows, top_count, -1)
    pick_table = jnp.any(places, 1).astype(jnp.bfloat16)
    weights = jnp.sum(jnp.where(places, gates[:, :, None], jnp.zeros((), jnp.bfloat16)), 1)
    return (pick_table, weights)


def run_expert(row_set, w_gate, w_up, w_down):
    local_experts = w_gate.shape[0]
    sources = row_set.shape[0] // local_experts
    grouped = row_set.reshape(sources, local_experts, row_set.shape[1], row_set.shape[2])
    gate_act = jnp.einsum("secd,edf->secf", grouped, w_gate, preferred_element_type=jnp.float32)
    up_act = jnp.einsum("secd,edf->secf", grouped, w_up, preferred_element_type=jnp.float32)
    hidden = (jax.nn.silu(gate_act) * up_act).astype(jnp.bfloat16)
    partial_value = jnp.einsum("secf,efd->secd", hidden, w_down, preferred_element_type=jnp.float32)
    return partial_value.reshape(sources * local_experts, row_set.shape[1], -1)


def on_device(
    layer_in,
    q_nope,
    q_pe,
    kv_cache,
    lengths,
    parents,
    accepted,
    kv_a,
    kv_gain,
    w_uk,
    w_uv,
    o_proj,
    post_gain,
    routes,
    gates,
    w_gate,
    w_up,
    w_down,
):
    tok_rows = layer_in.shape[0]
    local_requests, tree_size = parents.shape
    local_heads = q_nope.shape[1] // NOPE
    compressed_part = jnp.dot(layer_in, kv_a, preferred_element_type=jnp.float32).astype(
        jnp.bfloat16
    )
    tp_size = lax.axis_size("tp")
    tp_index = lax.axis_index("tp")
    quarter = D // tp_size
    parity = tp_index % 2
    beside = [(t, t ^ 1) for t in range(tp_size)]

    def features(block, first):
        return lax.dynamic_slice_in_dim(block, first * quarter, quarter, block.ndim - 1)

    pair_block = jnp.where(
        parity == 0,
        jnp.concatenate([compressed_part, lax.ppermute(compressed_part, "tp", beside)], 1),
        jnp.concatenate([lax.ppermute(compressed_part, "tp", beside), compressed_part], 1),
    )
    other_block = lax.ppermute(pair_block, "tp", [(t, t ^ 2) for t in range(tp_size)])
    compressed = jnp.where(
        tp_index // 2 == 0,
        jnp.concatenate([pair_block, other_block], 1),
        jnp.concatenate([other_block, pair_block], 1),
    )
    down_local = w_down[0]
    down_own = jnp.concatenate([features(down_local, parity), features(down_local, parity + 2)], -1)
    down_given = jnp.concatenate(
        [features(down_local, 1 - parity), features(down_local, 3 - parity)], -1
    )
    down_partner = lax.ppermute(down_given, "tp", beside)
    down_partner, compressed = lax.optimization_barrier((down_partner, compressed))
    ancestry = jax.vmap(ancestors)(parents)
    depths = jnp.sum(ancestry, -1) - 1.0
    positions = (lengths.astype(jnp.float32)[:, None] + depths).reshape(-1)
    new_rows = make_rows(compressed, kv_gain, positions)
    rows_by_request = new_rows.reshape(local_requests, tree_size, -1)
    accepted_rows = jax.vmap(compact)(ancestry, depths, accepted, rows_by_request)
    query_latent = jnp.einsum(
        "thn,hnl->thl",
        q_nope.reshape(tok_rows, local_heads, NOPE),
        w_uk.reshape(local_heads, NOPE, LATENT),
        preferred_element_type=jnp.float32,
    ).astype(jnp.bfloat16)
    queries = jnp.concatenate([query_latent, q_pe.reshape(tok_rows, local_heads, ROPE)], -1)
    q_rows = queries.reshape(local_requests, tree_size * local_heads, -1)
    mask_rows = jnp.repeat(ancestry > 0, local_heads, axis=1)
    latent_out = attend_dense(q_rows, kv_cache, lengths, rows_by_request, mask_rows)
    latent_out = latent_out.reshape(tok_rows, local_heads, LATENT)
    head_out = jnp.einsum(
        "thl,lhv->thv",
        latent_out,
        w_uv.reshape(LATENT, local_heads, VDIM),
        preferred_element_type=jnp.float32,
    ).astype(jnp.bfloat16)
    experts_all = w_gate.shape[0] * lax.axis_size("req")
    top_count = routes.shape[1]
    capacity = 4 * tok_rows * top_count // (3 * experts_all)
    pick_table, weights = route_tables(routes, gates, experts_all, capacity)
    upper = tp_index // 2
    across = [(t, t ^ 2) for t in range(tp_size)]

    def half_of(block, which):
        return jnp.concatenate([features(block, which), features(block, which + 2)], -1)

    attention = jnp.dot(
        head_out.reshape(tok_rows, local_heads * VDIM), o_proj, preferred_element_type=jnp.float32
    )
    pair_sum = half_of(attention, parity) + lax.ppermute(
        half_of(attention, 1 - parity).astype(jnp.bfloat16), "tp", beside
    ).astype(jnp.float32)
    attention_half = pair_sum + lax.ppermute(
        pair_sum.astype(jnp.bfloat16), "tp", across
    ).astype(jnp.float32)
    residual_half = half_of(layer_in, parity).astype(jnp.float32) + attention_half
    half_squares = jnp.sum(residual_half * residual_half, -1, keepdims=True)
    square_sum = half_squares + lax.ppermute(half_squares, "tp", beside)
    residual_quarter = features(residual_half, upper)
    gain_half = half_of(post_gain, parity)
    half_rows = (residual_half * lax.rsqrt(square_sum / D + epsilon) * gain_half).astype(
        jnp.bfloat16
    )
    outgoing = lax.dot_general(
        pick_table, half_rows, (((0,), (0,)), ((), ())), preferred_element_type=jnp.float32
    ).astype(jnp.bfloat16)
    outgoing = outgoing.reshape(experts_all, capacity, 2 * quarter)

    chunks = 1
    slot_step = capacity // chunks
    weights_by_slot = weights.reshape(tok_rows, experts_all, capacity)
    routed_half = jnp.zeros((tok_rows, 2 * quarter), jnp.float32)
    for chunk in range(chunks):
        slots = slice(chunk * slot_step, (chunk + 1) * slot_step)
        own_rows = lax.all_to_all(outgoing[:, slots], "req", split_axis=0, concat_axis=0, tiled=True)
        partner_rows = lax.ppermute(own_rows, "tp", beside)
        low_own, high_own = own_rows[..., :quarter], own_rows[..., quarter:]
        low_partner, high_partner = partner_rows[..., :quarter], partner_rows[..., quarter:]
        row_set = jnp.where(
            parity == 0,
            jnp.concatenate([low_own, low_partner, high_own, high_partner], -1),
            jnp.concatenate([low_partner, low_own, high_partner, high_own], -1),
        )
        gate_act = jnp.einsum("scf,fh->sch", row_set, w_gate[0], preferred_element_type=jnp.float32)
        up_act = jnp.einsum("scf,fh->sch", row_set, w_up[0], preferred_element_type=jnp.float32)
        expert_hidden = (jax.nn.silu(gate_act) * up_act).astype(jnp.bfloat16)
        partner_hidden = lax.ppermute(expert_hidden, "tp", beside)
        pair_value = (
            jnp.einsum("sch,hf->scf", expert_hidden, down_own, preferred_element_type=jnp.float32)
            + jnp.einsum(
                "sch,hf->scf", partner_hidden, down_partner, preferred_element_type=jnp.float32
            )
        ).astype(jnp.bfloat16)
        shares = lax.all_to_all(pair_value, "req", split_axis=0, concat_axis=0, tiled=True)
        routed_half = routed_half + jnp.dot(
            weights_by_slot[:, :, slots].reshape(tok_rows, experts_all * slot_step),
            shares.reshape(experts_all * slot_step, 2 * quarter),
            preferred_element_type=jnp.float32,
        )
    keep = features(routed_half, upper)
    give = features(routed_half, 1 - upper)
    routed = keep + lax.ppermute(give.astype(jnp.bfloat16), "tp", across).astype(jnp.float32)
    layer_out = (residual_quarter + routed).astype(jnp.bfloat16)
    return (layer_out, accepted_rows)


def solution(mesh):
    return jax.shard_map(
        on_device,
        mesh=mesh,
        in_specs=(
            P("req", None),
            P("req", "tp"),
            P("req", "tp"),
            P("req", None, None),
            P("req"),
            P("req", None),
            P("req"),
            P(None, "tp"),
            P(),
            P("tp", None),
            P(None, "tp"),
            P("tp", None),
            P(),
            P("req", None),
            P("req", None),
            P("req", None, "tp"),
            P("req", None, "tp"),
            P("req", "tp", None),
        ),
        out_specs=(P("req", "tp"), P("req", None, None)),
        check_vma=False,
    )
```

```python
import jax
import jax.numpy as jnp
from jax import lax
from jax.sharding import PartitionSpec as P

D = 2048
NOPE = 128
ROPE = 64
VDIM = 128
LATENT = 512


epsilon = 1e-06


def ancestors(parent_row):
    tree_size = parent_row.shape[0]
    indices = jnp.arange(tree_size, dtype=jnp.int32)
    link = (
        (parent_row[:, None] == indices[None, :]) | (indices[:, None] == indices[None, :])
    ).astype(jnp.float32)
    for repeat_index in range(tree_size.bit_length()):
        link = jnp.minimum(jnp.dot(link, link, precision=lax.Precision.HIGHEST), 1.0)
    return link


def rotate(vector, positions):
    half_width = vector.shape[-1] // 2
    frequency = 10000.0 ** (-jnp.arange(half_width, dtype=jnp.float32) / half_width)
    angles = positions[:, None] * frequency[None, :]
    first_half = vector[:, :half_width]
    second_half = vector[:, half_width:]
    return jnp.concatenate(
        [
            first_half * jnp.cos(angles) - second_half * jnp.sin(angles),
            first_half * jnp.sin(angles) + second_half * jnp.cos(angles),
        ],
        -1,
    )


def make_rows(compressed, kv_gain, positions):
    latent_raw = compressed[:, :LATENT].astype(jnp.float32)
    new_latent = (
        latent_raw
        * lax.rsqrt(jnp.mean(latent_raw * latent_raw, -1, keepdims=True) + epsilon)
        * kv_gain
    ).astype(jnp.bfloat16)
    new_rotary = rotate(compressed[:, LATENT:].astype(jnp.float32), positions).astype(jnp.bfloat16)
    return jnp.concatenate([new_latent, new_rotary], -1)


def compact(ancestry, depths, node_index, row_set):
    tree_size = ancestry.shape[0]
    chain_mask = jnp.take(ancestry, node_index, axis=0)
    selector = (depths[None, :] == jnp.arange(tree_size, dtype=jnp.float32)[:, None]).astype(
        jnp.float32
    ) * chain_mask[None, :]
    return jnp.dot(
        selector.astype(jnp.bfloat16), row_set, preferred_element_type=jnp.float32
    ).astype(jnp.bfloat16)


def attend_request(q_rows, cache_r, length, new_r, mask_rows):
    score_scale = (NOPE + ROPE) ** (-0.5)
    cache_slots = cache_r.shape[0]
    block_size = min(cache_slots, 512)
    block_total = cache_slots // block_size
    offsets = jnp.arange(block_size, dtype=jnp.int32)
    tree_scores = jnp.dot(q_rows, new_r.T, preferred_element_type=jnp.float32) * score_scale
    tree_scores = jnp.where(mask_rows, tree_scores, -jnp.inf)

    def block_scores(block_index):
        key_block = lax.dynamic_slice_in_dim(cache_r, block_index * block_size, block_size, 0)
        scores = jnp.dot(q_rows, key_block.T, preferred_element_type=jnp.float32) * score_scale
        valid = block_index * block_size + offsets < length
        return (jnp.where(valid[None, :], scores, -jnp.inf), key_block)

    def raise_max(block_index, row_max):
        scores, key_block = block_scores(block_index)
        return jnp.maximum(row_max, jnp.max(scores, -1))

    row_max = lax.fori_loop(0, block_total, raise_max, jnp.max(tree_scores, -1))
    tree_exps = jnp.exp(tree_scores - row_max[:, None])
    start_totals = jnp.sum(tree_exps, -1)
    start_sums = jnp.dot(
        tree_exps.astype(jnp.bfloat16), new_r[:, :LATENT], preferred_element_type=jnp.float32
    )

    def accumulate(block_index, carry):
        totals, weighted = carry
        scores, key_block = block_scores(block_index)
        exps = jnp.exp(scores - row_max[:, None])
        weighted = weighted + jnp.dot(
            exps.astype(jnp.bfloat16), key_block[:, :LATENT], preferred_element_type=jnp.float32
        )
        return (totals + jnp.sum(exps, -1), weighted)

    totals, weighted = lax.fori_loop(0, block_total, accumulate, (start_totals, start_sums))
    return (weighted / totals[:, None]).astype(jnp.bfloat16)


def attend_dense(q_rows, cache, lengths, new_rows, mask_rows):
    score_scale = (NOPE + ROPE) ** (-0.5)
    cache_slots = cache.shape[1]
    cache_scores = (
        jnp.einsum("rqk,rck->rqc", q_rows, cache, preferred_element_type=jnp.float32) * score_scale
    )
    valid = jnp.arange(cache_slots, dtype=jnp.int32)[None, :] < lengths[:, None]
    cache_scores = jnp.where(valid[:, None, :], cache_scores, -jnp.inf)
    tree_scores = (
        jnp.einsum("rqk,ruk->rqu", q_rows, new_rows, preferred_element_type=jnp.float32)
        * score_scale
    )
    tree_scores = jnp.where(mask_rows, tree_scores, -jnp.inf)
    row_max = jnp.maximum(jnp.max(cache_scores, -1), jnp.max(tree_scores, -1))
    cache_exps = jnp.exp(cache_scores - row_max[..., None])
    tree_exps = jnp.exp(tree_scores - row_max[..., None])
    totals = jnp.sum(cache_exps, -1) + jnp.sum(tree_exps, -1)
    summed = jnp.einsum(
        "rqc,rck->rqk", cache_exps.astype(jnp.bfloat16), cache, preferred_element_type=jnp.float32
    )
    summed = summed + jnp.einsum(
        "rqu,ruk->rqk", tree_exps.astype(jnp.bfloat16), new_rows, preferred_element_type=jnp.float32
    )
    return (summed[..., :LATENT] / totals[..., None]).astype(jnp.bfloat16)


def route_tables(routes, gates, experts_all, capacity):
    tok_rows, top_count = routes.shape
    flat_ids = routes.reshape(-1)
    pair_count = flat_ids.shape[0]
    hit_table = (flat_ids[:, None] == jnp.arange(experts_all, dtype=jnp.int32)[None, :]).astype(
        jnp.bfloat16
    )
    earlier = (
        jnp.arange(pair_count, dtype=jnp.int32)[:, None]
        > jnp.arange(pair_count, dtype=jnp.int32)[None, :]
    ).astype(jnp.bfloat16)
    before = jnp.dot(earlier, hit_table, preferred_element_type=jnp.float32)
    slot_rank = jnp.sum(before * hit_table.astype(jnp.float32), -1).astype(jnp.int32)
    slot_index = flat_ids * capacity + slot_rank
    places = (
        slot_index[:, None] == jnp.arange(experts_all * capacity, dtype=jnp.int32)[None, :]
    ).reshape(tok_rows, top_count, -1)
    pick_table = jnp.any(places, 1).astype(jnp.bfloat16)
    weights = jnp.sum(jnp.where(places, gates[:, :, None], jnp.zeros((), jnp.bfloat16)), 1)
    return (pick_table, weights)


def run_expert(row_set, w_gate, w_up, w_down):
    local_experts = w_gate.shape[0]
    sources = row_set.shape[0] // local_experts
    grouped = row_set.reshape(sources, local_experts, row_set.shape[1], row_set.shape[2])
    gate_act = jnp.einsum("secd,edf->secf", grouped, w_gate, preferred_element_type=jnp.float32)
    up_act = jnp.einsum("secd,edf->secf", grouped, w_up, preferred_element_type=jnp.float32)
    hidden = (jax.nn.silu(gate_act) * up_act).astype(jnp.bfloat16)
    partial_value = jnp.einsum("secf,efd->secd", hidden, w_down, preferred_element_type=jnp.float32)
    return partial_value.reshape(sources * local_experts, row_set.shape[1], -1)


def on_device(
    layer_in,
    q_nope,
    q_pe,
    kv_cache,
    lengths,
    parents,
    accepted,
    kv_a,
    kv_gain,
    w_uk,
    w_uv,
    o_proj,
    post_gain,
    routes,
    gates,
    w_gate,
    w_up,
    w_down,
):
    tok_rows = layer_in.shape[0]
    local_requests, tree_size = parents.shape
    local_heads = q_nope.shape[1] // NOPE
    compressed_part = jnp.dot(layer_in, kv_a, preferred_element_type=jnp.float32).astype(
        jnp.bfloat16
    )
    tp_size = lax.axis_size("tp")
    tp_index = lax.axis_index("tp")
    quarter = D // tp_size
    parity = tp_index % 2
    beside = [(t, t ^ 1) for t in range(tp_size)]

    def features(block, first):
        return lax.dynamic_slice_in_dim(block, first * quarter, quarter, block.ndim - 1)

    pair_block = jnp.where(
        parity == 0,
        jnp.concatenate([compressed_part, lax.ppermute(compressed_part, "tp", beside)], 1),
        jnp.concatenate([lax.ppermute(compressed_part, "tp", beside), compressed_part], 1),
    )
    other_block = lax.ppermute(pair_block, "tp", [(t, t ^ 2) for t in range(tp_size)])
    compressed = jnp.where(
        tp_index // 2 == 0,
        jnp.concatenate([pair_block, other_block], 1),
        jnp.concatenate([other_block, pair_block], 1),
    )
    down_local = w_down[0]
    down_own = jnp.concatenate([features(down_local, parity), features(down_local, parity + 2)], -1)
    down_given = jnp.concatenate(
        [features(down_local, 1 - parity), features(down_local, 3 - parity)], -1
    )
    down_partner = lax.ppermute(down_given, "tp", beside)
    def feature_rows(weight, which):
        return jnp.concatenate(
            [
                lax.dynamic_slice_in_dim(weight, which * quarter, quarter, 0),
                lax.dynamic_slice_in_dim(weight, (which + 2) * quarter, quarter, 0),
            ],
            0,
        )

    gate_up_local = jnp.concatenate([w_gate[0], w_up[0]], 1)
    gate_up_own = feature_rows(gate_up_local, parity)
    gate_up_partner = lax.ppermute(feature_rows(gate_up_local, 1 - parity), "tp", beside)
    down_partner, gate_up_partner, compressed = lax.optimization_barrier(
        (down_partner, gate_up_partner, compressed)
    )
    ancestry = jax.vmap(ancestors)(parents)
    depths = jnp.sum(ancestry, -1) - 1.0
    positions = (lengths.astype(jnp.float32)[:, None] + depths).reshape(-1)
    new_rows = make_rows(compressed, kv_gain, positions)
    rows_by_request = new_rows.reshape(local_requests, tree_size, -1)
    accepted_rows = jax.vmap(compact)(ancestry, depths, accepted, rows_by_request)
    query_latent = jnp.einsum(
        "thn,hnl->thl",
        q_nope.reshape(tok_rows, local_heads, NOPE),
        w_uk.reshape(local_heads, NOPE, LATENT),
        preferred_element_type=jnp.float32,
    ).astype(jnp.bfloat16)
    queries = jnp.concatenate([query_latent, q_pe.reshape(tok_rows, local_heads, ROPE)], -1)
    q_rows = queries.reshape(local_requests, tree_size * local_heads, -1)
    mask_rows = jnp.repeat(ancestry > 0, local_heads, axis=1)
    latent_out = attend_dense(q_rows, kv_cache, lengths, rows_by_request, mask_rows)
    latent_out = latent_out.reshape(tok_rows, local_heads, LATENT)
    head_out = jnp.einsum(
        "thl,lhv->thv",
        latent_out,
        w_uv.reshape(LATENT, local_heads, VDIM),
        preferred_element_type=jnp.float32,
    ).astype(jnp.bfloat16)
    experts_all = w_gate.shape[0] * lax.axis_size("req")
    top_count = routes.shape[1]
    capacity = 4 * tok_rows * top_count // (3 * experts_all)
    pick_table, weights = route_tables(routes, gates, experts_all, capacity)
    upper = tp_index // 2
    across = [(t, t ^ 2) for t in range(tp_size)]

    def half_of(block, which):
        return jnp.concatenate([features(block, which), features(block, which + 2)], -1)

    attention = jnp.dot(
        head_out.reshape(tok_rows, local_heads * VDIM), o_proj, preferred_element_type=jnp.float32
    )
    pair_sum = half_of(attention, parity) + lax.ppermute(
        half_of(attention, 1 - parity).astype(jnp.bfloat16), "tp", beside
    ).astype(jnp.float32)
    attention_half = pair_sum + lax.ppermute(
        pair_sum.astype(jnp.bfloat16), "tp", across
    ).astype(jnp.float32)
    residual_half = half_of(layer_in, parity).astype(jnp.float32) + attention_half
    half_squares = jnp.sum(residual_half * residual_half, -1, keepdims=True)
    square_sum = half_squares + lax.ppermute(half_squares, "tp", beside)
    residual_quarter = features(residual_half, upper)
    gain_half = half_of(post_gain, parity)
    half_rows = (residual_half * lax.rsqrt(square_sum / D + epsilon) * gain_half).astype(
        jnp.bfloat16
    )
    outgoing = lax.dot_general(
        pick_table, half_rows, (((0,), (0,)), ((), ())), preferred_element_type=jnp.float32
    ).astype(jnp.bfloat16)
    outgoing = outgoing.reshape(experts_all, capacity, 2 * quarter)

    chunks = 1
    slot_step = capacity // chunks
    weights_by_slot = weights.reshape(tok_rows, experts_all, capacity)
    routed_half = jnp.zeros((tok_rows, 2 * quarter), jnp.float32)
    for chunk in range(chunks):
        slots = slice(chunk * slot_step, (chunk + 1) * slot_step)
        own_rows = lax.all_to_all(outgoing[:, slots], "req", split_axis=0, concat_axis=0, tiled=True)
        own_part = jnp.einsum(
            "scf,fh->sch", own_rows, gate_up_own, preferred_element_type=jnp.float32
        )
        given_part = jnp.einsum(
            "scf,fh->sch", own_rows, gate_up_partner, preferred_element_type=jnp.float32
        ).astype(jnp.bfloat16)
        pre_act = own_part + lax.ppermute(given_part, "tp", beside).astype(jnp.float32)
        hidden_size = pre_act.shape[-1] // 2
        gate_act, up_act = pre_act[..., :hidden_size], pre_act[..., hidden_size:]
        expert_hidden = (jax.nn.silu(gate_act) * up_act).astype(jnp.bfloat16)
        partner_hidden = lax.ppermute(expert_hidden, "tp", beside)
        pair_value = (
            jnp.einsum("sch,hf->scf", expert_hidden, down_own, preferred_element_type=jnp.float32)
            + jnp.einsum(
                "sch,hf->scf", partner_hidden, down_partner, preferred_element_type=jnp.float32
            )
        ).astype(jnp.bfloat16)
        shares = lax.all_to_all(pair_value, "req", split_axis=0, concat_axis=0, tiled=True)
        routed_half = routed_half + jnp.dot(
            weights_by_slot[:, :, slots].reshape(tok_rows, experts_all * slot_step),
            shares.reshape(experts_all * slot_step, 2 * quarter),
            preferred_element_type=jnp.float32,
        )
    keep = features(routed_half, upper)
    give = features(routed_half, 1 - upper)
    routed = keep + lax.ppermute(give.astype(jnp.bfloat16), "tp", across).astype(jnp.float32)
    layer_out = (residual_quarter + routed).astype(jnp.bfloat16)
    return (layer_out, accepted_rows)


def solution(mesh):
    return jax.shard_map(
        on_device,
        mesh=mesh,
        in_specs=(
            P("req", None),
            P("req", "tp"),
            P("req", "tp"),
            P("req", None, None),
            P("req"),
            P("req", None),
            P("req"),
            P(None, "tp"),
            P(),
            P("tp", None),
            P(None, "tp"),
            P("tp", None),
            P(),
            P("req", None),
            P("req", None),
            P("req", None, "tp"),
            P("req", None, "tp"),
            P("req", "tp", None),
        ),
        out_specs=(P("req", "tp"), P("req", None, None)),
        check_vma=False,
    )
```

```python
import jax
import jax.numpy as jnp
from jax import lax
from jax.sharding import PartitionSpec as P

D = 2048
NOPE = 128
ROPE = 64
VDIM = 128
LATENT = 512


epsilon = 1e-06


def ancestors(parent_row):
    tree_size = parent_row.shape[0]
    indices = jnp.arange(tree_size, dtype=jnp.int32)
    link = (
        (parent_row[:, None] == indices[None, :]) | (indices[:, None] == indices[None, :])
    ).astype(jnp.float32)
    for repeat_index in range(tree_size.bit_length()):
        link = jnp.minimum(jnp.dot(link, link, precision=lax.Precision.HIGHEST), 1.0)
    return link


def rotate(vector, positions):
    half_width = vector.shape[-1] // 2
    frequency = 10000.0 ** (-jnp.arange(half_width, dtype=jnp.float32) / half_width)
    angles = positions[:, None] * frequency[None, :]
    first_half = vector[:, :half_width]
    second_half = vector[:, half_width:]
    return jnp.concatenate(
        [
            first_half * jnp.cos(angles) - second_half * jnp.sin(angles),
            first_half * jnp.sin(angles) + second_half * jnp.cos(angles),
        ],
        -1,
    )


def make_rows(compressed, kv_gain, positions):
    latent_raw = compressed[:, :LATENT].astype(jnp.float32)
    new_latent = (
        latent_raw
        * lax.rsqrt(jnp.mean(latent_raw * latent_raw, -1, keepdims=True) + epsilon)
        * kv_gain
    ).astype(jnp.bfloat16)
    new_rotary = rotate(compressed[:, LATENT:].astype(jnp.float32), positions).astype(jnp.bfloat16)
    return jnp.concatenate([new_latent, new_rotary], -1)


def compact(ancestry, depths, node_index, row_set):
    tree_size = ancestry.shape[0]
    chain_mask = jnp.take(ancestry, node_index, axis=0)
    selector = (depths[None, :] == jnp.arange(tree_size, dtype=jnp.float32)[:, None]).astype(
        jnp.float32
    ) * chain_mask[None, :]
    return jnp.dot(
        selector.astype(jnp.bfloat16), row_set, preferred_element_type=jnp.float32
    ).astype(jnp.bfloat16)


def attend_request(q_rows, cache_r, length, new_r, mask_rows):
    score_scale = (NOPE + ROPE) ** (-0.5)
    cache_slots = cache_r.shape[0]
    block_size = min(cache_slots, 512)
    block_total = cache_slots // block_size
    offsets = jnp.arange(block_size, dtype=jnp.int32)
    tree_scores = jnp.dot(q_rows, new_r.T, preferred_element_type=jnp.float32) * score_scale
    tree_scores = jnp.where(mask_rows, tree_scores, -jnp.inf)

    def block_scores(block_index):
        key_block = lax.dynamic_slice_in_dim(cache_r, block_index * block_size, block_size, 0)
        scores = jnp.dot(q_rows, key_block.T, preferred_element_type=jnp.float32) * score_scale
        valid = block_index * block_size + offsets < length
        return (jnp.where(valid[None, :], scores, -jnp.inf), key_block)

    def raise_max(block_index, row_max):
        scores, key_block = block_scores(block_index)
        return jnp.maximum(row_max, jnp.max(scores, -1))

    row_max = lax.fori_loop(0, block_total, raise_max, jnp.max(tree_scores, -1))
    tree_exps = jnp.exp(tree_scores - row_max[:, None])
    start_totals = jnp.sum(tree_exps, -1)
    start_sums = jnp.dot(
        tree_exps.astype(jnp.bfloat16), new_r[:, :LATENT], preferred_element_type=jnp.float32
    )

    def accumulate(block_index, carry):
        totals, weighted = carry
        scores, key_block = block_scores(block_index)
        exps = jnp.exp(scores - row_max[:, None])
        weighted = weighted + jnp.dot(
            exps.astype(jnp.bfloat16), key_block[:, :LATENT], preferred_element_type=jnp.float32
        )
        return (totals + jnp.sum(exps, -1), weighted)

    totals, weighted = lax.fori_loop(0, block_total, accumulate, (start_totals, start_sums))
    return (weighted / totals[:, None]).astype(jnp.bfloat16)


def attend_dense(q_rows, cache, lengths, new_rows, mask_rows):
    score_scale = (NOPE + ROPE) ** (-0.5)
    cache_slots = cache.shape[1]
    cache_scores = (
        jnp.einsum("rqk,rck->rqc", q_rows, cache, preferred_element_type=jnp.float32) * score_scale
    )
    valid = jnp.arange(cache_slots, dtype=jnp.int32)[None, :] < lengths[:, None]
    cache_scores = jnp.where(valid[:, None, :], cache_scores, -jnp.inf)
    tree_scores = (
        jnp.einsum("rqk,ruk->rqu", q_rows, new_rows, preferred_element_type=jnp.float32)
        * score_scale
    )
    tree_scores = jnp.where(mask_rows, tree_scores, -jnp.inf)
    row_max = jnp.maximum(jnp.max(cache_scores, -1), jnp.max(tree_scores, -1))
    cache_exps = jnp.exp(cache_scores - row_max[..., None])
    tree_exps = jnp.exp(tree_scores - row_max[..., None])
    totals = jnp.sum(cache_exps, -1) + jnp.sum(tree_exps, -1)
    summed = jnp.einsum(
        "rqc,rck->rqk", cache_exps.astype(jnp.bfloat16), cache, preferred_element_type=jnp.float32
    )
    summed = summed + jnp.einsum(
        "rqu,ruk->rqk", tree_exps.astype(jnp.bfloat16), new_rows, preferred_element_type=jnp.float32
    )
    return (summed[..., :LATENT] / totals[..., None]).astype(jnp.bfloat16)


def route_tables(routes, gates, experts_all, capacity):
    tok_rows, top_count = routes.shape
    flat_ids = routes.reshape(-1)
    pair_count = flat_ids.shape[0]
    hit_table = (flat_ids[:, None] == jnp.arange(experts_all, dtype=jnp.int32)[None, :]).astype(
        jnp.bfloat16
    )
    earlier = (
        jnp.arange(pair_count, dtype=jnp.int32)[:, None]
        > jnp.arange(pair_count, dtype=jnp.int32)[None, :]
    ).astype(jnp.bfloat16)
    before = jnp.dot(earlier, hit_table, preferred_element_type=jnp.float32)
    slot_rank = jnp.sum(before * hit_table.astype(jnp.float32), -1).astype(jnp.int32)
    slot_index = flat_ids * capacity + slot_rank
    places = (
        slot_index[:, None] == jnp.arange(experts_all * capacity, dtype=jnp.int32)[None, :]
    ).reshape(tok_rows, top_count, -1)
    pick_table = jnp.any(places, 1).astype(jnp.bfloat16)
    weights = jnp.sum(jnp.where(places, gates[:, :, None], jnp.zeros((), jnp.bfloat16)), 1)
    return (pick_table, weights)


def run_expert(row_set, w_gate, w_up, w_down):
    local_experts = w_gate.shape[0]
    sources = row_set.shape[0] // local_experts
    grouped = row_set.reshape(sources, local_experts, row_set.shape[1], row_set.shape[2])
    gate_act = jnp.einsum("secd,edf->secf", grouped, w_gate, preferred_element_type=jnp.float32)
    up_act = jnp.einsum("secd,edf->secf", grouped, w_up, preferred_element_type=jnp.float32)
    hidden = (jax.nn.silu(gate_act) * up_act).astype(jnp.bfloat16)
    partial_value = jnp.einsum("secf,efd->secd", hidden, w_down, preferred_element_type=jnp.float32)
    return partial_value.reshape(sources * local_experts, row_set.shape[1], -1)


def on_device(
    layer_in,
    q_nope,
    q_pe,
    kv_cache,
    lengths,
    parents,
    accepted,
    kv_a,
    kv_gain,
    w_uk,
    w_uv,
    o_proj,
    post_gain,
    routes,
    gates,
    w_gate,
    w_up,
    w_down,
):
    tok_rows = layer_in.shape[0]
    local_requests, tree_size = parents.shape
    local_heads = q_nope.shape[1] // NOPE
    compressed_part = jnp.dot(layer_in, kv_a, preferred_element_type=jnp.float32).astype(
        jnp.bfloat16
    )
    tp_size = lax.axis_size("tp")
    tp_index = lax.axis_index("tp")
    quarter = D // tp_size
    parity = tp_index % 2
    beside = [(t, t ^ 1) for t in range(tp_size)]

    def features(block, first):
        return lax.dynamic_slice_in_dim(block, first * quarter, quarter, block.ndim - 1)

    pair_block = jnp.where(
        parity == 0,
        jnp.concatenate([compressed_part, lax.ppermute(compressed_part, "tp", beside)], 1),
        jnp.concatenate([lax.ppermute(compressed_part, "tp", beside), compressed_part], 1),
    )
    other_block = lax.ppermute(pair_block, "tp", [(t, t ^ 2) for t in range(tp_size)])
    compressed = jnp.where(
        tp_index // 2 == 0,
        jnp.concatenate([pair_block, other_block], 1),
        jnp.concatenate([other_block, pair_block], 1),
    )
    down_local = w_down[0]
    down_own = jnp.concatenate([features(down_local, parity), features(down_local, parity + 2)], -1)
    down_given = jnp.concatenate(
        [features(down_local, 1 - parity), features(down_local, 3 - parity)], -1
    )
    down_partner = lax.ppermute(down_given, "tp", beside)
    down_partner, compressed = lax.optimization_barrier((down_partner, compressed))
    ancestry = jax.vmap(ancestors)(parents)
    depths = jnp.sum(ancestry, -1) - 1.0
    positions = (lengths.astype(jnp.float32)[:, None] + depths).reshape(-1)
    new_rows = make_rows(compressed, kv_gain, positions)
    rows_by_request = new_rows.reshape(local_requests, tree_size, -1)
    accepted_rows = jax.vmap(compact)(ancestry, depths, accepted, rows_by_request)
    query_latent = jnp.einsum(
        "thn,hnl->thl",
        q_nope.reshape(tok_rows, local_heads, NOPE),
        w_uk.reshape(local_heads, NOPE, LATENT),
        preferred_element_type=jnp.float32,
    ).astype(jnp.bfloat16)
    queries = jnp.concatenate([query_latent, q_pe.reshape(tok_rows, local_heads, ROPE)], -1)
    experts_all = w_gate.shape[0] * lax.axis_size("req")
    top_count = routes.shape[1]
    capacity = 4 * tok_rows * top_count // (3 * experts_all)
    pick_table, weights = route_tables(routes, gates, experts_all, capacity)
    upper = tp_index // 2
    across = [(t, t ^ 2) for t in range(tp_size)]

    def half_of(block, which):
        return jnp.concatenate([features(block, which), features(block, which + 2)], -1)

    q_rows = queries.reshape(local_requests, tree_size * local_heads, -1)
    mask_rows = jnp.repeat(ancestry > 0, local_heads, axis=1)
    gain_half = half_of(post_gain, parity)
    half_parts, quarter_parts = [], []
    for request in range(local_requests):
        picked = slice(request, request + 1)
        tokens = slice(request * tree_size, (request + 1) * tree_size)
        latent_out = attend_dense(
            q_rows[picked], kv_cache[picked], lengths[picked], rows_by_request[picked],
            mask_rows[picked],
        ).reshape(tree_size, local_heads, LATENT)
        head_out = jnp.einsum(
            "thl,lhv->thv",
            latent_out,
            w_uv.reshape(LATENT, local_heads, VDIM),
            preferred_element_type=jnp.float32,
        ).astype(jnp.bfloat16)
        attention = jnp.dot(
            head_out.reshape(tree_size, local_heads * VDIM), o_proj,
            preferred_element_type=jnp.float32,
        )
        pair_sum = half_of(attention, parity) + lax.ppermute(
            half_of(attention, 1 - parity).astype(jnp.bfloat16), "tp", beside
        ).astype(jnp.float32)
        attention_half = pair_sum + lax.ppermute(
            pair_sum.astype(jnp.bfloat16), "tp", across
        ).astype(jnp.float32)
        residual_half = half_of(layer_in[tokens], parity).astype(jnp.float32) + attention_half
        half_squares = jnp.sum(residual_half * residual_half, -1, keepdims=True)
        square_sum = half_squares + lax.ppermute(half_squares, "tp", beside)
        quarter_parts.append(features(residual_half, upper))
        half_parts.append(
            (residual_half * lax.rsqrt(square_sum / D + epsilon) * gain_half).astype(jnp.bfloat16)
        )
    residual_quarter = jnp.concatenate(quarter_parts, 0)
    half_rows = jnp.concatenate(half_parts, 0)
    outgoing = lax.dot_general(
        pick_table, half_rows, (((0,), (0,)), ((), ())), preferred_element_type=jnp.float32
    ).astype(jnp.bfloat16)
    outgoing = outgoing.reshape(experts_all, capacity, 2 * quarter)

    chunks = 1
    slot_step = capacity // chunks
    weights_by_slot = weights.reshape(tok_rows, experts_all, capacity)
    routed_half = jnp.zeros((tok_rows, 2 * quarter), jnp.float32)
    for chunk in range(chunks):
        slots = slice(chunk * slot_step, (chunk + 1) * slot_step)
        own_rows = lax.all_to_all(outgoing[:, slots], "req", split_axis=0, concat_axis=0, tiled=True)
        partner_rows = lax.ppermute(own_rows, "tp", beside)
        low_own, high_own = own_rows[..., :quarter], own_rows[..., quarter:]
        low_partner, high_partner = partner_rows[..., :quarter], partner_rows[..., quarter:]
        row_set = jnp.where(
            parity == 0,
            jnp.concatenate([low_own, low_partner, high_own, high_partner], -1),
            jnp.concatenate([low_partner, low_own, high_partner, high_own], -1),
        )
        gate_act = jnp.einsum("scf,fh->sch", row_set, w_gate[0], preferred_element_type=jnp.float32)
        up_act = jnp.einsum("scf,fh->sch", row_set, w_up[0], preferred_element_type=jnp.float32)
        expert_hidden = (jax.nn.silu(gate_act) * up_act).astype(jnp.bfloat16)
        partner_hidden = lax.ppermute(expert_hidden, "tp", beside)
        pair_value = (
            jnp.einsum("sch,hf->scf", expert_hidden, down_own, preferred_element_type=jnp.float32)
            + jnp.einsum(
                "sch,hf->scf", partner_hidden, down_partner, preferred_element_type=jnp.float32
            )
        ).astype(jnp.bfloat16)
        shares = lax.all_to_all(pair_value, "req", split_axis=0, concat_axis=0, tiled=True)
        routed_half = routed_half + jnp.dot(
            weights_by_slot[:, :, slots].reshape(tok_rows, experts_all * slot_step),
            shares.reshape(experts_all * slot_step, 2 * quarter),
            preferred_element_type=jnp.float32,
        )
    keep = features(routed_half, upper)
    give = features(routed_half, 1 - upper)
    routed = keep + lax.ppermute(give.astype(jnp.bfloat16), "tp", across).astype(jnp.float32)
    layer_out = (residual_quarter + routed).astype(jnp.bfloat16)
    return (layer_out, accepted_rows)


def solution(mesh):
    return jax.shard_map(
        on_device,
        mesh=mesh,
        in_specs=(
            P("req", None),
            P("req", "tp"),
            P("req", "tp"),
            P("req", None, None),
            P("req"),
            P("req", None),
            P("req"),
            P(None, "tp"),
            P(),
            P("tp", None),
            P(None, "tp"),
            P("tp", None),
            P(),
            P("req", None),
            P("req", None),
            P("req", None, "tp"),
            P("req", None, "tp"),
            P("req", "tp", None),
        ),
        out_specs=(P("req", "tp"), P("req", None, None)),
        check_vma=False,
    )
```

```python
import jax
import jax.numpy as jnp
from jax import lax
from jax.sharding import PartitionSpec as P

D = 2048
NOPE = 128
ROPE = 64
VDIM = 128
LATENT = 512


epsilon = 1e-06


def ancestors(parent_row):
    tree_size = parent_row.shape[0]
    indices = jnp.arange(tree_size, dtype=jnp.int32)
    link = (
        (parent_row[:, None] == indices[None, :]) | (indices[:, None] == indices[None, :])
    ).astype(jnp.float32)
    for repeat_index in range(tree_size.bit_length()):
        link = jnp.minimum(jnp.dot(link, link, precision=lax.Precision.HIGHEST), 1.0)
    return link


def rotate(vector, positions):
    half_width = vector.shape[-1] // 2
    frequency = 10000.0 ** (-jnp.arange(half_width, dtype=jnp.float32) / half_width)
    angles = positions[:, None] * frequency[None, :]
    first_half = vector[:, :half_width]
    second_half = vector[:, half_width:]
    return jnp.concatenate(
        [
            first_half * jnp.cos(angles) - second_half * jnp.sin(angles),
            first_half * jnp.sin(angles) + second_half * jnp.cos(angles),
        ],
        -1,
    )


def make_rows(compressed, kv_gain, positions):
    latent_raw = compressed[:, :LATENT].astype(jnp.float32)
    new_latent = (
        latent_raw
        * lax.rsqrt(jnp.mean(latent_raw * latent_raw, -1, keepdims=True) + epsilon)
        * kv_gain
    ).astype(jnp.bfloat16)
    new_rotary = rotate(compressed[:, LATENT:].astype(jnp.float32), positions).astype(jnp.bfloat16)
    return jnp.concatenate([new_latent, new_rotary], -1)


def compact(ancestry, depths, node_index, row_set):
    tree_size = ancestry.shape[0]
    chain_mask = jnp.take(ancestry, node_index, axis=0)
    selector = (depths[None, :] == jnp.arange(tree_size, dtype=jnp.float32)[:, None]).astype(
        jnp.float32
    ) * chain_mask[None, :]
    return jnp.dot(
        selector.astype(jnp.bfloat16), row_set, preferred_element_type=jnp.float32
    ).astype(jnp.bfloat16)


def attend_request(q_rows, cache_r, length, new_r, mask_rows):
    score_scale = (NOPE + ROPE) ** (-0.5)
    cache_slots = cache_r.shape[0]
    block_size = min(cache_slots, 512)
    block_total = cache_slots // block_size
    offsets = jnp.arange(block_size, dtype=jnp.int32)
    tree_scores = jnp.dot(q_rows, new_r.T, preferred_element_type=jnp.float32) * score_scale
    tree_scores = jnp.where(mask_rows, tree_scores, -jnp.inf)

    def block_scores(block_index):
        key_block = lax.dynamic_slice_in_dim(cache_r, block_index * block_size, block_size, 0)
        scores = jnp.dot(q_rows, key_block.T, preferred_element_type=jnp.float32) * score_scale
        valid = block_index * block_size + offsets < length
        return (jnp.where(valid[None, :], scores, -jnp.inf), key_block)

    def raise_max(block_index, row_max):
        scores, key_block = block_scores(block_index)
        return jnp.maximum(row_max, jnp.max(scores, -1))

    row_max = lax.fori_loop(0, block_total, raise_max, jnp.max(tree_scores, -1))
    tree_exps = jnp.exp(tree_scores - row_max[:, None])
    start_totals = jnp.sum(tree_exps, -1)
    start_sums = jnp.dot(
        tree_exps.astype(jnp.bfloat16), new_r[:, :LATENT], preferred_element_type=jnp.float32
    )

    def accumulate(block_index, carry):
        totals, weighted = carry
        scores, key_block = block_scores(block_index)
        exps = jnp.exp(scores - row_max[:, None])
        weighted = weighted + jnp.dot(
            exps.astype(jnp.bfloat16), key_block[:, :LATENT], preferred_element_type=jnp.float32
        )
        return (totals + jnp.sum(exps, -1), weighted)

    totals, weighted = lax.fori_loop(0, block_total, accumulate, (start_totals, start_sums))
    return (weighted / totals[:, None]).astype(jnp.bfloat16)


def attend_dense(q_rows, cache, lengths, new_rows, mask_rows):
    score_scale = (NOPE + ROPE) ** (-0.5)
    cache_slots = cache.shape[1]
    cache_scores = (
        jnp.einsum("rqk,rck->rqc", q_rows, cache, preferred_element_type=jnp.float32) * score_scale
    )
    valid = jnp.arange(cache_slots, dtype=jnp.int32)[None, :] < lengths[:, None]
    cache_scores = jnp.where(valid[:, None, :], cache_scores, -jnp.inf)
    tree_scores = (
        jnp.einsum("rqk,ruk->rqu", q_rows, new_rows, preferred_element_type=jnp.float32)
        * score_scale
    )
    tree_scores = jnp.where(mask_rows, tree_scores, -jnp.inf)
    row_max = jnp.maximum(jnp.max(cache_scores, -1), jnp.max(tree_scores, -1))
    cache_exps = jnp.exp(cache_scores - row_max[..., None])
    tree_exps = jnp.exp(tree_scores - row_max[..., None])
    totals = jnp.sum(cache_exps, -1) + jnp.sum(tree_exps, -1)
    summed = jnp.einsum(
        "rqc,rck->rqk", cache_exps.astype(jnp.bfloat16), cache, preferred_element_type=jnp.float32
    )
    summed = summed + jnp.einsum(
        "rqu,ruk->rqk", tree_exps.astype(jnp.bfloat16), new_rows, preferred_element_type=jnp.float32
    )
    return (summed[..., :LATENT] / totals[..., None]).astype(jnp.bfloat16)


def route_tables(routes, gates, experts_all, capacity):
    tok_rows, top_count = routes.shape
    flat_ids = routes.reshape(-1)
    pair_count = flat_ids.shape[0]
    hit_table = (flat_ids[:, None] == jnp.arange(experts_all, dtype=jnp.int32)[None, :]).astype(
        jnp.bfloat16
    )
    earlier = (
        jnp.arange(pair_count, dtype=jnp.int32)[:, None]
        > jnp.arange(pair_count, dtype=jnp.int32)[None, :]
    ).astype(jnp.bfloat16)
    before = jnp.dot(earlier, hit_table, preferred_element_type=jnp.float32)
    slot_rank = jnp.sum(before * hit_table.astype(jnp.float32), -1).astype(jnp.int32)
    slot_index = flat_ids * capacity + slot_rank
    places = (
        slot_index[:, None] == jnp.arange(experts_all * capacity, dtype=jnp.int32)[None, :]
    ).reshape(tok_rows, top_count, -1)
    pick_table = jnp.any(places, 1).astype(jnp.bfloat16)
    weights = jnp.sum(jnp.where(places, gates[:, :, None], jnp.zeros((), jnp.bfloat16)), 1)
    return (pick_table, weights)


def run_expert(row_set, w_gate, w_up, w_down):
    local_experts = w_gate.shape[0]
    sources = row_set.shape[0] // local_experts
    grouped = row_set.reshape(sources, local_experts, row_set.shape[1], row_set.shape[2])
    gate_act = jnp.einsum("secd,edf->secf", grouped, w_gate, preferred_element_type=jnp.float32)
    up_act = jnp.einsum("secd,edf->secf", grouped, w_up, preferred_element_type=jnp.float32)
    hidden = (jax.nn.silu(gate_act) * up_act).astype(jnp.bfloat16)
    partial_value = jnp.einsum("secf,efd->secd", hidden, w_down, preferred_element_type=jnp.float32)
    return partial_value.reshape(sources * local_experts, row_set.shape[1], -1)


def on_device(
    layer_in,
    q_nope,
    q_pe,
    kv_cache,
    lengths,
    parents,
    accepted,
    kv_a,
    kv_gain,
    w_uk,
    w_uv,
    o_proj,
    post_gain,
    routes,
    gates,
    w_gate,
    w_up,
    w_down,
):
    tok_rows = layer_in.shape[0]
    local_requests, tree_size = parents.shape
    local_heads = q_nope.shape[1] // NOPE
    compressed_part = jnp.dot(layer_in, kv_a, preferred_element_type=jnp.float32).astype(
        jnp.bfloat16
    )
    tp_size = lax.axis_size("tp")
    tp_index = lax.axis_index("tp")
    quarter = D // tp_size
    parity = tp_index % 2
    beside = [(t, t ^ 1) for t in range(tp_size)]

    def features(block, first):
        return lax.dynamic_slice_in_dim(block, first * quarter, quarter, block.ndim - 1)

    pair_block = jnp.where(
        parity == 0,
        jnp.concatenate([compressed_part, lax.ppermute(compressed_part, "tp", beside)], 1),
        jnp.concatenate([lax.ppermute(compressed_part, "tp", beside), compressed_part], 1),
    )
    other_block = lax.ppermute(pair_block, "tp", [(t, t ^ 2) for t in range(tp_size)])
    compressed = jnp.where(
        tp_index // 2 == 0,
        jnp.concatenate([pair_block, other_block], 1),
        jnp.concatenate([other_block, pair_block], 1),
    )
    down_local = w_down[0]
    down_own = jnp.concatenate([features(down_local, parity), features(down_local, parity + 2)], -1)
    down_given = jnp.concatenate(
        [features(down_local, 1 - parity), features(down_local, 3 - parity)], -1
    )
    down_partner = lax.ppermute(down_given, "tp", beside)
    down_partner, compressed = lax.optimization_barrier((down_partner, compressed))
    ancestry = jax.vmap(ancestors)(parents)
    depths = jnp.sum(ancestry, -1) - 1.0
    positions = (lengths.astype(jnp.float32)[:, None] + depths).reshape(-1)
    new_rows = make_rows(compressed, kv_gain, positions)
    rows_by_request = new_rows.reshape(local_requests, tree_size, -1)
    accepted_rows = jax.vmap(compact)(ancestry, depths, accepted, rows_by_request)
    query_latent = jnp.einsum(
        "thn,hnl->thl",
        q_nope.reshape(tok_rows, local_heads, NOPE),
        w_uk.reshape(local_heads, NOPE, LATENT),
        preferred_element_type=jnp.float32,
    ).astype(jnp.bfloat16)
    queries = jnp.concatenate([query_latent, q_pe.reshape(tok_rows, local_heads, ROPE)], -1)
    q_rows = queries.reshape(local_requests, tree_size * local_heads, -1)
    mask_rows = jnp.repeat(ancestry > 0, local_heads, axis=1)
    latent_out = attend_dense(q_rows, kv_cache, lengths, rows_by_request, mask_rows)
    latent_out = latent_out.reshape(tok_rows, local_heads, LATENT)
    head_out = jnp.einsum(
        "thl,lhv->thv",
        latent_out,
        w_uv.reshape(LATENT, local_heads, VDIM),
        preferred_element_type=jnp.float32,
    ).astype(jnp.bfloat16)
    experts_all = w_gate.shape[0] * lax.axis_size("req")
    top_count = routes.shape[1]
    capacity = 4 * tok_rows * top_count // (3 * experts_all)
    pick_table, weights = route_tables(routes, gates, experts_all, capacity)
    upper = tp_index // 2
    across = [(t, t ^ 2) for t in range(tp_size)]

    def half_of(block, which):
        return jnp.concatenate([features(block, which), features(block, which + 2)], -1)

    attention = jnp.dot(
        head_out.reshape(tok_rows, local_heads * VDIM), o_proj, preferred_element_type=jnp.float32
    )
    pair_sum = half_of(attention, parity) + lax.ppermute(
        half_of(attention, 1 - parity).astype(jnp.bfloat16), "tp", beside
    ).astype(jnp.float32)
    attention_half = pair_sum + lax.ppermute(
        pair_sum.astype(jnp.bfloat16), "tp", across
    ).astype(jnp.float32)
    residual_half = half_of(layer_in, parity).astype(jnp.float32) + attention_half
    half_squares = jnp.sum(residual_half * residual_half, -1, keepdims=True)
    square_sum = half_squares + lax.ppermute(half_squares, "tp", beside)
    residual_quarter = features(residual_half, upper)
    gain_half = half_of(post_gain, parity)
    half_rows = (residual_half * lax.rsqrt(square_sum / D + epsilon) * gain_half).astype(
        jnp.bfloat16
    )
    outgoing = lax.dot_general(
        pick_table, half_rows, (((0,), (0,)), ((), ())), preferred_element_type=jnp.float32
    ).astype(jnp.bfloat16)
    outgoing = outgoing.reshape(experts_all, capacity, 2 * quarter)

    def feature_rows(weight, which):
        return jnp.concatenate(
            [
                lax.dynamic_slice_in_dim(weight, which * quarter, quarter, 0),
                lax.dynamic_slice_in_dim(weight, (which + 2) * quarter, quarter, 0),
            ],
            0,
        )

    chunks = 1
    slot_step = capacity // chunks
    weights_by_slot = weights.reshape(tok_rows, experts_all, capacity)
    routed_half = jnp.zeros((tok_rows, 2 * quarter), jnp.float32)
    for chunk in range(chunks):
        slots = slice(chunk * slot_step, (chunk + 1) * slot_step)
        own_rows = lax.all_to_all(outgoing[:, slots], "req", split_axis=0, concat_axis=0, tiled=True)
        partner_rows = lax.ppermute(own_rows, "tp", beside)
        gate_act = jnp.einsum(
            "scf,fh->sch", own_rows, feature_rows(w_gate[0], parity),
            preferred_element_type=jnp.float32,
        ) + jnp.einsum(
            "scf,fh->sch", partner_rows, feature_rows(w_gate[0], 1 - parity),
            preferred_element_type=jnp.float32,
        )
        up_act = jnp.einsum(
            "scf,fh->sch", own_rows, feature_rows(w_up[0], parity),
            preferred_element_type=jnp.float32,
        ) + jnp.einsum(
            "scf,fh->sch", partner_rows, feature_rows(w_up[0], 1 - parity),
            preferred_element_type=jnp.float32,
        )
        expert_hidden = (jax.nn.silu(gate_act) * up_act).astype(jnp.bfloat16)
        partner_hidden = lax.ppermute(expert_hidden, "tp", beside)
        pair_value = (
            jnp.einsum("sch,hf->scf", expert_hidden, down_own, preferred_element_type=jnp.float32)
            + jnp.einsum(
                "sch,hf->scf", partner_hidden, down_partner, preferred_element_type=jnp.float32
            )
        ).astype(jnp.bfloat16)
        shares = lax.all_to_all(pair_value, "req", split_axis=0, concat_axis=0, tiled=True)
        routed_half = routed_half + jnp.dot(
            weights_by_slot[:, :, slots].reshape(tok_rows, experts_all * slot_step),
            shares.reshape(experts_all * slot_step, 2 * quarter),
            preferred_element_type=jnp.float32,
        )
    keep = features(routed_half, upper)
    give = features(routed_half, 1 - upper)
    routed = keep + lax.ppermute(give.astype(jnp.bfloat16), "tp", across).astype(jnp.float32)
    layer_out = (residual_quarter + routed).astype(jnp.bfloat16)
    return (layer_out, accepted_rows)


def solution(mesh):
    return jax.shard_map(
        on_device,
        mesh=mesh,
        in_specs=(
            P("req", None),
            P("req", "tp"),
            P("req", "tp"),
            P("req", None, None),
            P("req"),
            P("req", None),
            P("req"),
            P(None, "tp"),
            P(),
            P("tp", None),
            P(None, "tp"),
            P("tp", None),
            P(),
            P("req", None),
            P("req", None),
            P("req", None, "tp"),
            P("req", None, "tp"),
            P("req", "tp", None),
        ),
        out_specs=(P("req", "tp"), P("req", None, None)),
        check_vma=False,
    )
```

```python
import jax
import jax.numpy as jnp
from jax import lax
from jax.sharding import PartitionSpec as P

D = 2048
NOPE = 128
ROPE = 64
VDIM = 128
LATENT = 512


epsilon = 1e-06


def ancestors(parent_row):
    tree_size = parent_row.shape[0]
    indices = jnp.arange(tree_size, dtype=jnp.int32)
    link = (
        (parent_row[:, None] == indices[None, :]) | (indices[:, None] == indices[None, :])
    ).astype(jnp.float32)
    for repeat_index in range(tree_size.bit_length()):
        link = jnp.minimum(jnp.dot(link, link, precision=lax.Precision.HIGHEST), 1.0)
    return link


def rotate(vector, positions):
    half_width = vector.shape[-1] // 2
    frequency = 10000.0 ** (-jnp.arange(half_width, dtype=jnp.float32) / half_width)
    angles = positions[:, None] * frequency[None, :]
    first_half = vector[:, :half_width]
    second_half = vector[:, half_width:]
    return jnp.concatenate(
        [
            first_half * jnp.cos(angles) - second_half * jnp.sin(angles),
            first_half * jnp.sin(angles) + second_half * jnp.cos(angles),
        ],
        -1,
    )


def make_rows(compressed, kv_gain, positions):
    latent_raw = compressed[:, :LATENT].astype(jnp.float32)
    new_latent = (
        latent_raw
        * lax.rsqrt(jnp.mean(latent_raw * latent_raw, -1, keepdims=True) + epsilon)
        * kv_gain
    ).astype(jnp.bfloat16)
    new_rotary = rotate(compressed[:, LATENT:].astype(jnp.float32), positions).astype(jnp.bfloat16)
    return jnp.concatenate([new_latent, new_rotary], -1)


def compact(ancestry, depths, node_index, row_set):
    tree_size = ancestry.shape[0]
    chain_mask = jnp.take(ancestry, node_index, axis=0)
    selector = (depths[None, :] == jnp.arange(tree_size, dtype=jnp.float32)[:, None]).astype(
        jnp.float32
    ) * chain_mask[None, :]
    return jnp.dot(
        selector.astype(jnp.bfloat16), row_set, preferred_element_type=jnp.float32
    ).astype(jnp.bfloat16)


def attend_request(q_rows, cache_r, length, new_r, mask_rows):
    score_scale = (NOPE + ROPE) ** (-0.5)
    cache_slots = cache_r.shape[0]
    block_size = min(cache_slots, 512)
    block_total = cache_slots // block_size
    offsets = jnp.arange(block_size, dtype=jnp.int32)
    tree_scores = jnp.dot(q_rows, new_r.T, preferred_element_type=jnp.float32) * score_scale
    tree_scores = jnp.where(mask_rows, tree_scores, -jnp.inf)

    def block_scores(block_index):
        key_block = lax.dynamic_slice_in_dim(cache_r, block_index * block_size, block_size, 0)
        scores = jnp.dot(q_rows, key_block.T, preferred_element_type=jnp.float32) * score_scale
        valid = block_index * block_size + offsets < length
        return (jnp.where(valid[None, :], scores, -jnp.inf), key_block)

    def raise_max(block_index, row_max):
        scores, key_block = block_scores(block_index)
        return jnp.maximum(row_max, jnp.max(scores, -1))

    row_max = lax.fori_loop(0, block_total, raise_max, jnp.max(tree_scores, -1))
    tree_exps = jnp.exp(tree_scores - row_max[:, None])
    start_totals = jnp.sum(tree_exps, -1)
    start_sums = jnp.dot(
        tree_exps.astype(jnp.bfloat16), new_r[:, :LATENT], preferred_element_type=jnp.float32
    )

    def accumulate(block_index, carry):
        totals, weighted = carry
        scores, key_block = block_scores(block_index)
        exps = jnp.exp(scores - row_max[:, None])
        weighted = weighted + jnp.dot(
            exps.astype(jnp.bfloat16), key_block[:, :LATENT], preferred_element_type=jnp.float32
        )
        return (totals + jnp.sum(exps, -1), weighted)

    totals, weighted = lax.fori_loop(0, block_total, accumulate, (start_totals, start_sums))
    return (weighted / totals[:, None]).astype(jnp.bfloat16)


def attend_dense(q_rows, cache, lengths, new_rows, mask_rows):
    score_scale = (NOPE + ROPE) ** (-0.5)
    cache_slots = cache.shape[1]
    cache_scores = (
        jnp.einsum("rqk,rck->rqc", q_rows, cache, preferred_element_type=jnp.float32) * score_scale
    )
    valid = jnp.arange(cache_slots, dtype=jnp.int32)[None, :] < lengths[:, None]
    cache_scores = jnp.where(valid[:, None, :], cache_scores, -jnp.inf)
    tree_scores = (
        jnp.einsum("rqk,ruk->rqu", q_rows, new_rows, preferred_element_type=jnp.float32)
        * score_scale
    )
    tree_scores = jnp.where(mask_rows, tree_scores, -jnp.inf)
    row_max = jnp.maximum(jnp.max(cache_scores, -1), jnp.max(tree_scores, -1))
    cache_exps = jnp.exp(cache_scores - row_max[..., None])
    tree_exps = jnp.exp(tree_scores - row_max[..., None])
    totals = jnp.sum(cache_exps, -1) + jnp.sum(tree_exps, -1)
    summed = jnp.einsum(
        "rqc,rck->rqk", cache_exps.astype(jnp.bfloat16), cache, preferred_element_type=jnp.float32
    )
    summed = summed + jnp.einsum(
        "rqu,ruk->rqk", tree_exps.astype(jnp.bfloat16), new_rows, preferred_element_type=jnp.float32
    )
    return (summed[..., :LATENT] / totals[..., None]).astype(jnp.bfloat16)


def route_tables(routes, gates, experts_all, capacity):
    tok_rows, top_count = routes.shape
    flat_ids = routes.reshape(-1)
    pair_count = flat_ids.shape[0]
    hit_table = (flat_ids[:, None] == jnp.arange(experts_all, dtype=jnp.int32)[None, :]).astype(
        jnp.bfloat16
    )
    earlier = (
        jnp.arange(pair_count, dtype=jnp.int32)[:, None]
        > jnp.arange(pair_count, dtype=jnp.int32)[None, :]
    ).astype(jnp.bfloat16)
    before = jnp.dot(earlier, hit_table, preferred_element_type=jnp.float32)
    slot_rank = jnp.sum(before * hit_table.astype(jnp.float32), -1).astype(jnp.int32)
    slot_index = flat_ids * capacity + slot_rank
    places = (
        slot_index[:, None] == jnp.arange(experts_all * capacity, dtype=jnp.int32)[None, :]
    ).reshape(tok_rows, top_count, -1)
    pick_table = jnp.any(places, 1).astype(jnp.bfloat16)
    weights = jnp.sum(jnp.where(places, gates[:, :, None], jnp.zeros((), jnp.bfloat16)), 1)
    return (pick_table, weights)


def run_expert(row_set, w_gate, w_up, w_down):
    local_experts = w_gate.shape[0]
    sources = row_set.shape[0] // local_experts
    grouped = row_set.reshape(sources, local_experts, row_set.shape[1], row_set.shape[2])
    gate_act = jnp.einsum("secd,edf->secf", grouped, w_gate, preferred_element_type=jnp.float32)
    up_act = jnp.einsum("secd,edf->secf", grouped, w_up, preferred_element_type=jnp.float32)
    hidden = (jax.nn.silu(gate_act) * up_act).astype(jnp.bfloat16)
    partial_value = jnp.einsum("secf,efd->secd", hidden, w_down, preferred_element_type=jnp.float32)
    return partial_value.reshape(sources * local_experts, row_set.shape[1], -1)


def on_device(
    layer_in,
    q_nope,
    q_pe,
    kv_cache,
    lengths,
    parents,
    accepted,
    kv_a,
    kv_gain,
    w_uk,
    w_uv,
    o_proj,
    post_gain,
    routes,
    gates,
    w_gate,
    w_up,
    w_down,
):
    tok_rows = layer_in.shape[0]
    local_requests, tree_size = parents.shape
    local_heads = q_nope.shape[1] // NOPE
    compressed_part = jnp.dot(layer_in, kv_a, preferred_element_type=jnp.float32).astype(
        jnp.bfloat16
    )
    tp_size = lax.axis_size("tp")
    tp_index = lax.axis_index("tp")
    quarter = D // tp_size
    parity = tp_index % 2
    beside = [(t, t ^ 1) for t in range(tp_size)]

    def features(block, first):
        return lax.dynamic_slice_in_dim(block, first * quarter, quarter, block.ndim - 1)

    pair_block = jnp.where(
        parity == 0,
        jnp.concatenate([compressed_part, lax.ppermute(compressed_part, "tp", beside)], 1),
        jnp.concatenate([lax.ppermute(compressed_part, "tp", beside), compressed_part], 1),
    )
    other_block = lax.ppermute(pair_block, "tp", [(t, t ^ 2) for t in range(tp_size)])
    compressed = jnp.where(
        tp_index // 2 == 0,
        jnp.concatenate([pair_block, other_block], 1),
        jnp.concatenate([other_block, pair_block], 1),
    )
    down_local = w_down[0]
    down_own = jnp.concatenate([features(down_local, parity), features(down_local, parity + 2)], -1)
    down_given = jnp.concatenate(
        [features(down_local, 1 - parity), features(down_local, 3 - parity)], -1
    )
    down_partner = lax.ppermute(down_given, "tp", beside)
    down_partner, compressed = lax.optimization_barrier((down_partner, compressed))
    ancestry = jax.vmap(ancestors)(parents)
    depths = jnp.sum(ancestry, -1) - 1.0
    positions = (lengths.astype(jnp.float32)[:, None] + depths).reshape(-1)
    new_rows = make_rows(compressed, kv_gain, positions)
    rows_by_request = new_rows.reshape(local_requests, tree_size, -1)
    accepted_rows = jax.vmap(compact)(ancestry, depths, accepted, rows_by_request)
    query_latent = jnp.einsum(
        "thn,hnl->thl",
        q_nope.reshape(tok_rows, local_heads, NOPE),
        w_uk.reshape(local_heads, NOPE, LATENT),
        preferred_element_type=jnp.float32,
    ).astype(jnp.bfloat16)
    queries = jnp.concatenate([query_latent, q_pe.reshape(tok_rows, local_heads, ROPE)], -1)
    q_rows = queries.reshape(local_requests, tree_size * local_heads, -1)
    mask_rows = jnp.repeat(ancestry > 0, local_heads, axis=1)
    latent_out = attend_dense(q_rows, kv_cache, lengths, rows_by_request, mask_rows)
    latent_out = latent_out.reshape(tok_rows, local_heads, LATENT)
    head_out = jnp.einsum(
        "thl,lhv->thv",
        latent_out,
        w_uv.reshape(LATENT, local_heads, VDIM),
        preferred_element_type=jnp.float32,
    ).astype(jnp.bfloat16)
    experts_all = w_gate.shape[0] * lax.axis_size("req")
    top_count = routes.shape[1]
    capacity = 4 * tok_rows * top_count // (3 * experts_all)
    pick_table, weights = route_tables(routes, gates, experts_all, capacity)
    upper = tp_index // 2
    across = [(t, t ^ 2) for t in range(tp_size)]

    def half_of(block, which):
        return jnp.concatenate([features(block, which), features(block, which + 2)], -1)

    attention = jnp.dot(
        head_out.reshape(tok_rows, local_heads * VDIM), o_proj, preferred_element_type=jnp.float32
    )
    pair_sum = half_of(attention, parity) + lax.ppermute(
        half_of(attention, 1 - parity).astype(jnp.bfloat16), "tp", beside
    ).astype(jnp.float32)
    attention_half = pair_sum + lax.ppermute(
        pair_sum.astype(jnp.bfloat16), "tp", across
    ).astype(jnp.float32)
    residual_half = half_of(layer_in, parity).astype(jnp.float32) + attention_half
    half_squares = jnp.sum(residual_half * residual_half, -1, keepdims=True)
    square_sum = half_squares + lax.ppermute(half_squares, "tp", beside)
    residual_quarter = features(residual_half, upper)
    gain_half = half_of(post_gain, parity)
    half_rows = (residual_half * lax.rsqrt(square_sum / D + epsilon) * gain_half).astype(
        jnp.bfloat16
    )
    outgoing = lax.dot_general(
        pick_table, half_rows, (((0,), (0,)), ((), ())), preferred_element_type=jnp.float32
    ).astype(jnp.bfloat16)
    outgoing = outgoing.reshape(experts_all, capacity, 2 * quarter)

    def feature_rows(weight, which):
        return jnp.concatenate(
            [
                lax.dynamic_slice_in_dim(weight, which * quarter, quarter, 0),
                lax.dynamic_slice_in_dim(weight, (which + 2) * quarter, quarter, 0),
            ],
            0,
        )

    chunks = 1
    slot_step = capacity // chunks
    weights_by_slot = weights.reshape(tok_rows, experts_all, capacity)
    routed_keep = jnp.zeros((tok_rows, quarter), jnp.float32)
    routed_give = jnp.zeros((tok_rows, quarter), jnp.float32)
    for chunk in range(chunks):
        slots = slice(chunk * slot_step, (chunk + 1) * slot_step)
        own_rows = lax.all_to_all(outgoing[:, slots], "req", split_axis=0, concat_axis=0, tiled=True)
        partner_rows = lax.ppermute(own_rows, "tp", beside)
        gate_act = jnp.einsum(
            "scf,fh->sch", own_rows, feature_rows(w_gate[0], parity),
            preferred_element_type=jnp.float32,
        ) + jnp.einsum(
            "scf,fh->sch", partner_rows, feature_rows(w_gate[0], 1 - parity),
            preferred_element_type=jnp.float32,
        )
        up_act = jnp.einsum(
            "scf,fh->sch", own_rows, feature_rows(w_up[0], parity),
            preferred_element_type=jnp.float32,
        ) + jnp.einsum(
            "scf,fh->sch", partner_rows, feature_rows(w_up[0], 1 - parity),
            preferred_element_type=jnp.float32,
        )
        expert_hidden = (jax.nn.silu(gate_act) * up_act).astype(jnp.bfloat16)
        partner_hidden = lax.ppermute(expert_hidden, "tp", beside)
        pair_value = (
            jnp.einsum("sch,hf->scf", expert_hidden, down_own, preferred_element_type=jnp.float32)
            + jnp.einsum(
                "sch,hf->scf", partner_hidden, down_partner, preferred_element_type=jnp.float32
            )
        ).astype(jnp.bfloat16)
        shares = lax.all_to_all(pair_value, "req", split_axis=0, concat_axis=0, tiled=True)
        slot_weights = weights_by_slot[:, :, slots].reshape(tok_rows, experts_all * slot_step)
        share_rows = shares.reshape(experts_all * slot_step, 2 * quarter)
        routed_give = routed_give + jnp.dot(
            slot_weights, features(share_rows, 1 - upper), preferred_element_type=jnp.float32
        )
        routed_keep = routed_keep + jnp.dot(
            slot_weights, features(share_rows, upper), preferred_element_type=jnp.float32
        )
    routed = routed_keep + lax.ppermute(
        routed_give.astype(jnp.bfloat16), "tp", across
    ).astype(jnp.float32)
    layer_out = (residual_quarter + routed).astype(jnp.bfloat16)
    return (layer_out, accepted_rows)


def solution(mesh):
    return jax.shard_map(
        on_device,
        mesh=mesh,
        in_specs=(
            P("req", None),
            P("req", "tp"),
            P("req", "tp"),
            P("req", None, None),
            P("req"),
            P("req", None),
            P("req"),
            P(None, "tp"),
            P(),
            P("tp", None),
            P(None, "tp"),
            P("tp", None),
            P(),
            P("req", None),
            P("req", None),
            P("req", None, "tp"),
            P("req", None, "tp"),
            P("req", "tp", None),
        ),
        out_specs=(P("req", "tp"), P("req", None, None)),
        check_vma=False,
    )
```

```python
import jax
import jax.numpy as jnp
from jax import lax
from jax.sharding import PartitionSpec as P

D = 2048
NOPE = 128
ROPE = 64
VDIM = 128
LATENT = 512


epsilon = 1e-06


def ancestors(parent_row):
    tree_size = parent_row.shape[0]
    indices = jnp.arange(tree_size, dtype=jnp.int32)
    link = (
        (parent_row[:, None] == indices[None, :]) | (indices[:, None] == indices[None, :])
    ).astype(jnp.float32)
    for repeat_index in range(tree_size.bit_length()):
        link = jnp.minimum(jnp.dot(link, link, precision=lax.Precision.HIGHEST), 1.0)
    return link


def rotate(vector, positions):
    half_width = vector.shape[-1] // 2
    frequency = 10000.0 ** (-jnp.arange(half_width, dtype=jnp.float32) / half_width)
    angles = positions[:, None] * frequency[None, :]
    first_half = vector[:, :half_width]
    second_half = vector[:, half_width:]
    return jnp.concatenate(
        [
            first_half * jnp.cos(angles) - second_half * jnp.sin(angles),
            first_half * jnp.sin(angles) + second_half * jnp.cos(angles),
        ],
        -1,
    )


def make_rows(compressed, kv_gain, positions):
    latent_raw = compressed[:, :LATENT].astype(jnp.float32)
    new_latent = (
        latent_raw
        * lax.rsqrt(jnp.mean(latent_raw * latent_raw, -1, keepdims=True) + epsilon)
        * kv_gain
    ).astype(jnp.bfloat16)
    new_rotary = rotate(compressed[:, LATENT:].astype(jnp.float32), positions).astype(jnp.bfloat16)
    return jnp.concatenate([new_latent, new_rotary], -1)


def compact(ancestry, depths, node_index, row_set):
    tree_size = ancestry.shape[0]
    chain_mask = jnp.take(ancestry, node_index, axis=0)
    selector = (depths[None, :] == jnp.arange(tree_size, dtype=jnp.float32)[:, None]).astype(
        jnp.float32
    ) * chain_mask[None, :]
    return jnp.dot(
        selector.astype(jnp.bfloat16), row_set, preferred_element_type=jnp.float32
    ).astype(jnp.bfloat16)


def attend_request(q_rows, cache_r, length, new_r, mask_rows):
    score_scale = (NOPE + ROPE) ** (-0.5)
    cache_slots = cache_r.shape[0]
    block_size = min(cache_slots, 512)
    block_total = cache_slots // block_size
    offsets = jnp.arange(block_size, dtype=jnp.int32)
    tree_scores = jnp.dot(q_rows, new_r.T, preferred_element_type=jnp.float32) * score_scale
    tree_scores = jnp.where(mask_rows, tree_scores, -jnp.inf)

    def block_scores(block_index):
        key_block = lax.dynamic_slice_in_dim(cache_r, block_index * block_size, block_size, 0)
        scores = jnp.dot(q_rows, key_block.T, preferred_element_type=jnp.float32) * score_scale
        valid = block_index * block_size + offsets < length
        return (jnp.where(valid[None, :], scores, -jnp.inf), key_block)

    def raise_max(block_index, row_max):
        scores, key_block = block_scores(block_index)
        return jnp.maximum(row_max, jnp.max(scores, -1))

    row_max = lax.fori_loop(0, block_total, raise_max, jnp.max(tree_scores, -1))
    tree_exps = jnp.exp(tree_scores - row_max[:, None])
    start_totals = jnp.sum(tree_exps, -1)
    start_sums = jnp.dot(
        tree_exps.astype(jnp.bfloat16), new_r[:, :LATENT], preferred_element_type=jnp.float32
    )

    def accumulate(block_index, carry):
        totals, weighted = carry
        scores, key_block = block_scores(block_index)
        exps = jnp.exp(scores - row_max[:, None])
        weighted = weighted + jnp.dot(
            exps.astype(jnp.bfloat16), key_block[:, :LATENT], preferred_element_type=jnp.float32
        )
        return (totals + jnp.sum(exps, -1), weighted)

    totals, weighted = lax.fori_loop(0, block_total, accumulate, (start_totals, start_sums))
    return (weighted / totals[:, None]).astype(jnp.bfloat16)


def attend_dense(q_rows, cache, lengths, new_rows, mask_rows):
    score_scale = (NOPE + ROPE) ** (-0.5)
    cache_slots = cache.shape[1]
    cache_scores = (
        jnp.einsum("rqk,rck->rqc", q_rows, cache, preferred_element_type=jnp.float32) * score_scale
    )
    valid = jnp.arange(cache_slots, dtype=jnp.int32)[None, :] < lengths[:, None]
    cache_scores = jnp.where(valid[:, None, :], cache_scores, -jnp.inf)
    tree_scores = (
        jnp.einsum("rqk,ruk->rqu", q_rows, new_rows, preferred_element_type=jnp.float32)
        * score_scale
    )
    tree_scores = jnp.where(mask_rows, tree_scores, -jnp.inf)
    row_max = jnp.maximum(jnp.max(cache_scores, -1), jnp.max(tree_scores, -1))
    cache_exps = jnp.exp(cache_scores - row_max[..., None])
    tree_exps = jnp.exp(tree_scores - row_max[..., None])
    totals = jnp.sum(cache_exps, -1) + jnp.sum(tree_exps, -1)
    summed = jnp.einsum(
        "rqc,rck->rqk", cache_exps.astype(jnp.bfloat16), cache, preferred_element_type=jnp.float32
    )
    summed = summed + jnp.einsum(
        "rqu,ruk->rqk", tree_exps.astype(jnp.bfloat16), new_rows, preferred_element_type=jnp.float32
    )
    return (summed[..., :LATENT] / totals[..., None]).astype(jnp.bfloat16)


def route_tables(routes, gates, experts_all, capacity):
    tok_rows, top_count = routes.shape
    flat_ids = routes.reshape(-1)
    pair_count = flat_ids.shape[0]
    hit_table = (flat_ids[:, None] == jnp.arange(experts_all, dtype=jnp.int32)[None, :]).astype(
        jnp.bfloat16
    )
    earlier = (
        jnp.arange(pair_count, dtype=jnp.int32)[:, None]
        > jnp.arange(pair_count, dtype=jnp.int32)[None, :]
    ).astype(jnp.bfloat16)
    before = jnp.dot(earlier, hit_table, preferred_element_type=jnp.float32)
    slot_rank = jnp.sum(before * hit_table.astype(jnp.float32), -1).astype(jnp.int32)
    slot_index = flat_ids * capacity + slot_rank
    places = (
        slot_index[:, None] == jnp.arange(experts_all * capacity, dtype=jnp.int32)[None, :]
    ).reshape(tok_rows, top_count, -1)
    pick_table = jnp.any(places, 1).astype(jnp.bfloat16)
    weights = jnp.sum(jnp.where(places, gates[:, :, None], jnp.zeros((), jnp.bfloat16)), 1)
    return (pick_table, weights)


def run_expert(row_set, w_gate, w_up, w_down):
    local_experts = w_gate.shape[0]
    sources = row_set.shape[0] // local_experts
    grouped = row_set.reshape(sources, local_experts, row_set.shape[1], row_set.shape[2])
    gate_act = jnp.einsum("secd,edf->secf", grouped, w_gate, preferred_element_type=jnp.float32)
    up_act = jnp.einsum("secd,edf->secf", grouped, w_up, preferred_element_type=jnp.float32)
    hidden = (jax.nn.silu(gate_act) * up_act).astype(jnp.bfloat16)
    partial_value = jnp.einsum("secf,efd->secd", hidden, w_down, preferred_element_type=jnp.float32)
    return partial_value.reshape(sources * local_experts, row_set.shape[1], -1)


def on_device(
    layer_in,
    q_nope,
    q_pe,
    kv_cache,
    lengths,
    parents,
    accepted,
    kv_a,
    kv_gain,
    w_uk,
    w_uv,
    o_proj,
    post_gain,
    routes,
    gates,
    w_gate,
    w_up,
    w_down,
):
    tok_rows = layer_in.shape[0]
    local_requests, tree_size = parents.shape
    local_heads = q_nope.shape[1] // NOPE
    compressed_part = jnp.dot(layer_in, kv_a, preferred_element_type=jnp.float32).astype(
        jnp.bfloat16
    )
    tp_size = lax.axis_size("tp")
    tp_index = lax.axis_index("tp")
    quarter = D // tp_size
    parity = tp_index % 2
    beside = [(t, t ^ 1) for t in range(tp_size)]

    def features(block, first):
        return lax.dynamic_slice_in_dim(block, first * quarter, quarter, block.ndim - 1)

    blocks = jnp.stack(
        [compressed_part]
        + [
            lax.ppermute(compressed_part, "tp", [(t, t ^ step) for t in range(tp_size)])
            for step in range(1, tp_size)
        ],
        0,
    )
    ordered = jnp.take(blocks, jnp.arange(tp_size, dtype=jnp.int32) ^ tp_index, axis=0)
    compressed = jnp.transpose(ordered, (1, 0, 2)).reshape(tok_rows, -1)
    down_local = w_down[0]
    down_own = jnp.concatenate([features(down_local, parity), features(down_local, parity + 2)], -1)
    down_given = jnp.concatenate(
        [features(down_local, 1 - parity), features(down_local, 3 - parity)], -1
    )
    down_partner = lax.ppermute(down_given, "tp", beside)
    down_partner, compressed = lax.optimization_barrier((down_partner, compressed))
    ancestry = jax.vmap(ancestors)(parents)
    depths = jnp.sum(ancestry, -1) - 1.0
    positions = (lengths.astype(jnp.float32)[:, None] + depths).reshape(-1)
    new_rows = make_rows(compressed, kv_gain, positions)
    rows_by_request = new_rows.reshape(local_requests, tree_size, -1)
    accepted_rows = jax.vmap(compact)(ancestry, depths, accepted, rows_by_request)
    query_latent = jnp.einsum(
        "thn,hnl->thl",
        q_nope.reshape(tok_rows, local_heads, NOPE),
        w_uk.reshape(local_heads, NOPE, LATENT),
        preferred_element_type=jnp.float32,
    ).astype(jnp.bfloat16)
    queries = jnp.concatenate([query_latent, q_pe.reshape(tok_rows, local_heads, ROPE)], -1)
    q_rows = queries.reshape(local_requests, tree_size * local_heads, -1)
    mask_rows = jnp.repeat(ancestry > 0, local_heads, axis=1)
    latent_out = attend_dense(q_rows, kv_cache, lengths, rows_by_request, mask_rows)
    latent_out = latent_out.reshape(tok_rows, local_heads, LATENT)
    head_out = jnp.einsum(
        "thl,lhv->thv",
        latent_out,
        w_uv.reshape(LATENT, local_heads, VDIM),
        preferred_element_type=jnp.float32,
    ).astype(jnp.bfloat16)
    experts_all = w_gate.shape[0] * lax.axis_size("req")
    top_count = routes.shape[1]
    capacity = 4 * tok_rows * top_count // (3 * experts_all)
    pick_table, weights = route_tables(routes, gates, experts_all, capacity)
    upper = tp_index // 2
    across = [(t, t ^ 2) for t in range(tp_size)]

    def half_of(block, which):
        return jnp.concatenate([features(block, which), features(block, which + 2)], -1)

    attention = jnp.dot(
        head_out.reshape(tok_rows, local_heads * VDIM), o_proj, preferred_element_type=jnp.float32
    )
    pair_sum = half_of(attention, parity) + lax.ppermute(
        half_of(attention, 1 - parity).astype(jnp.bfloat16), "tp", beside
    ).astype(jnp.float32)
    attention_half = pair_sum + lax.ppermute(
        pair_sum.astype(jnp.bfloat16), "tp", across
    ).astype(jnp.float32)
    residual_half = half_of(layer_in, parity).astype(jnp.float32) + attention_half
    half_squares = jnp.sum(residual_half * residual_half, -1, keepdims=True)
    square_sum = half_squares + lax.ppermute(half_squares, "tp", beside)
    residual_quarter = features(residual_half, upper)
    gain_half = half_of(post_gain, parity)
    half_rows = (residual_half * lax.rsqrt(square_sum / D + epsilon) * gain_half).astype(
        jnp.bfloat16
    )
    outgoing = lax.dot_general(
        pick_table, half_rows, (((0,), (0,)), ((), ())), preferred_element_type=jnp.float32
    ).astype(jnp.bfloat16)
    outgoing = outgoing.reshape(experts_all, capacity, 2 * quarter)

    def feature_rows(weight, which):
        return jnp.concatenate(
            [
                lax.dynamic_slice_in_dim(weight, which * quarter, quarter, 0),
                lax.dynamic_slice_in_dim(weight, (which + 2) * quarter, quarter, 0),
            ],
            0,
        )

    chunks = 1
    slot_step = capacity // chunks
    weights_by_slot = weights.reshape(tok_rows, experts_all, capacity)
    routed_half = jnp.zeros((tok_rows, 2 * quarter), jnp.float32)
    for chunk in range(chunks):
        slots = slice(chunk * slot_step, (chunk + 1) * slot_step)
        own_rows = lax.all_to_all(outgoing[:, slots], "req", split_axis=0, concat_axis=0, tiled=True)
        partner_rows = lax.ppermute(own_rows, "tp", beside)
        gate_act = jnp.einsum(
            "scf,fh->sch", own_rows, feature_rows(w_gate[0], parity),
            preferred_element_type=jnp.float32,
        ) + jnp.einsum(
            "scf,fh->sch", partner_rows, feature_rows(w_gate[0], 1 - parity),
            preferred_element_type=jnp.float32,
        )
        up_act = jnp.einsum(
            "scf,fh->sch", own_rows, feature_rows(w_up[0], parity),
            preferred_element_type=jnp.float32,
        ) + jnp.einsum(
            "scf,fh->sch", partner_rows, feature_rows(w_up[0], 1 - parity),
            preferred_element_type=jnp.float32,
        )
        expert_hidden = (jax.nn.silu(gate_act) * up_act).astype(jnp.bfloat16)
        partner_hidden = lax.ppermute(expert_hidden, "tp", beside)
        pair_value = (
            jnp.einsum("sch,hf->scf", expert_hidden, down_own, preferred_element_type=jnp.float32)
            + jnp.einsum(
                "sch,hf->scf", partner_hidden, down_partner, preferred_element_type=jnp.float32
            )
        ).astype(jnp.bfloat16)
        shares = lax.all_to_all(pair_value, "req", split_axis=0, concat_axis=0, tiled=True)
        routed_half = routed_half + jnp.dot(
            weights_by_slot[:, :, slots].reshape(tok_rows, experts_all * slot_step),
            shares.reshape(experts_all * slot_step, 2 * quarter),
            preferred_element_type=jnp.float32,
        )
    keep = features(routed_half, upper)
    give = features(routed_half, 1 - upper)
    routed = keep + lax.ppermute(give.astype(jnp.bfloat16), "tp", across).astype(jnp.float32)
    layer_out = (residual_quarter + routed).astype(jnp.bfloat16)
    return (layer_out, accepted_rows)


def solution(mesh):
    return jax.shard_map(
        on_device,
        mesh=mesh,
        in_specs=(
            P("req", None),
            P("req", "tp"),
            P("req", "tp"),
            P("req", None, None),
            P("req"),
            P("req", None),
            P("req"),
            P(None, "tp"),
            P(),
            P("tp", None),
            P(None, "tp"),
            P("tp", None),
            P(),
            P("req", None),
            P("req", None),
            P("req", None, "tp"),
            P("req", None, "tp"),
            P("req", "tp", None),
        ),
        out_specs=(P("req", "tp"), P("req", None, None)),
        check_vma=False,
    )
```

```python
import jax
import jax.numpy as jnp
from jax import lax
from jax.sharding import PartitionSpec as P

D = 2048
NOPE = 128
ROPE = 64
VDIM = 128
LATENT = 512


epsilon = 1e-06


def ancestors(parent_row):
    tree_size = parent_row.shape[0]
    indices = jnp.arange(tree_size, dtype=jnp.int32)
    link = (
        (parent_row[:, None] == indices[None, :]) | (indices[:, None] == indices[None, :])
    ).astype(jnp.float32)
    for repeat_index in range(tree_size.bit_length()):
        link = jnp.minimum(jnp.dot(link, link, precision=lax.Precision.HIGHEST), 1.0)
    return link


def rotate(vector, positions):
    half_width = vector.shape[-1] // 2
    frequency = 10000.0 ** (-jnp.arange(half_width, dtype=jnp.float32) / half_width)
    angles = positions[:, None] * frequency[None, :]
    first_half = vector[:, :half_width]
    second_half = vector[:, half_width:]
    return jnp.concatenate(
        [
            first_half * jnp.cos(angles) - second_half * jnp.sin(angles),
            first_half * jnp.sin(angles) + second_half * jnp.cos(angles),
        ],
        -1,
    )


def make_rows(compressed, kv_gain, positions):
    latent_raw = compressed[:, :LATENT].astype(jnp.float32)
    new_latent = (
        latent_raw
        * lax.rsqrt(jnp.mean(latent_raw * latent_raw, -1, keepdims=True) + epsilon)
        * kv_gain
    ).astype(jnp.bfloat16)
    new_rotary = rotate(compressed[:, LATENT:].astype(jnp.float32), positions).astype(jnp.bfloat16)
    return jnp.concatenate([new_latent, new_rotary], -1)


def compact(ancestry, depths, node_index, row_set):
    tree_size = ancestry.shape[0]
    chain_mask = jnp.take(ancestry, node_index, axis=0)
    selector = (depths[None, :] == jnp.arange(tree_size, dtype=jnp.float32)[:, None]).astype(
        jnp.float32
    ) * chain_mask[None, :]
    return jnp.dot(
        selector.astype(jnp.bfloat16), row_set, preferred_element_type=jnp.float32
    ).astype(jnp.bfloat16)


def attend_request(q_rows, cache_r, length, new_r, mask_rows):
    score_scale = (NOPE + ROPE) ** (-0.5)
    cache_slots = cache_r.shape[0]
    block_size = min(cache_slots, 512)
    block_total = cache_slots // block_size
    offsets = jnp.arange(block_size, dtype=jnp.int32)
    tree_scores = jnp.dot(q_rows, new_r.T, preferred_element_type=jnp.float32) * score_scale
    tree_scores = jnp.where(mask_rows, tree_scores, -jnp.inf)

    def block_scores(block_index):
        key_block = lax.dynamic_slice_in_dim(cache_r, block_index * block_size, block_size, 0)
        scores = jnp.dot(q_rows, key_block.T, preferred_element_type=jnp.float32) * score_scale
        valid = block_index * block_size + offsets < length
        return (jnp.where(valid[None, :], scores, -jnp.inf), key_block)

    def raise_max(block_index, row_max):
        scores, key_block = block_scores(block_index)
        return jnp.maximum(row_max, jnp.max(scores, -1))

    row_max = lax.fori_loop(0, block_total, raise_max, jnp.max(tree_scores, -1))
    tree_exps = jnp.exp(tree_scores - row_max[:, None])
    start_totals = jnp.sum(tree_exps, -1)
    start_sums = jnp.dot(
        tree_exps.astype(jnp.bfloat16), new_r[:, :LATENT], preferred_element_type=jnp.float32
    )

    def accumulate(block_index, carry):
        totals, weighted = carry
        scores, key_block = block_scores(block_index)
        exps = jnp.exp(scores - row_max[:, None])
        weighted = weighted + jnp.dot(
            exps.astype(jnp.bfloat16), key_block[:, :LATENT], preferred_element_type=jnp.float32
        )
        return (totals + jnp.sum(exps, -1), weighted)

    totals, weighted = lax.fori_loop(0, block_total, accumulate, (start_totals, start_sums))
    return (weighted / totals[:, None]).astype(jnp.bfloat16)


def attend_dense(q_rows, cache, lengths, new_rows, mask_rows):
    score_scale = (NOPE + ROPE) ** (-0.5)
    cache_slots = cache.shape[1]
    cache_scores = (
        jnp.einsum("rqk,rck->rqc", q_rows, cache, preferred_element_type=jnp.float32) * score_scale
    )
    valid = jnp.arange(cache_slots, dtype=jnp.int32)[None, :] < lengths[:, None]
    cache_scores = jnp.where(valid[:, None, :], cache_scores, -jnp.inf)
    tree_scores = (
        jnp.einsum("rqk,ruk->rqu", q_rows, new_rows, preferred_element_type=jnp.float32)
        * score_scale
    )
    tree_scores = jnp.where(mask_rows, tree_scores, -jnp.inf)
    row_max = jnp.maximum(jnp.max(cache_scores, -1), jnp.max(tree_scores, -1))
    cache_exps = jnp.exp(cache_scores - row_max[..., None])
    tree_exps = jnp.exp(tree_scores - row_max[..., None])
    totals = jnp.sum(cache_exps, -1) + jnp.sum(tree_exps, -1)
    summed = jnp.einsum(
        "rqc,rck->rqk", cache_exps.astype(jnp.bfloat16), cache, preferred_element_type=jnp.float32
    )
    summed = summed + jnp.einsum(
        "rqu,ruk->rqk", tree_exps.astype(jnp.bfloat16), new_rows, preferred_element_type=jnp.float32
    )
    return (summed[..., :LATENT] / totals[..., None]).astype(jnp.bfloat16)


def route_tables(routes, gates, experts_all, capacity):
    tok_rows, top_count = routes.shape
    flat_ids = routes.reshape(-1)
    pair_count = flat_ids.shape[0]
    hit_table = (flat_ids[:, None] == jnp.arange(experts_all, dtype=jnp.int32)[None, :]).astype(
        jnp.bfloat16
    )
    earlier = (
        jnp.arange(pair_count, dtype=jnp.int32)[:, None]
        > jnp.arange(pair_count, dtype=jnp.int32)[None, :]
    ).astype(jnp.bfloat16)
    before = jnp.dot(earlier, hit_table, preferred_element_type=jnp.float32)
    slot_rank = jnp.sum(before * hit_table.astype(jnp.float32), -1).astype(jnp.int32)
    slot_index = flat_ids * capacity + slot_rank
    places = (
        slot_index[:, None] == jnp.arange(experts_all * capacity, dtype=jnp.int32)[None, :]
    ).reshape(tok_rows, top_count, -1)
    pick_table = jnp.any(places, 1).astype(jnp.bfloat16)
    weights = jnp.sum(jnp.where(places, gates[:, :, None], jnp.zeros((), jnp.bfloat16)), 1)
    return (pick_table, weights)


def run_expert(row_set, w_gate, w_up, w_down):
    local_experts = w_gate.shape[0]
    sources = row_set.shape[0] // local_experts
    grouped = row_set.reshape(sources, local_experts, row_set.shape[1], row_set.shape[2])
    gate_act = jnp.einsum("secd,edf->secf", grouped, w_gate, preferred_element_type=jnp.float32)
    up_act = jnp.einsum("secd,edf->secf", grouped, w_up, preferred_element_type=jnp.float32)
    hidden = (jax.nn.silu(gate_act) * up_act).astype(jnp.bfloat16)
    partial_value = jnp.einsum("secf,efd->secd", hidden, w_down, preferred_element_type=jnp.float32)
    return partial_value.reshape(sources * local_experts, row_set.shape[1], -1)


def on_device(
    layer_in,
    q_nope,
    q_pe,
    kv_cache,
    lengths,
    parents,
    accepted,
    kv_a,
    kv_gain,
    w_uk,
    w_uv,
    o_proj,
    post_gain,
    routes,
    gates,
    w_gate,
    w_up,
    w_down,
):
    tok_rows = layer_in.shape[0]
    local_requests, tree_size = parents.shape
    local_heads = q_nope.shape[1] // NOPE
    compressed_part = jnp.dot(layer_in, kv_a, preferred_element_type=jnp.float32).astype(
        jnp.bfloat16
    )
    tp_size = lax.axis_size("tp")
    tp_index = lax.axis_index("tp")
    quarter = D // tp_size
    parity = tp_index % 2
    beside = [(t, t ^ 1) for t in range(tp_size)]

    def features(block, first):
        return lax.dynamic_slice_in_dim(block, first * quarter, quarter, block.ndim - 1)

    pair_block = jnp.where(
        parity == 0,
        jnp.concatenate([compressed_part, lax.ppermute(compressed_part, "tp", beside)], 1),
        jnp.concatenate([lax.ppermute(compressed_part, "tp", beside), compressed_part], 1),
    )
    other_block = lax.ppermute(pair_block, "tp", [(t, t ^ 2) for t in range(tp_size)])
    compressed = jnp.where(
        tp_index // 2 == 0,
        jnp.concatenate([pair_block, other_block], 1),
        jnp.concatenate([other_block, pair_block], 1),
    )
    down_local = w_down[0]
    down_own = jnp.concatenate([features(down_local, parity), features(down_local, parity + 2)], -1)
    down_given = jnp.concatenate(
        [features(down_local, 1 - parity), features(down_local, 3 - parity)], -1
    )
    down_partner = lax.ppermute(down_given, "tp", beside)
    down_partner, compressed = lax.optimization_barrier((down_partner, compressed))
    ancestry = jax.vmap(ancestors)(parents)
    depths = jnp.sum(ancestry, -1) - 1.0
    positions = (lengths.astype(jnp.float32)[:, None] + depths).reshape(-1)
    new_rows = make_rows(compressed, kv_gain, positions)
    rows_by_request = new_rows.reshape(local_requests, tree_size, -1)
    accepted_rows = jax.vmap(compact)(ancestry, depths, accepted, rows_by_request)
    query_latent = jnp.einsum(
        "thn,hnl->thl",
        q_nope.reshape(tok_rows, local_heads, NOPE),
        w_uk.reshape(local_heads, NOPE, LATENT),
        preferred_element_type=jnp.float32,
    ).astype(jnp.bfloat16)
    queries = jnp.concatenate([query_latent, q_pe.reshape(tok_rows, local_heads, ROPE)], -1)
    q_rows = queries.reshape(local_requests, tree_size * local_heads, -1)
    mask_rows = jnp.repeat(ancestry > 0, local_heads, axis=1)
    latent_out = attend_dense(q_rows, kv_cache, lengths, rows_by_request, mask_rows)
    latent_out = latent_out.reshape(tok_rows, local_heads, LATENT)
    head_out = jnp.einsum(
        "thl,lhv->thv",
        latent_out,
        w_uv.reshape(LATENT, local_heads, VDIM),
        preferred_element_type=jnp.float32,
    ).astype(jnp.bfloat16)
    experts_all = w_gate.shape[0] * lax.axis_size("req")
    top_count = routes.shape[1]
    capacity = 4 * tok_rows * top_count // (3 * experts_all)
    pick_table, weights = route_tables(routes, gates, experts_all, capacity)
    upper = tp_index // 2
    across = [(t, t ^ 2) for t in range(tp_size)]

    def half_of(block, which):
        return jnp.concatenate([features(block, which), features(block, which + 2)], -1)

    head_rows = head_out.reshape(tok_rows, local_heads * VDIM)
    given_attention = jnp.dot(
        head_rows, half_of(o_proj, 1 - parity), preferred_element_type=jnp.float32
    )
    pair_sum = jnp.dot(
        head_rows, half_of(o_proj, parity), preferred_element_type=jnp.float32
    ) + lax.ppermute(given_attention.astype(jnp.bfloat16), "tp", beside).astype(jnp.float32)
    attention_half = pair_sum + lax.ppermute(
        pair_sum.astype(jnp.bfloat16), "tp", across
    ).astype(jnp.float32)
    residual_half = half_of(layer_in, parity).astype(jnp.float32) + attention_half
    half_squares = jnp.sum(residual_half * residual_half, -1, keepdims=True)
    square_sum = half_squares + lax.ppermute(half_squares, "tp", beside)
    residual_quarter = features(residual_half, upper)
    gain_half = half_of(post_gain, parity)
    half_rows = (residual_half * lax.rsqrt(square_sum / D + epsilon) * gain_half).astype(
        jnp.bfloat16
    )
    outgoing = lax.dot_general(
        pick_table, half_rows, (((0,), (0,)), ((), ())), preferred_element_type=jnp.float32
    ).astype(jnp.bfloat16)
    outgoing = outgoing.reshape(experts_all, capacity, 2 * quarter)

    def feature_rows(weight, which):
        return jnp.concatenate(
            [
                lax.dynamic_slice_in_dim(weight, which * quarter, quarter, 0),
                lax.dynamic_slice_in_dim(weight, (which + 2) * quarter, quarter, 0),
            ],
            0,
        )

    chunks = 1
    slot_step = capacity // chunks
    weights_by_slot = weights.reshape(tok_rows, experts_all, capacity)
    routed_half = jnp.zeros((tok_rows, 2 * quarter), jnp.float32)
    for chunk in range(chunks):
        slots = slice(chunk * slot_step, (chunk + 1) * slot_step)
        own_rows = lax.all_to_all(outgoing[:, slots], "req", split_axis=0, concat_axis=0, tiled=True)
        partner_rows = lax.ppermute(own_rows, "tp", beside)
        gate_act = jnp.einsum(
            "scf,fh->sch", own_rows, feature_rows(w_gate[0], parity),
            preferred_element_type=jnp.float32,
        ) + jnp.einsum(
            "scf,fh->sch", partner_rows, feature_rows(w_gate[0], 1 - parity),
            preferred_element_type=jnp.float32,
        )
        up_act = jnp.einsum(
            "scf,fh->sch", own_rows, feature_rows(w_up[0], parity),
            preferred_element_type=jnp.float32,
        ) + jnp.einsum(
            "scf,fh->sch", partner_rows, feature_rows(w_up[0], 1 - parity),
            preferred_element_type=jnp.float32,
        )
        expert_hidden = (jax.nn.silu(gate_act) * up_act).astype(jnp.bfloat16)
        partner_hidden = lax.ppermute(expert_hidden, "tp", beside)
        pair_value = (
            jnp.einsum("sch,hf->scf", expert_hidden, down_own, preferred_element_type=jnp.float32)
            + jnp.einsum(
                "sch,hf->scf", partner_hidden, down_partner, preferred_element_type=jnp.float32
            )
        ).astype(jnp.bfloat16)
        shares = lax.all_to_all(pair_value, "req", split_axis=0, concat_axis=0, tiled=True)
        routed_half = routed_half + jnp.dot(
            weights_by_slot[:, :, slots].reshape(tok_rows, experts_all * slot_step),
            shares.reshape(experts_all * slot_step, 2 * quarter),
            preferred_element_type=jnp.float32,
        )
    keep = features(routed_half, upper)
    give = features(routed_half, 1 - upper)
    routed = keep + lax.ppermute(give.astype(jnp.bfloat16), "tp", across).astype(jnp.float32)
    layer_out = (residual_quarter + routed).astype(jnp.bfloat16)
    return (layer_out, accepted_rows)


def solution(mesh):
    return jax.shard_map(
        on_device,
        mesh=mesh,
        in_specs=(
            P("req", None),
            P("req", "tp"),
            P("req", "tp"),
            P("req", None, None),
            P("req"),
            P("req", None),
            P("req"),
            P(None, "tp"),
            P(),
            P("tp", None),
            P(None, "tp"),
            P("tp", None),
            P(),
            P("req", None),
            P("req", None),
            P("req", None, "tp"),
            P("req", None, "tp"),
            P("req", "tp", None),
        ),
        out_specs=(P("req", "tp"), P("req", None, None)),
        check_vma=False,
    )
```
